32 devices in a mesh: outer: 4 (over y, core), inner: 8 (over z, x).
Axes of the slice: x: 2, y: 2, z: 4, core: 2. Of those that a mesh axis runs over, the one named last changes fastest.
Arguments:
- queries: bfloat16 [4, 8, 8, 64, 512], P('outer', None, 'inner'), may hold values from -240 to 240
- keys: bfloat16 [4, 8, 8, 64, 128], P('outer', None, 'inner'), may hold values from -6 to 6
- values: bfloat16 [4, 8, 8, 64, 128], P('outer', None, 'inner'), may hold values from -6 to 6
- grad_out: bfloat16 [4, 8, 8, 64, 512], P('outer', None, 'inner'), may hold values from -6 to 6
- doc_starts: int32 [4, 8, 4], replicated, may hold values from 0 to 512, as said below
Outputs:
- attn_out: bfloat16 [4, 8, 8, 64, 512], P('outer', None, 'inner')
- query_grads: bfloat16 [4, 8, 8, 64, 512], P('outer', None, 'inner')
- key_grads: bfloat16 [4, 8, 8, 64, 128], P('outer', None, 'inner')
- value_grads: bfloat16 [4, 8, 8, 64, 128], P('outer', None, 'inner')
The draws below stay inside these ranges and needn't reach their ends.
Inputs may be any that keep to these rules, and one draw needn't show every extreme that they name: `doc_starts`: entry [o, u, j] is an offset within unit u of segment o at which a document starts, or 512 for none. The offsets below 512 of a unit are distinct, rise with j and stand before all its 512 entries. Offset 0 starts a document in every even unit except unit 0 of segments o > 0; unit 0 of such a segment and an odd unit may continue the document of the position before them (then their first entry is not 0). The last unit of every segment continues the one before it; position 0 of the sequence starts a document.
All inputs are finite; a program needn't handle non-finite values.
Results may differ from the reference program's by a relative error of at most 0.0075.
Values may be sent and summed in bfloat16 or wider, within the bound.
No kernel may reach another device: no remote copies, remote signals or barrier semaphores. Data moves between devices by JAX's collectives and lax.ppermute only.
A program may use at most 128 MiB of HBM per device.

```python
import math
import jax
import jax.numpy as jnp
from jax import lax

HEAD_DIM = 128
HEADS = 4
TOK_DEV = 512
DOC_SLOTS = 4
PIECE = 64
N_OUTER = 4
N_INNER = 8


def draw_doc_starts(key, part):
    base = jax.random.fold_in(key, 7)
    k_join, k_start, k_keep = jax.random.split(base, 3)
    pairs = N_INNER // 2
    joined = jax.random.randint(k_join, (N_OUTER, pairs), 0, 2)
    joined = joined.at[:, pairs - 1].set(1)
    unit_ids = jnp.arange(N_INNER)
    joined_units = jnp.repeat(joined, 2, axis=1)
    continues = (unit_ids[None, :] % 2 == 1) & (joined_units == 1) | (unit_ids[None, :] == 0) & (jnp.arange(N_OUTER)[:, None] > 0)
    stride = TOK_DEV // DOC_SLOTS
    first_start = jnp.where(continues, TOK_DEV, 0)
    extra = jnp.arange(1, DOC_SLOTS)[None, None, :] * stride + jax.random.randint(k_start, (N_OUTER, N_INNER, DOC_SLOTS - 1), 0, stride)
    keeping = jax.random.randint(k_keep, (N_OUTER, N_INNER, DOC_SLOTS - 1), 0, 2)
    extra = jnp.where(keeping == 1, extra, TOK_DEV)
    starts = jnp.sort(jnp.concatenate([first_start[:, :, None], extra], axis=2), axis=2)
    return starts.astype(jnp.int32)


def pair_draw(key):
    base = jax.random.fold_in(key, 11)
    k_key, k_query = jax.random.split(base, 2)
    rows = (N_OUTER, N_INNER, N_INNER, PIECE)
    key_vals = jnp.clip(jax.random.normal(k_key, rows + (HEAD_DIM,), jnp.float32), -6.0, 6.0)
    query_vals = jnp.clip(jax.random.normal(k_query, rows + (HEADS * HEAD_DIM,), jnp.float32), -6.0, 6.0)
    return (query_vals, key_vals)


def draw_queries(key, part):
    return pair_draw(key)[0].astype(jnp.bfloat16)


def draw_keys(key, part):
    return pair_draw(key)[1].astype(jnp.bfloat16)


def block_scale(own_key, extent, cuts, least, high):
    def one(axis_at, shards_of):
        steps = jax.random.uniform(jax.random.fold_in(jax.random.fold_in(own_key, 6), axis_at), (shards_of,), jnp.float32, least / len(cuts), high / len(cuts))
        return jnp.repeat(jnp.exp(steps), extent[axis_at] // shards_of).reshape((-1,) + (1,) * (len(extent) - axis_at - 1))

    level = one(*cuts[0])
    for cut in cuts[1:]:
        level = level * one(*cut)
    return level


def scatter_about(stream_key, dims, width, reach, pieces=(), kind=jnp.bfloat16):
    values = jax.random.normal(stream_key, dims, jnp.float32) * width
    if len(pieces) > 0:
        values = block_scale(stream_key, dims, pieces, -0.22, 0.18) * values
    return jnp.clip(values, min=-reach, max=reach).astype(kind)


def setup_inputs(seed: int = 0) -> dict:
    key_list = jax.random.split(jax.random.key(seed), 6)
    return {
        "queries": draw_queries(jax.random.fold_in(key_list[5], 71), 0),
        "keys": draw_keys(jax.random.fold_in(key_list[5], 71), 0),
        "values": scatter_about(key_list[2], (N_OUTER, N_INNER, N_INNER, PIECE, HEAD_DIM), 1.0, 6.0, ((0, 4), (2, 8))),
        "grad_out": scatter_about(key_list[3], (N_OUTER, N_INNER, N_INNER, PIECE, HEADS * HEAD_DIM), 1.0, 6.0, ((0, 4), (2, 8))),
        "doc_starts": draw_doc_starts(jax.random.fold_in(key_list[5], 71), 0),
    }


def doc_table(doc_starts):
    flat_starts = doc_starts.reshape(N_OUTER * N_INNER, DOC_SLOTS)
    start_counts = lax.optimization_barrier(jnp.sum((flat_starts < TOK_DEV).astype(jnp.int32), axis=1))
    first_index = jnp.cumsum(start_counts) - start_counts
    offsets = jnp.arange(TOK_DEV, dtype=jnp.int32)
    inside_count = lax.optimization_barrier(jnp.sum((flat_starts[:, None, :] <= offsets[None, :, None]).astype(jnp.int32), axis=2))
    return (first_index[:, None] + inside_count - 1).astype(jnp.int32)

def reference(queries, keys, values, grad_out, doc_starts):
    n_tokens = N_OUTER * N_INNER * TOK_DEV
    n_units = N_OUTER * N_INNER
    width_q = HEADS * HEAD_DIM
    scaling = 1.0 / math.sqrt(HEAD_DIM)
    span = 4 * TOK_DEV
    behind = 3 * TOK_DEV
    q_flat = queries.reshape(n_tokens, width_q)
    g_flat = grad_out.reshape(n_tokens, width_q)
    k_flat = keys.reshape(n_tokens, HEAD_DIM)
    v_flat = values.reshape(n_tokens, HEAD_DIM)
    doc_ids = doc_table(doc_starts).reshape(n_tokens)
    positions = jnp.arange(n_tokens, dtype=jnp.int32)
    key_front = jnp.concatenate([jnp.zeros((behind, HEAD_DIM), keys.dtype), k_flat])
    value_front = jnp.concatenate([jnp.zeros((behind, HEAD_DIM), values.dtype), v_flat])
    doc_front = jnp.concatenate([jnp.full((behind,), -1, jnp.int32), doc_ids])
    pos_front = jnp.concatenate([jnp.zeros((behind,), jnp.int32), positions])

    def forward_unit(unit_id):
        begin = (unit_id * TOK_DEV).astype(jnp.int32)
        q_part = lax.dynamic_slice_in_dim(q_flat, begin, TOK_DEV).astype(jnp.float32).reshape(TOK_DEV, HEADS, HEAD_DIM)
        g_part = lax.dynamic_slice_in_dim(g_flat, begin, TOK_DEV).astype(jnp.float32).reshape(TOK_DEV, HEADS, HEAD_DIM)
        doc_q = lax.dynamic_slice_in_dim(doc_ids, begin, TOK_DEV)
        pos_q = lax.dynamic_slice_in_dim(positions, begin, TOK_DEV)
        k_win = lax.dynamic_slice_in_dim(key_front, begin, span).astype(jnp.float32)
        v_win = lax.dynamic_slice_in_dim(value_front, begin, span).astype(jnp.float32)
        doc_k = lax.dynamic_slice_in_dim(doc_front, begin, span)
        pos_k = lax.dynamic_slice_in_dim(pos_front, begin, span)
        allowed = (doc_q[:, None] == doc_k[None, :]) & (pos_k[None, :] <= pos_q[:, None])
        scores = jnp.einsum('qhd,kd->hqk', q_part, k_win) * scaling
        scores = jnp.where(allowed[None], scores, -jnp.inf)
        row_max = lax.optimization_barrier(jnp.max(scores, axis=2, keepdims=True))
        log_total = row_max + jnp.log(lax.optimization_barrier(jnp.sum(jnp.exp(scores - row_max), axis=2, keepdims=True)))
        probs = jnp.exp(scores - log_total)
        probs_low = probs.astype(jnp.bfloat16)
        attn = jnp.einsum('hqk,kd->qhd', probs_low.astype(jnp.float32), v_win).astype(jnp.bfloat16)
        inner_prod = lax.optimization_barrier(jnp.sum(g_part * attn.astype(jnp.float32), axis=2))
        grad_probs = jnp.einsum('qhd,kd->hqk', g_part, v_win)
        score_grads = (probs * (grad_probs - inner_prod.T[:, :, None])).astype(jnp.bfloat16)
        q_grads = (jnp.einsum('hqk,kd->qhd', score_grads.astype(jnp.float32), k_win) * scaling).astype(jnp.bfloat16)
        return (attn.reshape(TOK_DEV, width_q), q_grads.reshape(TOK_DEV, width_q), log_total[:, :, 0].T, inner_prod)
    unit_ids = jnp.arange(n_units, dtype=jnp.int32)
    attn_all, qgrad_all, log_all, inner_all = lax.map(forward_unit, unit_ids)
    log_flat = log_all.reshape(n_tokens, HEADS)
    inner_flat = inner_all.reshape(n_tokens, HEADS)
    q_back = jnp.concatenate([q_flat, jnp.zeros((behind, width_q), queries.dtype)])
    g_back = jnp.concatenate([g_flat, jnp.zeros((behind, width_q), grad_out.dtype)])
    log_back = jnp.concatenate([log_flat, jnp.zeros((behind, HEADS), jnp.float32)])
    inner_back = jnp.concatenate([inner_flat, jnp.zeros((behind, HEADS), jnp.float32)])
    doc_back = jnp.concatenate([doc_ids, jnp.full((behind,), -1, jnp.int32)])
    pos_back = jnp.concatenate([positions, jnp.zeros((behind,), jnp.int32)])

    def key_unit(unit_id):
        begin = (unit_id * TOK_DEV).astype(jnp.int32)
        k_part = lax.dynamic_slice_in_dim(k_flat, begin, TOK_DEV).astype(jnp.float32)
        v_part = lax.dynamic_slice_in_dim(v_flat, begin, TOK_DEV).astype(jnp.float32)
        doc_k = lax.dynamic_slice_in_dim(doc_ids, begin, TOK_DEV)
        pos_k = lax.dynamic_slice_in_dim(positions, begin, TOK_DEV)
        q_win = lax.dynamic_slice_in_dim(q_back, begin, span).astype(jnp.float32).reshape(span, HEADS, HEAD_DIM)
        g_win = lax.dynamic_slice_in_dim(g_back, begin, span).astype(jnp.float32).reshape(span, HEADS, HEAD_DIM)
        log_win = lax.dynamic_slice_in_dim(log_back, begin, span)
        inner_win = lax.dynamic_slice_in_dim(inner_back, begin, span)
        doc_q = lax.dynamic_slice_in_dim(doc_back, begin, span)
        pos_q = lax.dynamic_slice_in_dim(pos_back, begin, span)
        allowed = (doc_q[:, None] == doc_k[None, :]) & (pos_k[None, :] <= pos_q[:, None])
        scores = jnp.einsum('qhd,kd->hqk', q_win, k_part) * scaling
        scores = jnp.where(allowed[None], scores, -jnp.inf)
        probs = jnp.exp(scores - log_win.T[:, :, None])
        probs_low = probs.astype(jnp.bfloat16)
        v_grads = jnp.einsum('hqk,qhd->kd', probs_low.astype(jnp.float32), g_win)
        grad_probs = jnp.einsum('qhd,kd->hqk', g_win, v_part)
        score_grads = (probs * (grad_probs - inner_win.T[:, :, None])).astype(jnp.bfloat16)
        k_grads = jnp.einsum('hqk,qhd->kd', score_grads.astype(jnp.float32), q_win) * scaling
        return (k_grads.astype(jnp.bfloat16), v_grads.astype(jnp.bfloat16))
    kgrad_all, vgrad_all = lax.map(key_unit, unit_ids)
    shape_q = (N_OUTER, N_INNER, N_INNER, PIECE, width_q)
    shape_k = (N_OUTER, N_INNER, N_INNER, PIECE, HEAD_DIM)
    return (attn_all.reshape(shape_q), qgrad_all.reshape(shape_q), kgrad_all.reshape(shape_k), vgrad_all.reshape(shape_k))
```

```python
import math

import jax
import jax.numpy as jnp
from jax import lax
from jax.sharding import PartitionSpec as P


def doc_table(doc_starts, tok_dev):
    n_outer, n_inner, n_slots = doc_starts.shape
    flat_starts = doc_starts.reshape(n_outer * n_inner, n_slots)
    start_counts = jnp.sum((flat_starts < tok_dev).astype(jnp.int32), axis=1)
    first_index = jnp.cumsum(start_counts) - start_counts
    offsets = jnp.arange(tok_dev, dtype=jnp.int32)
    inside_count = jnp.sum(
        (flat_starts[:, None, :] <= offsets[None, :, None]).astype(jnp.int32), axis=2
    )
    return (first_index[:, None] + inside_count - 1).reshape(n_outer, n_inner, tok_dev)


def attend(
    query_buf, grad_buf, query_pos, query_doc, key_buf, value_buf, key_pos, key_doc, n_heads
):
    n_rows = query_buf.shape[0]
    head_dim = key_buf.shape[1]
    scaling = 1.0 / math.sqrt(head_dim)
    q_three = query_buf.reshape(n_rows, n_heads, head_dim)
    g_three = grad_buf.reshape(n_rows, n_heads, head_dim)
    scores = (
        jnp.einsum("qhd,kd->hqk", q_three, key_buf, preferred_element_type=jnp.float32) * scaling
    )
    allowed = (query_doc[:, None] == key_doc[None, :]) & (key_pos[None, :] <= query_pos[:, None])
    scores = jnp.where(allowed[None], scores, -jnp.inf)
    row_max = jnp.max(scores, axis=2, keepdims=True)
    log_total = row_max + jnp.log(jnp.sum(jnp.exp(scores - row_max), axis=2, keepdims=True))
    probs = jnp.exp(scores - log_total)
    probs_low = probs.astype(jnp.bfloat16)
    attn = jnp.einsum(
        "hqk,kd->qhd", probs_low, value_buf, preferred_element_type=jnp.float32
    ).astype(jnp.bfloat16)
    inner_prod = jnp.sum(g_three.astype(jnp.float32) * attn.astype(jnp.float32), axis=2)
    grad_probs = jnp.einsum("qhd,kd->hqk", g_three, value_buf, preferred_element_type=jnp.float32)
    score_grads = (probs * (grad_probs - inner_prod.T[:, :, None])).astype(jnp.bfloat16)
    q_grads = (
        jnp.einsum("hqk,kd->qhd", score_grads, key_buf, preferred_element_type=jnp.float32)
        * scaling
    )
    k_grads = (
        jnp.einsum("hqk,qhd->kd", score_grads, q_three, preferred_element_type=jnp.float32)
        * scaling
    )
    v_grads = jnp.einsum("hqk,qhd->kd", probs_low, g_three, preferred_element_type=jnp.float32)
    return (
        attn.reshape(n_rows, -1),
        q_grads.astype(jnp.bfloat16).reshape(n_rows, -1),
        k_grads,
        v_grads,
    )


def shards(queries, keys, values, grad_out, doc_starts):
    n_inner = lax.axis_size("inner")
    n_outer = lax.axis_size("outer")
    n_units = queries.shape[1]
    piece_len = queries.shape[3]
    width_q = queries.shape[4]
    head_dim = keys.shape[4]
    n_heads = width_q // head_dim
    tok_dev = piece_len * n_inner
    outer_id = lax.axis_index("outer")
    inner_id = lax.axis_index("inner")
    docs_all = doc_table(doc_starts, tok_dev)
    offsets = jnp.arange(tok_dev, dtype=jnp.int32)

    packed = jnp.concatenate(
        [queries[0, :, 0], keys[0, :, 0], values[0, :, 0], grad_out[0, :, 0]], axis=-1
    )
    arrived = lax.all_to_all(packed, "inner", 0, 0, tiled=True).reshape(tok_dev, -1)
    query_buf = arrived[:, :width_q]
    kv_own = arrived[:, width_q : width_q + 2 * head_dim]
    grad_buf = arrived[:, width_q + 2 * head_dim :]

    pairs_up = [(2 * p, 2 * p + 1) for p in range(n_inner // 2)]
    kv_partner = lax.ppermute(kv_own, "inner", pairs_up)

    both = ("outer", "inner")
    last_a, last_b = n_inner - 2, n_inner - 1
    send_a = [((o - 1) * n_inner + last_a, o * n_inner) for o in range(1, n_outer)] + [
        ((o - 1) * n_inner + last_b, o * n_inner + 1) for o in range(1, n_outer)
    ]
    send_b = [((o - 1) * n_inner + last_a, o * n_inner + 1) for o in range(1, n_outer)] + [
        ((o - 1) * n_inner + last_b, o * n_inner) for o in range(1, n_outer)
    ]
    recv_a = lax.ppermute(kv_own, both, send_a)
    recv_b = lax.ppermute(kv_own, both, send_b)
    first = inner_id == 0
    kv_prev_a = jnp.where(first, recv_a, recv_b)
    kv_prev_b = jnp.where(first, recv_b, recv_a)

    unit_id = outer_id * n_units + inner_id
    before = jnp.maximum(outer_id - 1, 0)
    has_prev = (outer_id > 0) & (inner_id < 2)
    has_partner = inner_id % 2 == 1
    query_doc = docs_all[outer_id, inner_id]
    query_pos = unit_id * tok_dev + offsets
    partner_doc = jnp.where(has_partner, docs_all[outer_id, jnp.maximum(inner_id - 1, 0)], -3)
    prev_a_doc = jnp.where(has_prev, docs_all[before, last_a], -4)
    prev_b_doc = jnp.where(has_prev, docs_all[before, last_b], -5)
    key_doc = jnp.concatenate([prev_a_doc, prev_b_doc, partner_doc, query_doc])
    key_pos = jnp.concatenate(
        [
            (before * n_units + last_a) * tok_dev + offsets,
            (before * n_units + last_b) * tok_dev + offsets,
            (unit_id - 1) * tok_dev + offsets,
            query_pos,
        ]
    )
    ctx = jnp.concatenate([kv_prev_a, kv_prev_b, kv_partner, kv_own])
    attn, q_grads, k_grads, v_grads = attend(
        query_buf,
        grad_buf,
        query_pos,
        query_doc,
        ctx[:, :head_dim],
        ctx[:, head_dim:],
        key_pos,
        key_doc,
        n_heads,
    )
    kv_grads = jnp.concatenate([k_grads, v_grads], axis=1).reshape(4, tok_dev, 2 * head_dim)

    pairs_down = [(b, a) for a, b in pairs_up]
    from_partner = lax.ppermute(kv_grads[2], "inner", pairs_down)
    back_a = [(b, a) for a, b in send_a]
    back_b = [(b, a) for a, b in send_b]
    grads_a = jnp.where(first, kv_grads[0], kv_grads[1])
    grads_b = jnp.where(first, kv_grads[1], kv_grads[0])
    from_next_a = lax.ppermute(grads_a, both, back_a)
    from_next_b = lax.ppermute(grads_b, both, back_b)
    kv_total = (kv_grads[3] + from_partner + from_next_a + from_next_b).astype(jnp.bfloat16)

    result = jnp.concatenate([attn, q_grads, kv_total], axis=-1).reshape(
        n_inner, piece_len, -1
    )
    returned = lax.all_to_all(result, "inner", 0, 0, tiled=True)
    shape_q = (1, n_units, 1, piece_len, width_q)
    shape_k = (1, n_units, 1, piece_len, head_dim)
    return (
        returned[..., :width_q].reshape(shape_q),
        returned[..., width_q : 2 * width_q].reshape(shape_q),
        returned[..., 2 * width_q : 2 * width_q + head_dim].reshape(shape_k),
        returned[..., 2 * width_q + head_dim :].reshape(shape_k),
    )


def solution(mesh):
    return jax.shard_map(
        shards,
        mesh=mesh,
        in_specs=(
            P("outer", None, "inner", None, None),
            P("outer", None, "inner", None, None),
            P("outer", None, "inner", None, None),
            P("outer", None, "inner", None, None),
            P(),
        ),
        out_specs=(
            P("outer", None, "inner", None, None),
            P("outer", None, "inner", None, None),
            P("outer", None, "inner", None, None),
            P("outer", None, "inner", None, None),
        ),
        check_vma=False,
    )
```

```python
import math

import jax
import jax.numpy as jnp
from jax import lax
from jax.sharding import PartitionSpec as P


def doc_table(doc_starts, tok_dev):
    n_outer, n_inner, n_slots = doc_starts.shape
    flat_starts = doc_starts.reshape(n_outer * n_inner, n_slots)
    start_counts = jnp.sum((flat_starts < tok_dev).astype(jnp.int32), axis=1)
    first_index = jnp.cumsum(start_counts) - start_counts
    offsets = jnp.arange(tok_dev, dtype=jnp.int32)
    inside_count = jnp.sum(
        (flat_starts[:, None, :] <= offsets[None, :, None]).astype(jnp.int32), axis=2
    )
    return (first_index[:, None] + inside_count - 1).reshape(n_outer, n_inner, tok_dev)


def attend(
    query_buf, grad_buf, query_pos, query_doc, key_buf, value_buf, key_pos, key_doc, n_heads
):
    n_rows = query_buf.shape[0]
    head_dim = key_buf.shape[1]
    scaling = 1.0 / math.sqrt(head_dim)
    q_three = query_buf.reshape(n_rows, n_heads, head_dim)
    g_three = grad_buf.reshape(n_rows, n_heads, head_dim)
    scores = (
        jnp.einsum("qhd,kd->hqk", q_three, key_buf, preferred_element_type=jnp.float32) * scaling
    )
    allowed = (query_doc[:, None] == key_doc[None, :]) & (key_pos[None, :] <= query_pos[:, None])
    scores = jnp.where(allowed[None], scores, -jnp.inf)
    row_max = jnp.max(scores, axis=2, keepdims=True)
    log_total = row_max + jnp.log(jnp.sum(jnp.exp(scores - row_max), axis=2, keepdims=True))
    probs = jnp.exp(scores - log_total)
    probs_low = probs.astype(jnp.bfloat16)
    attn = jnp.einsum(
        "hqk,kd->qhd", probs_low, value_buf, preferred_element_type=jnp.float32
    ).astype(jnp.bfloat16)
    inner_prod = jnp.sum(g_three.astype(jnp.float32) * attn.astype(jnp.float32), axis=2)
    grad_probs = jnp.einsum("qhd,kd->hqk", g_three, value_buf, preferred_element_type=jnp.float32)
    score_grads = (probs * (grad_probs - inner_prod.T[:, :, None])).astype(jnp.bfloat16)
    q_grads = (
        jnp.einsum("hqk,kd->qhd", score_grads, key_buf, preferred_element_type=jnp.float32)
        * scaling
    )
    k_grads = (
        jnp.einsum("hqk,qhd->kd", score_grads, q_three, preferred_element_type=jnp.float32)
        * scaling
    )
    v_grads = jnp.einsum("hqk,qhd->kd", probs_low, g_three, preferred_element_type=jnp.float32)
    return (
        attn.reshape(n_rows, -1),
        q_grads.astype(jnp.bfloat16).reshape(n_rows, -1),
        k_grads,
        v_grads,
    )


def shards(queries, keys, values, grad_out, doc_starts):
    n_inner = lax.axis_size("inner")
    n_outer = lax.axis_size("outer")
    n_units = queries.shape[1]
    piece_len = queries.shape[3]
    width_q = queries.shape[4]
    head_dim = keys.shape[4]
    n_heads = width_q // head_dim
    tok_dev = piece_len * n_inner
    outer_id = lax.axis_index("outer")
    inner_id = lax.axis_index("inner")
    docs_all = doc_table(doc_starts, tok_dev)
    offsets = jnp.arange(tok_dev, dtype=jnp.int32)

    kv_packed = jnp.concatenate([keys[0, :, 0], values[0, :, 0]], axis=-1)
    kv_own = lax.all_to_all(kv_packed, "inner", 0, 0, tiled=True).reshape(tok_dev, -1)
    qg_packed = jnp.concatenate([queries[0, :, 0], grad_out[0, :, 0]], axis=-1)
    qg_own = lax.all_to_all(qg_packed, "inner", 0, 0, tiled=True).reshape(tok_dev, -1)
    query_buf = qg_own[:, :width_q]
    grad_buf = qg_own[:, width_q:]

    pairs_up = [(2 * p, 2 * p + 1) for p in range(n_inner // 2)]
    kv_partner = lax.ppermute(kv_own, "inner", pairs_up)

    both = ("outer", "inner")
    last_a, last_b = n_inner - 2, n_inner - 1
    send_a = [((o - 1) * n_inner + last_a, o * n_inner) for o in range(1, n_outer)] + [
        ((o - 1) * n_inner + last_b, o * n_inner + 1) for o in range(1, n_outer)
    ]
    send_b = [((o - 1) * n_inner + last_a, o * n_inner + 1) for o in range(1, n_outer)] + [
        ((o - 1) * n_inner + last_b, o * n_inner) for o in range(1, n_outer)
    ]
    recv_a = lax.ppermute(kv_own, both, send_a)
    recv_b = lax.ppermute(kv_own, both, send_b)
    first = inner_id == 0
    kv_prev_a = jnp.where(first, recv_a, recv_b)
    kv_prev_b = jnp.where(first, recv_b, recv_a)

    unit_id = outer_id * n_units + inner_id
    before = jnp.maximum(outer_id - 1, 0)
    has_prev = (outer_id > 0) & (inner_id < 2)
    has_partner = inner_id % 2 == 1
    query_doc = docs_all[outer_id, inner_id]
    query_pos = unit_id * tok_dev + offsets
    partner_doc = jnp.where(has_partner, docs_all[outer_id, jnp.maximum(inner_id - 1, 0)], -3)
    prev_a_doc = jnp.where(has_prev, docs_all[before, last_a], -4)
    prev_b_doc = jnp.where(has_prev, docs_all[before, last_b], -5)
    key_doc = jnp.concatenate([prev_a_doc, prev_b_doc, partner_doc, query_doc])
    key_pos = jnp.concatenate(
        [
            (before * n_units + last_a) * tok_dev + offsets,
            (before * n_units + last_b) * tok_dev + offsets,
            (unit_id - 1) * tok_dev + offsets,
            query_pos,
        ]
    )
    ctx = jnp.concatenate([kv_prev_a, kv_prev_b, kv_partner, kv_own])
    attn, q_grads, k_grads, v_grads = attend(
        query_buf,
        grad_buf,
        query_pos,
        query_doc,
        ctx[:, :head_dim],
        ctx[:, head_dim:],
        key_pos,
        key_doc,
        n_heads,
    )
    kv_grads = jnp.concatenate([k_grads, v_grads], axis=1).reshape(4, tok_dev, 2 * head_dim)

    pairs_down = [(b, a) for a, b in pairs_up]
    from_partner = lax.ppermute(kv_grads[2], "inner", pairs_down)
    back_a = [(b, a) for a, b in send_a]
    back_b = [(b, a) for a, b in send_b]
    grads_a = jnp.where(first, kv_grads[0], kv_grads[1])
    grads_b = jnp.where(first, kv_grads[1], kv_grads[0])
    from_next_a = lax.ppermute(grads_a, both, back_a)
    from_next_b = lax.ppermute(grads_b, both, back_b)
    kv_total = (kv_grads[3] + from_partner + from_next_a + from_next_b).astype(jnp.bfloat16)

    out_rows = jnp.concatenate([attn, q_grads], axis=-1).reshape(n_inner, piece_len, -1)
    out_back = lax.all_to_all(out_rows, "inner", 0, 0, tiled=True)
    kv_back = lax.all_to_all(
        kv_total.reshape(n_inner, piece_len, -1), "inner", 0, 0, tiled=True
    )
    shape_q = (1, n_units, 1, piece_len, width_q)
    shape_k = (1, n_units, 1, piece_len, head_dim)
    return (
        out_back[..., :width_q].reshape(shape_q),
        out_back[..., width_q:].reshape(shape_q),
        kv_back[..., :head_dim].reshape(shape_k),
        kv_back[..., head_dim:].reshape(shape_k),
    )


def solution(mesh):
    return jax.shard_map(
        shards,
        mesh=mesh,
        in_specs=(
            P("outer", None, "inner", None, None),
            P("outer", None, "inner", None, None),
            P("outer", None, "inner", None, None),
            P("outer", None, "inner", None, None),
            P(),
        ),
        out_specs=(
            P("outer", None, "inner", None, None),
            P("outer", None, "inner", None, None),
            P("outer", None, "inner", None, None),
            P("outer", None, "inner", None, None),
        ),
        check_vma=False,
    )
```

```python
import functools
import math

import jax
import jax.numpy as jnp
from jax import lax
from jax.experimental import pallas as pl
from jax.experimental.pallas import tpu as pltpu
from jax.sharding import PartitionSpec as P


def doc_table(doc_starts, tok_dev):
    n_outer, n_inner, n_slots = doc_starts.shape
    flat_starts = doc_starts.reshape(n_outer * n_inner, n_slots)
    start_counts = jnp.sum((flat_starts < tok_dev).astype(jnp.int32), axis=1)
    first_index = jnp.cumsum(start_counts) - start_counts
    offsets = jnp.arange(tok_dev, dtype=jnp.int32)
    inside_count = jnp.sum(
        (flat_starts[:, None, :] <= offsets[None, :, None]).astype(jnp.int32), axis=2
    )
    return (first_index[:, None] + inside_count - 1).reshape(n_outer, n_inner, tok_dev)


def attention_kernel(
    qdoc_ref, qpos_ref, kdoc_ref, kpos_ref, q_ref, g_ref, k_ref, v_ref,
    o_ref, dq_ref, dk_ref, dv_ref, *, scaling
):
    @pl.when((pl.program_id(0) == 0) & (pl.program_id(1) == 0))
    def _():
        dk_ref[...] = jnp.zeros_like(dk_ref)
        dv_ref[...] = jnp.zeros_like(dv_ref)

    q = q_ref[...]
    g = g_ref[...]
    k = k_ref[...]
    v = v_ref[...]
    contract_last = (((1,), (1,)), ((), ()))
    contract_first = (((0,), (0,)), ((), ()))
    scores = lax.dot_general(q, k, contract_last, preferred_element_type=jnp.float32) * scaling
    allowed = (qdoc_ref[...] == kdoc_ref[...]) & (kpos_ref[...] <= qpos_ref[...])
    scores = jnp.where(allowed, scores, -jnp.inf)
    row_max = jnp.max(scores, axis=1, keepdims=True)
    log_total = row_max + jnp.log(jnp.sum(jnp.exp(scores - row_max), axis=1, keepdims=True))
    probs = jnp.exp(scores - log_total)
    probs_low = probs.astype(jnp.bfloat16)
    attn = jnp.dot(probs_low, v, preferred_element_type=jnp.float32).astype(jnp.bfloat16)
    o_ref[...] = attn
    inner_prod = jnp.sum(
        g.astype(jnp.float32) * attn.astype(jnp.float32), axis=1, keepdims=True
    )
    grad_probs = lax.dot_general(g, v, contract_last, preferred_element_type=jnp.float32)
    score_grads = (probs * (grad_probs - inner_prod)).astype(jnp.bfloat16)
    dq_ref[...] = (
        jnp.dot(score_grads, k, preferred_element_type=jnp.float32) * scaling
    ).astype(jnp.bfloat16)
    dk_ref[...] += (
        lax.dot_general(score_grads, q, contract_first, preferred_element_type=jnp.float32)
        * scaling
    )
    dv_ref[...] += lax.dot_general(
        probs_low, g, contract_first, preferred_element_type=jnp.float32
    )


def attend(
    query_buf, grad_buf, query_pos, query_doc, key_buf, value_buf, key_pos, key_doc, n_heads
):
    n_rows, width_q = query_buf.shape
    n_keys, head_dim = key_buf.shape
    block_q = min(256, n_rows)
    grid = (n_rows // block_q, n_heads)
    row_spec = pl.BlockSpec((block_q, head_dim), lambda i, h: (i, h))
    col_spec = pl.BlockSpec((block_q, 1), lambda i, h: (i, 0))
    key_meta_spec = pl.BlockSpec((1, n_keys), lambda i, h: (0, 0))
    key_spec = pl.BlockSpec((n_keys, head_dim), lambda i, h: (0, 0))
    kernel = functools.partial(attention_kernel, scaling=1.0 / math.sqrt(head_dim))
    attn, q_grads, k_grads, v_grads = pl.pallas_call(
        kernel,
        grid=grid,
        in_specs=[col_spec, col_spec, key_meta_spec, key_meta_spec,
                  row_spec, row_spec, key_spec, key_spec],
        out_specs=[row_spec, row_spec, key_spec, key_spec],
        out_shape=[
            jax.ShapeDtypeStruct((n_rows, width_q), jnp.bfloat16),
            jax.ShapeDtypeStruct((n_rows, width_q), jnp.bfloat16),
            jax.ShapeDtypeStruct((n_keys, head_dim), jnp.float32),
            jax.ShapeDtypeStruct((n_keys, head_dim), jnp.float32),
        ],
        compiler_params=pltpu.CompilerParams(dimension_semantics=("arbitrary", "arbitrary")),
    )(
        query_doc.reshape(n_rows, 1),
        query_pos.reshape(n_rows, 1),
        key_doc.reshape(1, n_keys),
        key_pos.reshape(1, n_keys),
        query_buf,
        grad_buf,
        key_buf,
        value_buf,
    )
    return attn, q_grads, k_grads, v_grads


def shards(queries, keys, values, grad_out, doc_starts):
    n_inner = lax.axis_size("inner")
    n_outer = lax.axis_size("outer")
    n_units = queries.shape[1]
    piece_len = queries.shape[3]
    width_q = queries.shape[4]
    head_dim = keys.shape[4]
    n_heads = width_q // head_dim
    tok_dev = piece_len * n_inner
    outer_id = lax.axis_index("outer")
    inner_id = lax.axis_index("inner")
    docs_all = doc_table(doc_starts, tok_dev)
    offsets = jnp.arange(tok_dev, dtype=jnp.int32)

    packed = jnp.concatenate(
        [queries[0, :, 0], keys[0, :, 0], values[0, :, 0], grad_out[0, :, 0]], axis=-1
    )
    arrived = lax.all_to_all(packed, "inner", 0, 0, tiled=True).reshape(tok_dev, -1)
    query_buf = arrived[:, :width_q]
    kv_own = arrived[:, width_q : width_q + 2 * head_dim]
    grad_buf = arrived[:, width_q + 2 * head_dim :]

    pairs_up = [(2 * p, 2 * p + 1) for p in range(n_inner // 2)]
    kv_partner = lax.ppermute(kv_own, "inner", pairs_up)

    both = ("outer", "inner")
    last_a, last_b = n_inner - 2, n_inner - 1
    send_a = [((o - 1) * n_inner + last_a, o * n_inner) for o in range(1, n_outer)] + [
        ((o - 1) * n_inner + last_b, o * n_inner + 1) for o in range(1, n_outer)
    ]
    send_b = [((o - 1) * n_inner + last_a, o * n_inner + 1) for o in range(1, n_outer)] + [
        ((o - 1) * n_inner + last_b, o * n_inner) for o in range(1, n_outer)
    ]
    recv_a = lax.ppermute(kv_own, both, send_a)
    recv_b = lax.ppermute(kv_own, both, send_b)
    first = inner_id == 0
    kv_prev_a = jnp.where(first, recv_a, recv_b)
    kv_prev_b = jnp.where(first, recv_b, recv_a)

    unit_id = outer_id * n_units + inner_id
    before = jnp.maximum(outer_id - 1, 0)
    has_prev = (outer_id > 0) & (inner_id < 2)
    has_partner = inner_id % 2 == 1
    query_doc = docs_all[outer_id, inner_id]
    query_pos = unit_id * tok_dev + offsets
    partner_doc = jnp.where(has_partner, docs_all[outer_id, jnp.maximum(inner_id - 1, 0)], -3)
    prev_a_doc = jnp.where(has_prev, docs_all[before, last_a], -4)
    prev_b_doc = jnp.where(has_prev, docs_all[before, last_b], -5)
    key_doc = jnp.concatenate([prev_a_doc, prev_b_doc, partner_doc, query_doc])
    key_pos = jnp.concatenate(
        [
            (before * n_units + last_a) * tok_dev + offsets,
            (before * n_units + last_b) * tok_dev + offsets,
            (unit_id - 1) * tok_dev + offsets,
            query_pos,
        ]
    )
    ctx = jnp.concatenate([kv_prev_a, kv_prev_b, kv_partner, kv_own])
    attn, q_grads, k_grads, v_grads = attend(
        query_buf,
        grad_buf,
        query_pos,
        query_doc,
        ctx[:, :head_dim],
        ctx[:, head_dim:],
        key_pos,
        key_doc,
        n_heads,
    )
    kv_grads = jnp.concatenate([k_grads, v_grads], axis=1).reshape(4, tok_dev, 2 * head_dim)

    pairs_down = [(b, a) for a, b in pairs_up]
    from_partner = lax.ppermute(kv_grads[2], "inner", pairs_down)
    back_a = [(b, a) for a, b in send_a]
    back_b = [(b, a) for a, b in send_b]
    grads_a = jnp.where(first, kv_grads[0], kv_grads[1])
    grads_b = jnp.where(first, kv_grads[1], kv_grads[0])
    from_next_a = lax.ppermute(grads_a, both, back_a)
    from_next_b = lax.ppermute(grads_b, both, back_b)
    kv_total = (kv_grads[3] + from_partner + from_next_a + from_next_b).astype(jnp.bfloat16)

    result = jnp.concatenate([attn, q_grads, kv_total], axis=-1).reshape(
        n_inner, piece_len, -1
    )
    returned = lax.all_to_all(result, "inner", 0, 0, tiled=True)
    shape_q = (1, n_units, 1, piece_len, width_q)
    shape_k = (1, n_units, 1, piece_len, head_dim)
    return (
        returned[..., :width_q].reshape(shape_q),
        returned[..., width_q : 2 * width_q].reshape(shape_q),
        returned[..., 2 * width_q : 2 * width_q + head_dim].reshape(shape_k),
        returned[..., 2 * width_q + head_dim :].reshape(shape_k),
    )


def solution(mesh):
    return jax.shard_map(
        shards,
        mesh=mesh,
        in_specs=(
            P("outer", None, "inner", None, None),
            P("outer", None, "inner", None, None),
            P("outer", None, "inner", None, None),
            P("outer", None, "inner", None, None),
            P(),
        ),
        out_specs=(
            P("outer", None, "inner", None, None),
            P("outer", None, "inner", None, None),
            P("outer", None, "inner", None, None),
            P("outer", None, "inner", None, None),
        ),
        check_vma=False,
    )
```

```python
import functools
import math

import jax
import jax.numpy as jnp
from jax import lax
from jax.experimental import pallas as pl
from jax.experimental.pallas import tpu as pltpu
from jax.sharding import PartitionSpec as P


def doc_table(doc_starts, tok_dev):
    n_outer, n_inner, n_slots = doc_starts.shape
    flat_starts = doc_starts.reshape(n_outer * n_inner, n_slots)
    start_counts = jnp.sum((flat_starts < tok_dev).astype(jnp.int32), axis=1)
    first_index = jnp.cumsum(start_counts) - start_counts
    offsets = jnp.arange(tok_dev, dtype=jnp.int32)
    inside_count = jnp.sum(
        (flat_starts[:, None, :] <= offsets[None, :, None]).astype(jnp.int32), axis=2
    )
    return (first_index[:, None] + inside_count - 1).reshape(n_outer, n_inner, tok_dev)


def attention_kernel(
    qdoc_ref, qpos_ref, kdoc_ref, kpos_ref, q_ref, g_ref, k_ref, v_ref, kt_ref, vt_ref,
    o_ref, dq_ref, dkt_ref, dvt_ref, *, scaling
):
    @pl.when((pl.program_id(0) == 0) & (pl.program_id(1) == 0))
    def _():
        dkt_ref[...] = jnp.zeros_like(dkt_ref)
        dvt_ref[...] = jnp.zeros_like(dvt_ref)

    q = q_ref[...]
    g = g_ref[...]
    k = k_ref[...]
    v = v_ref[...]
    contract_first = (((0,), (0,)), ((), ()))
    scores = jnp.dot(q, kt_ref[...], preferred_element_type=jnp.float32) * scaling
    allowed = (qdoc_ref[...] == kdoc_ref[...]) & (kpos_ref[...] <= qpos_ref[...])
    scores = jnp.where(allowed, scores, -jnp.inf)
    row_max = jnp.max(scores, axis=1, keepdims=True)
    log_total = row_max + jnp.log(jnp.sum(jnp.exp(scores - row_max), axis=1, keepdims=True))
    probs = jnp.exp(scores - log_total)
    probs_low = probs.astype(jnp.bfloat16)
    attn = jnp.dot(probs_low, v, preferred_element_type=jnp.float32).astype(jnp.bfloat16)
    o_ref[...] = attn
    inner_prod = jnp.sum(
        g.astype(jnp.float32) * attn.astype(jnp.float32), axis=1, keepdims=True
    )
    grad_probs = jnp.dot(g, vt_ref[...], preferred_element_type=jnp.float32)
    score_grads = (probs * (grad_probs - inner_prod)).astype(jnp.bfloat16)
    dq_ref[...] = (
        jnp.dot(score_grads, k, preferred_element_type=jnp.float32) * scaling
    ).astype(jnp.bfloat16)
    dkt_ref[...] += (
        lax.dot_general(q, score_grads, contract_first, preferred_element_type=jnp.float32)
        * scaling
    )
    dvt_ref[...] += lax.dot_general(
        g, probs_low, contract_first, preferred_element_type=jnp.float32
    )


def attend(
    query_buf, grad_buf, query_pos, query_doc, key_buf, value_buf, key_pos, key_doc, n_heads
):
    n_rows, width_q = query_buf.shape
    n_keys, head_dim = key_buf.shape
    block_q = min(256, n_rows)
    grid = (n_rows // block_q, n_heads)
    row_spec = pl.BlockSpec((block_q, head_dim), lambda i, h: (i, h))
    col_spec = pl.BlockSpec((block_q, 1), lambda i, h: (i, 0))
    key_meta_spec = pl.BlockSpec((1, n_keys), lambda i, h: (0, 0))
    key_spec = pl.BlockSpec((n_keys, head_dim), lambda i, h: (0, 0))
    key_t_spec = pl.BlockSpec((head_dim, n_keys), lambda i, h: (0, 0))
    kernel = functools.partial(attention_kernel, scaling=1.0 / math.sqrt(head_dim))
    attn, q_grads, k_grads_t, v_grads_t = pl.pallas_call(
        kernel,
        grid=grid,
        in_specs=[col_spec, col_spec, key_meta_spec, key_meta_spec,
                  row_spec, row_spec, key_spec, key_spec, key_t_spec, key_t_spec],
        out_specs=[row_spec, row_spec, key_t_spec, key_t_spec],
        out_shape=[
            jax.ShapeDtypeStruct((n_rows, width_q), jnp.bfloat16),
            jax.ShapeDtypeStruct((n_rows, width_q), jnp.bfloat16),
            jax.ShapeDtypeStruct((head_dim, n_keys), jnp.float32),
            jax.ShapeDtypeStruct((head_dim, n_keys), jnp.float32),
        ],
        compiler_params=pltpu.CompilerParams(dimension_semantics=("arbitrary", "arbitrary")),
    )(
        query_doc.reshape(n_rows, 1),
        query_pos.reshape(n_rows, 1),
        key_doc.reshape(1, n_keys),
        key_pos.reshape(1, n_keys),
        query_buf,
        grad_buf,
        key_buf,
        value_buf,
        key_buf.T,
        value_buf.T,
    )
    return attn, q_grads, k_grads_t.T, v_grads_t.T


def shards(queries, keys, values, grad_out, doc_starts):
    n_inner = lax.axis_size("inner")
    n_outer = lax.axis_size("outer")
    n_units = queries.shape[1]
    piece_len = queries.shape[3]
    width_q = queries.shape[4]
    head_dim = keys.shape[4]
    n_heads = width_q // head_dim
    tok_dev = piece_len * n_inner
    outer_id = lax.axis_index("outer")
    inner_id = lax.axis_index("inner")
    docs_all = doc_table(doc_starts, tok_dev)
    offsets = jnp.arange(tok_dev, dtype=jnp.int32)

    packed = jnp.concatenate(
        [queries[0, :, 0], keys[0, :, 0], values[0, :, 0], grad_out[0, :, 0]], axis=-1
    )
    arrived = lax.all_to_all(packed, "inner", 0, 0, tiled=True).reshape(tok_dev, -1)
    query_buf = arrived[:, :width_q]
    kv_own = arrived[:, width_q : width_q + 2 * head_dim]
    grad_buf = arrived[:, width_q + 2 * head_dim :]

    pairs_up = [(2 * p, 2 * p + 1) for p in range(n_inner // 2)]
    kv_partner = lax.ppermute(kv_own, "inner", pairs_up)

    both = ("outer", "inner")
    last_a, last_b = n_inner - 2, n_inner - 1
    send_a = [((o - 1) * n_inner + last_a, o * n_inner) for o in range(1, n_outer)] + [
        ((o - 1) * n_inner + last_b, o * n_inner + 1) for o in range(1, n_outer)
    ]
    send_b = [((o - 1) * n_inner + last_a, o * n_inner + 1) for o in range(1, n_outer)] + [
        ((o - 1) * n_inner + last_b, o * n_inner) for o in range(1, n_outer)
    ]
    recv_a = lax.ppermute(kv_own, both, send_a)
    recv_b = lax.ppermute(kv_own, both, send_b)
    first = inner_id == 0
    kv_prev_a = jnp.where(first, recv_a, recv_b)
    kv_prev_b = jnp.where(first, recv_b, recv_a)

    unit_id = outer_id * n_units + inner_id
    before = jnp.maximum(outer_id - 1, 0)
    has_prev = (outer_id > 0) & (inner_id < 2)
    has_partner = inner_id % 2 == 1
    query_doc = docs_all[outer_id, inner_id]
    query_pos = unit_id * tok_dev + offsets
    partner_doc = jnp.where(has_partner, docs_all[outer_id, jnp.maximum(inner_id - 1, 0)], -3)
    prev_a_doc = jnp.where(has_prev, docs_all[before, last_a], -4)
    prev_b_doc = jnp.where(has_prev, docs_all[before, last_b], -5)
    key_doc = jnp.concatenate([prev_a_doc, prev_b_doc, partner_doc, query_doc])
    key_pos = jnp.concatenate(
        [
            (before * n_units + last_a) * tok_dev + offsets,
            (before * n_units + last_b) * tok_dev + offsets,
            (unit_id - 1) * tok_dev + offsets,
            query_pos,
        ]
    )
    ctx = jnp.concatenate([kv_prev_a, kv_prev_b, kv_partner, kv_own])
    attn, q_grads, k_grads, v_grads = attend(
        query_buf,
        grad_buf,
        query_pos,
        query_doc,
        ctx[:, :head_dim],
        ctx[:, head_dim:],
        key_pos,
        key_doc,
        n_heads,
    )
    kv_grads = jnp.concatenate([k_grads, v_grads], axis=1).reshape(4, tok_dev, 2 * head_dim)

    pairs_down = [(b, a) for a, b in pairs_up]
    from_partner = lax.ppermute(kv_grads[2], "inner", pairs_down)
    back_a = [(b, a) for a, b in send_a]
    back_b = [(b, a) for a, b in send_b]
    grads_a = jnp.where(first, kv_grads[0], kv_grads[1])
    grads_b = jnp.where(first, kv_grads[1], kv_grads[0])
    from_next_a = lax.ppermute(grads_a, both, back_a)
    from_next_b = lax.ppermute(grads_b, both, back_b)
    kv_total = (kv_grads[3] + from_partner + from_next_a + from_next_b).astype(jnp.bfloat16)

    result = jnp.concatenate([attn, q_grads, kv_total], axis=-1).reshape(
        n_inner, piece_len, -1
    )
    returned = lax.all_to_all(result, "inner", 0, 0, tiled=True)
    shape_q = (1, n_units, 1, piece_len, width_q)
    shape_k = (1, n_units, 1, piece_len, head_dim)
    return (
        returned[..., :width_q].reshape(shape_q),
        returned[..., width_q : 2 * width_q].reshape(shape_q),
        returned[..., 2 * width_q : 2 * width_q + head_dim].reshape(shape_k),
        returned[..., 2 * width_q + head_dim :].reshape(shape_k),
    )


def solution(mesh):
    return jax.shard_map(
        shards,
        mesh=mesh,
        in_specs=(
            P("outer", None, "inner", None, None),
            P("outer", None, "inner", None, None),
            P("outer", None, "inner", None, None),
            P("outer", None, "inner", None, None),
            P(),
        ),
        out_specs=(
            P("outer", None, "inner", None, None),
            P("outer", None, "inner", None, None),
            P("outer", None, "inner", None, None),
            P("outer", None, "inner", None, None),
        ),
        check_vma=False,
    )
```

```python
import functools
import math

import jax
import jax.numpy as jnp
from jax import lax
from jax.experimental import pallas as pl
from jax.experimental.pallas import tpu as pltpu
from jax.sharding import PartitionSpec as P


def doc_table(doc_starts, tok_dev):
    n_outer, n_inner, n_slots = doc_starts.shape
    flat_starts = doc_starts.reshape(n_outer * n_inner, n_slots)
    start_counts = jnp.sum((flat_starts < tok_dev).astype(jnp.int32), axis=1)
    first_index = jnp.cumsum(start_counts) - start_counts
    offsets = jnp.arange(tok_dev, dtype=jnp.int32)
    inside_count = jnp.sum(
        (flat_starts[:, None, :] <= offsets[None, :, None]).astype(jnp.int32), axis=2
    )
    return (first_index[:, None] + inside_count - 1).reshape(n_outer, n_inner, tok_dev)


def attention_kernel(
    flags_ref, qdoc_ref, qpos_ref, kdoc_ref, kpos_ref, q_ref, g_ref, k_ref, v_ref, kt_ref,
    vt_ref, o_ref, dq_ref, dkt_ref, dvt_ref, scores_ref, max_ref, sum_ref, acc_ref,
    *, scaling, n_chunks, chunk
):
    block = pl.program_id(0)

    @pl.when((block == 0) & (pl.program_id(1) == 0))
    def _():
        dkt_ref[...] = jnp.zeros_like(dkt_ref)
        dvt_ref[...] = jnp.zeros_like(dvt_ref)

    contract_first = (((0,), (0,)), ((), ()))
    q = q_ref[...]
    g = g_ref[...]
    qdoc = qdoc_ref[...]
    qpos = qpos_ref[...]
    max_ref[...] = jnp.full_like(max_ref, -jnp.inf)
    sum_ref[...] = jnp.zeros_like(sum_ref)
    acc_ref[...] = jnp.zeros_like(acc_ref)

    def cols(c):
        return slice(c * chunk, (c + 1) * chunk)

    for c in range(n_chunks):
        @pl.when(flags_ref[block, c] != 0)
        def _():
            scores = (
                jnp.dot(q, kt_ref[:, cols(c)], preferred_element_type=jnp.float32) * scaling
            )
            allowed = (qdoc == kdoc_ref[:, cols(c)]) & (kpos_ref[:, cols(c)] <= qpos)
            scores = jnp.where(allowed, scores, -jnp.inf)
            scores_ref[:, cols(c)] = scores
            max_ref[...] = jnp.maximum(max_ref[...], jnp.max(scores, axis=1, keepdims=True))

    row_max = max_ref[...]
    for c in range(n_chunks):
        @pl.when(flags_ref[block, c] != 0)
        def _():
            sum_ref[...] += jnp.sum(
                jnp.exp(scores_ref[:, cols(c)] - row_max), axis=1, keepdims=True
            )

    log_total = row_max + jnp.log(sum_ref[...])
    for c in range(n_chunks):
        @pl.when(flags_ref[block, c] != 0)
        def _():
            probs = jnp.exp(scores_ref[:, cols(c)] - log_total)
            scores_ref[:, cols(c)] = probs
            acc_ref[...] += jnp.dot(
                probs.astype(jnp.bfloat16), v_ref[cols(c), :],
                preferred_element_type=jnp.float32,
            )

    attn = acc_ref[...].astype(jnp.bfloat16)
    o_ref[...] = attn
    inner_prod = jnp.sum(
        g.astype(jnp.float32) * attn.astype(jnp.float32), axis=1, keepdims=True
    )
    acc_ref[...] = jnp.zeros_like(acc_ref)
    for c in range(n_chunks):
        @pl.when(flags_ref[block, c] != 0)
        def _():
            probs = scores_ref[:, cols(c)]
            probs_low = probs.astype(jnp.bfloat16)
            grad_probs = jnp.dot(g, vt_ref[:, cols(c)], preferred_element_type=jnp.float32)
            score_grads = (probs * (grad_probs - inner_prod)).astype(jnp.bfloat16)
            acc_ref[...] += jnp.dot(
                score_grads, k_ref[cols(c), :], preferred_element_type=jnp.float32
            )
            dkt_ref[:, cols(c)] += (
                lax.dot_general(q, score_grads, contract_first,
                                preferred_element_type=jnp.float32)
                * scaling
            )
            dvt_ref[:, cols(c)] += lax.dot_general(
                g, probs_low, contract_first, preferred_element_type=jnp.float32
            )

    dq_ref[...] = (acc_ref[...] * scaling).astype(jnp.bfloat16)


def attend(
    query_buf, grad_buf, query_pos, query_doc, key_buf, value_buf, key_pos, key_doc, n_heads
):
    n_rows, width_q = query_buf.shape
    n_keys, head_dim = key_buf.shape
    block_q = min(256, n_rows)
    chunk = min(256, n_keys)
    n_blocks = n_rows // block_q
    n_chunks = n_keys // chunk
    qd = query_doc.reshape(n_blocks, block_q)
    kd = key_doc.reshape(n_chunks, chunk)
    qp = query_pos.reshape(n_blocks, block_q)
    kp = key_pos.reshape(n_chunks, chunk)
    flags = (
        (jnp.min(qd, axis=1)[:, None] <= jnp.max(kd, axis=1)[None, :])
        & (jnp.min(kd, axis=1)[None, :] <= jnp.max(qd, axis=1)[:, None])
        & (jnp.min(kp, axis=1)[None, :] <= jnp.max(qp, axis=1)[:, None])
    ).astype(jnp.int32)
    grid = (n_blocks, n_heads)
    row_spec = pl.BlockSpec((block_q, head_dim), lambda i, h, f: (i, h))
    col_spec = pl.BlockSpec((block_q, 1), lambda i, h, f: (i, 0))
    key_meta_spec = pl.BlockSpec((1, n_keys), lambda i, h, f: (0, 0))
    key_spec = pl.BlockSpec((n_keys, head_dim), lambda i, h, f: (0, 0))
    key_t_spec = pl.BlockSpec((head_dim, n_keys), lambda i, h, f: (0, 0))
    kernel = functools.partial(
        attention_kernel, scaling=1.0 / math.sqrt(head_dim), n_chunks=n_chunks, chunk=chunk
    )
    attn, q_grads, k_grads_t, v_grads_t = pl.pallas_call(
        kernel,
        grid_spec=pltpu.PrefetchScalarGridSpec(
            num_scalar_prefetch=1,
            grid=grid,
            in_specs=[col_spec, col_spec, key_meta_spec, key_meta_spec,
                      row_spec, row_spec, key_spec, key_spec, key_t_spec, key_t_spec],
            out_specs=[row_spec, row_spec, key_t_spec, key_t_spec],
            scratch_shapes=[
                pltpu.VMEM((block_q, n_keys), jnp.float32),
                pltpu.VMEM((block_q, 1), jnp.float32),
                pltpu.VMEM((block_q, 1), jnp.float32),
                pltpu.VMEM((block_q, head_dim), jnp.float32),
            ],
        ),
        out_shape=[
            jax.ShapeDtypeStruct((n_rows, width_q), jnp.bfloat16),
            jax.ShapeDtypeStruct((n_rows, width_q), jnp.bfloat16),
            jax.ShapeDtypeStruct((head_dim, n_keys), jnp.float32),
            jax.ShapeDtypeStruct((head_dim, n_keys), jnp.float32),
        ],
        compiler_params=pltpu.CompilerParams(dimension_semantics=("arbitrary", "arbitrary")),
    )(
        flags,
        query_doc.reshape(n_rows, 1),
        query_pos.reshape(n_rows, 1),
        key_doc.reshape(1, n_keys),
        key_pos.reshape(1, n_keys),
        query_buf,
        grad_buf,
        key_buf,
        value_buf,
        key_buf.T,
        value_buf.T,
    )
    return attn, q_grads, k_grads_t.T, v_grads_t.T


def shards(queries, keys, values, grad_out, doc_starts):
    n_inner = lax.axis_size("inner")
    n_outer = lax.axis_size("outer")
    n_units = queries.shape[1]
    piece_len = queries.shape[3]
    width_q = queries.shape[4]
    head_dim = keys.shape[4]
    n_heads = width_q // head_dim
    tok_dev = piece_len * n_inner
    outer_id = lax.axis_index("outer")
    inner_id = lax.axis_index("inner")
    docs_all = doc_table(doc_starts, tok_dev)
    offsets = jnp.arange(tok_dev, dtype=jnp.int32)

    packed = jnp.concatenate(
        [queries[0, :, 0], keys[0, :, 0], values[0, :, 0], grad_out[0, :, 0]], axis=-1
    )
    arrived = lax.all_to_all(packed, "inner", 0, 0, tiled=True).reshape(tok_dev, -1)
    query_buf = arrived[:, :width_q]
    kv_own = arrived[:, width_q : width_q + 2 * head_dim]
    grad_buf = arrived[:, width_q + 2 * head_dim :]

    pairs_up = [(2 * p, 2 * p + 1) for p in range(n_inner // 2)]
    kv_partner = lax.ppermute(kv_own, "inner", pairs_up)

    both = ("outer", "inner")
    last_a, last_b = n_inner - 2, n_inner - 1
    send_a = [((o - 1) * n_inner + last_a, o * n_inner) for o in range(1, n_outer)] + [
        ((o - 1) * n_inner + last_b, o * n_inner + 1) for o in range(1, n_outer)
    ]
    send_b = [((o - 1) * n_inner + last_a, o * n_inner + 1) for o in range(1, n_outer)] + [
        ((o - 1) * n_inner + last_b, o * n_inner) for o in range(1, n_outer)
    ]
    recv_a = lax.ppermute(kv_own, both, send_a)
    recv_b = lax.ppermute(kv_own, both, send_b)
    first = inner_id == 0
    kv_prev_a = jnp.where(first, recv_a, recv_b)
    kv_prev_b = jnp.where(first, recv_b, recv_a)

    unit_id = outer_id * n_units + inner_id
    before = jnp.maximum(outer_id - 1, 0)
    has_prev = (outer_id > 0) & (inner_id < 2)
    has_partner = inner_id % 2 == 1
    query_doc = docs_all[outer_id, inner_id]
    query_pos = unit_id * tok_dev + offsets
    partner_doc = jnp.where(has_partner, docs_all[outer_id, jnp.maximum(inner_id - 1, 0)], -3)
    prev_a_doc = jnp.where(has_prev, docs_all[before, last_a], -4)
    prev_b_doc = jnp.where(has_prev, docs_all[before, last_b], -5)
    key_doc = jnp.concatenate([prev_a_doc, prev_b_doc, partner_doc, query_doc])
    key_pos = jnp.concatenate(
        [
            (before * n_units + last_a) * tok_dev + offsets,
            (before * n_units + last_b) * tok_dev + offsets,
            (unit_id - 1) * tok_dev + offsets,
            query_pos,
        ]
    )
    ctx = jnp.concatenate([kv_prev_a, kv_prev_b, kv_partner, kv_own])
    attn, q_grads, k_grads, v_grads = attend(
        query_buf,
        grad_buf,
        query_pos,
        query_doc,
        ctx[:, :head_dim],
        ctx[:, head_dim:],
        key_pos,
        key_doc,
        n_heads,
    )
    kv_grads = jnp.concatenate([k_grads, v_grads], axis=1).reshape(4, tok_dev, 2 * head_dim)

    pairs_down = [(b, a) for a, b in pairs_up]
    from_partner = lax.ppermute(kv_grads[2], "inner", pairs_down)
    back_a = [(b, a) for a, b in send_a]
    back_b = [(b, a) for a, b in send_b]
    grads_a = jnp.where(first, kv_grads[0], kv_grads[1])
    grads_b = jnp.where(first, kv_grads[1], kv_grads[0])
    from_next_a = lax.ppermute(grads_a, both, back_a)
    from_next_b = lax.ppermute(grads_b, both, back_b)
    kv_total = (kv_grads[3] + from_partner + from_next_a + from_next_b).astype(jnp.bfloat16)

    result = jnp.concatenate([attn, q_grads, kv_total], axis=-1).reshape(
        n_inner, piece_len, -1
    )
    returned = lax.all_to_all(result, "inner", 0, 0, tiled=True)
    shape_q = (1, n_units, 1, piece_len, width_q)
    shape_k = (1, n_units, 1, piece_len, head_dim)
    return (
        returned[..., :width_q].reshape(shape_q),
        returned[..., width_q : 2 * width_q].reshape(shape_q),
        returned[..., 2 * width_q : 2 * width_q + head_dim].reshape(shape_k),
        returned[..., 2 * width_q + head_dim :].reshape(shape_k),
    )


def solution(mesh):
    return jax.shard_map(
        shards,
        mesh=mesh,
        in_specs=(
            P("outer", None, "inner", None, None),
            P("outer", None, "inner", None, None),
            P("outer", None, "inner", None, None),
            P("outer", None, "inner", None, None),
            P(),
        ),
        out_specs=(
            P("outer", None, "inner", None, None),
            P("outer", None, "inner", None, None),
            P("outer", None, "inner", None, None),
            P("outer", None, "inner", None, None),
        ),
        check_vma=False,
    )
```

```python
import functools
import math

import jax
import jax.numpy as jnp
from jax import lax
from jax.experimental import pallas as pl
from jax.experimental.pallas import tpu as pltpu
from jax.sharding import PartitionSpec as P


def doc_table(doc_starts, tok_dev):
    n_outer, n_inner, n_slots = doc_starts.shape
    flat_starts = doc_starts.reshape(n_outer * n_inner, n_slots)
    start_counts = jnp.sum((flat_starts < tok_dev).astype(jnp.int32), axis=1)
    first_index = jnp.cumsum(start_counts) - start_counts
    offsets = jnp.arange(tok_dev, dtype=jnp.int32)
    inside_count = jnp.sum(
        (flat_starts[:, None, :] <= offsets[None, :, None]).astype(jnp.int32), axis=2
    )
    return (first_index[:, None] + inside_count - 1).reshape(n_outer, n_inner, tok_dev)


def attention_kernel(
    qdoc_ref, qpos_ref, kdoc_ref, kpos_ref, q_ref, g_ref, k_ref, v_ref, kt_ref, vt_ref,
    o_ref, dq_ref, dkt_ref, dvt_ref, *, scaling
):
    @pl.when((pl.program_id(0) == 0) & (pl.program_id(1) == 0))
    def _():
        dkt_ref[...] = jnp.zeros_like(dkt_ref)
        dvt_ref[...] = jnp.zeros_like(dvt_ref)

    q = q_ref[...]
    g = g_ref[...]
    k = k_ref[...]
    v = v_ref[...]
    contract_first = (((0,), (0,)), ((), ()))
    scores = jnp.dot(q, kt_ref[...], preferred_element_type=jnp.float32) * scaling
    allowed = (qdoc_ref[...] == kdoc_ref[...]) & (kpos_ref[...] <= qpos_ref[...])
    scores = jnp.where(allowed, scores, -jnp.inf)
    row_max = jnp.max(scores, axis=1, keepdims=True)
    log_total = row_max + jnp.log(jnp.sum(jnp.exp(scores - row_max), axis=1, keepdims=True))
    probs = jnp.exp(scores - log_total)
    probs_low = probs.astype(jnp.bfloat16)
    attn = jnp.dot(probs_low, v, preferred_element_type=jnp.float32).astype(jnp.bfloat16)
    o_ref[...] = attn
    inner_prod = jnp.sum(
        g.astype(jnp.float32) * attn.astype(jnp.float32), axis=1, keepdims=True
    )
    grad_probs = jnp.dot(g, vt_ref[...], preferred_element_type=jnp.float32)
    score_grads = (probs * (grad_probs - inner_prod)).astype(jnp.bfloat16)
    dq_ref[...] = (
        jnp.dot(score_grads, k, preferred_element_type=jnp.float32) * scaling
    ).astype(jnp.bfloat16)
    dkt_ref[...] += (
        lax.dot_general(q, score_grads, contract_first, preferred_element_type=jnp.float32)
        * scaling
    )
    dvt_ref[...] += lax.dot_general(
        g, probs_low, contract_first, preferred_element_type=jnp.float32
    )


def attend(
    query_buf, grad_buf, query_pos, query_doc, key_buf, value_buf, key_pos, key_doc, n_heads
):
    n_rows, width_q = query_buf.shape
    n_keys, head_dim = key_buf.shape
    block_q = min(256, n_rows)
    grid = (n_rows // block_q, n_heads)
    row_spec = pl.BlockSpec((block_q, head_dim), lambda i, h: (i, h))
    col_spec = pl.BlockSpec((block_q, 1), lambda i, h: (i, 0))
    key_meta_spec = pl.BlockSpec((1, n_keys), lambda i, h: (0, 0))
    key_spec = pl.BlockSpec((n_keys, head_dim), lambda i, h: (0, 0))
    key_t_spec = pl.BlockSpec((head_dim, n_keys), lambda i, h: (0, 0))
    kernel = functools.partial(attention_kernel, scaling=1.0 / math.sqrt(head_dim))
    attn, q_grads, k_grads_t, v_grads_t = pl.pallas_call(
        kernel,
        grid=grid,
        in_specs=[col_spec, col_spec, key_meta_spec, key_meta_spec,
                  row_spec, row_spec, key_spec, key_spec, key_t_spec, key_t_spec],
        out_specs=[row_spec, row_spec, key_t_spec, key_t_spec],
        out_shape=[
            jax.ShapeDtypeStruct((n_rows, width_q), jnp.bfloat16),
            jax.ShapeDtypeStruct((n_rows, width_q), jnp.bfloat16),
            jax.ShapeDtypeStruct((head_dim, n_keys), jnp.float32),
            jax.ShapeDtypeStruct((head_dim, n_keys), jnp.float32),
        ],
        compiler_params=pltpu.CompilerParams(dimension_semantics=("arbitrary", "arbitrary")),
    )(
        query_doc.reshape(n_rows, 1),
        query_pos.reshape(n_rows, 1),
        key_doc.reshape(1, n_keys),
        key_pos.reshape(1, n_keys),
        query_buf,
        grad_buf,
        key_buf,
        value_buf,
        key_buf.T,
        value_buf.T,
    )
    return attn, q_grads, k_grads_t.T, v_grads_t.T


def shards(queries, keys, values, grad_out, doc_starts):
    n_inner = lax.axis_size("inner")
    n_outer = lax.axis_size("outer")
    n_units = queries.shape[1]
    piece_len = queries.shape[3]
    width_q = queries.shape[4]
    head_dim = keys.shape[4]
    n_heads = width_q // head_dim
    tok_dev = piece_len * n_inner
    outer_id = lax.axis_index("outer")
    inner_id = lax.axis_index("inner")
    docs_all = doc_table(doc_starts, tok_dev)
    offsets = jnp.arange(tok_dev, dtype=jnp.int32)

    packed = jnp.concatenate(
        [queries[0, :, 0], keys[0, :, 0], values[0, :, 0], grad_out[0, :, 0]], axis=-1
    )
    arrived = lax.all_to_all(packed, "inner", 0, 0, tiled=True).reshape(tok_dev, -1)
    query_buf = arrived[:, :width_q]
    kv_own = arrived[:, width_q : width_q + 2 * head_dim]
    grad_buf = arrived[:, width_q + 2 * head_dim :]

    pairs_up = [(2 * p, 2 * p + 1) for p in range(n_inner // 2)]
    kv_partner = lax.ppermute(kv_own, "inner", pairs_up)

    both = ("outer", "inner")
    last_a, last_b = n_inner - 2, n_inner - 1
    send_a = [((o - 1) * n_inner + last_a, o * n_inner) for o in range(1, n_outer)] + [
        ((o - 1) * n_inner + last_b, o * n_inner + 1) for o in range(1, n_outer)
    ]
    send_b = [((o - 1) * n_inner + last_a, o * n_inner + 1) for o in range(1, n_outer)] + [
        ((o - 1) * n_inner + last_b, o * n_inner) for o in range(1, n_outer)
    ]
    recv_a = lax.ppermute(kv_own, both, send_a)
    recv_b = lax.ppermute(kv_own, both, send_b)
    first = inner_id == 0
    kv_prev_a = jnp.where(first, recv_a, recv_b)
    kv_prev_b = jnp.where(first, recv_b, recv_a)

    unit_id = outer_id * n_units + inner_id
    before = jnp.maximum(outer_id - 1, 0)
    has_prev = (outer_id > 0) & (inner_id < 2)
    has_partner = inner_id % 2 == 1
    query_doc = docs_all[outer_id, inner_id]
    query_pos = unit_id * tok_dev + offsets
    partner_doc = jnp.where(has_partner, docs_all[outer_id, jnp.maximum(inner_id - 1, 0)], -3)
    prev_a_doc = jnp.where(has_prev, docs_all[before, last_a], -4)
    prev_b_doc = jnp.where(has_prev, docs_all[before, last_b], -5)
    key_doc = jnp.concatenate([prev_a_doc, prev_b_doc, partner_doc, query_doc])
    key_pos = jnp.concatenate(
        [
            (before * n_units + last_a) * tok_dev + offsets,
            (before * n_units + last_b) * tok_dev + offsets,
            (unit_id - 1) * tok_dev + offsets,
            query_pos,
        ]
    )
    n_slots = 4
    slot_kv = jnp.stack([kv_prev_a, kv_prev_b, kv_partner, kv_own])
    slot_doc = key_doc.reshape(n_slots, tok_dev)
    slot_pos = key_pos.reshape(n_slots, tok_dev)
    needed = (
        (jnp.min(slot_doc, axis=1) <= jnp.max(query_doc))
        & (jnp.max(slot_doc, axis=1) >= jnp.min(query_doc))
        & (jnp.min(slot_pos, axis=1) <= jnp.max(query_pos))
    )
    needed = needed | (jnp.arange(n_slots) == n_slots - 1)
    needed_i = needed.astype(jnp.int32)
    count = jnp.sum(needed_i)
    rank = jnp.where(
        needed, jnp.cumsum(needed_i) - 1, count + jnp.cumsum(1 - needed_i) - 1
    )
    slot_ids = jnp.arange(n_slots, dtype=jnp.int32)
    order = jnp.sum(
        jnp.where(rank[None, :] == slot_ids[:, None], slot_ids[None, :], 0), axis=1
    )
    kv_sorted = slot_kv[order]
    doc_sorted = slot_doc[order]
    pos_sorted = slot_pos[order]

    def branch(n_used):
        def run(kv_sorted, doc_sorted, pos_sorted):
            ctx = kv_sorted[:n_used].reshape(n_used * tok_dev, 2 * head_dim)
            attn, q_grads, k_grads, v_grads = attend(
                query_buf,
                grad_buf,
                query_pos,
                query_doc,
                ctx[:, :head_dim],
                ctx[:, head_dim:],
                pos_sorted[:n_used].reshape(-1),
                doc_sorted[:n_used].reshape(-1),
                n_heads,
            )
            grads = jnp.concatenate([k_grads, v_grads], axis=1).reshape(
                n_used, tok_dev, 2 * head_dim
            )
            grads = jnp.concatenate(
                [grads, jnp.zeros((n_slots - n_used, tok_dev, 2 * head_dim), jnp.float32)]
            )
            return attn, q_grads, grads

        return run

    attn, q_grads, grads_sorted = lax.switch(
        count - 1, [branch(n) for n in range(1, n_slots + 1)], kv_sorted, doc_sorted, pos_sorted
    )
    kv_grads = grads_sorted[rank]

    pairs_down = [(b, a) for a, b in pairs_up]
    from_partner = lax.ppermute(kv_grads[2], "inner", pairs_down)
    back_a = [(b, a) for a, b in send_a]
    back_b = [(b, a) for a, b in send_b]
    grads_a = jnp.where(first, kv_grads[0], kv_grads[1])
    grads_b = jnp.where(first, kv_grads[1], kv_grads[0])
    from_next_a = lax.ppermute(grads_a, both, back_a)
    from_next_b = lax.ppermute(grads_b, both, back_b)
    kv_total = (kv_grads[3] + from_partner + from_next_a + from_next_b).astype(jnp.bfloat16)

    result = jnp.concatenate([attn, q_grads, kv_total], axis=-1).reshape(
        n_inner, piece_len, -1
    )
    returned = lax.all_to_all(result, "inner", 0, 0, tiled=True)
    shape_q = (1, n_units, 1, piece_len, width_q)
    shape_k = (1, n_units, 1, piece_len, head_dim)
    return (
        returned[..., :width_q].reshape(shape_q),
        returned[..., width_q : 2 * width_q].reshape(shape_q),
        returned[..., 2 * width_q : 2 * width_q + head_dim].reshape(shape_k),
        returned[..., 2 * width_q + head_dim :].reshape(shape_k),
    )


def solution(mesh):
    return jax.shard_map(
        shards,
        mesh=mesh,
        in_specs=(
            P("outer", None, "inner", None, None),
            P("outer", None, "inner", None, None),
            P("outer", None, "inner", None, None),
            P("outer", None, "inner", None, None),
            P(),
        ),
        out_specs=(
            P("outer", None, "inner", None, None),
            P("outer", None, "inner", None, None),
            P("outer", None, "inner", None, None),
            P("outer", None, "inner", None, None),
        ),
        check_vma=False,
    )
```

```python
import functools
import math

import jax
import jax.numpy as jnp
from jax import lax
from jax.experimental import pallas as pl
from jax.experimental.pallas import tpu as pltpu
from jax.sharding import PartitionSpec as P


def doc_table(doc_starts, tok_dev):
    n_outer, n_inner, n_slots = doc_starts.shape
    flat_starts = doc_starts.reshape(n_outer * n_inner, n_slots)
    start_counts = jnp.sum((flat_starts < tok_dev).astype(jnp.int32), axis=1)
    first_index = jnp.cumsum(start_counts) - start_counts
    offsets = jnp.arange(tok_dev, dtype=jnp.int32)
    inside_count = jnp.sum(
        (flat_starts[:, None, :] <= offsets[None, :, None]).astype(jnp.int32), axis=2
    )
    return (first_index[:, None] + inside_count - 1).reshape(n_outer, n_inner, tok_dev)


def attention_kernel(
    qdoc_ref, qpos_ref, kdoc_ref, kpos_ref, q_ref, g_ref, k_ref, v_ref, kt_ref, vt_ref,
    o_ref, dq_ref, dkt_ref, dvt_ref, *, scaling
):
    @pl.when((pl.program_id(0) == 0) & (pl.program_id(1) == 0))
    def _():
        dkt_ref[...] = jnp.zeros_like(dkt_ref)
        dvt_ref[...] = jnp.zeros_like(dvt_ref)

    q = q_ref[...]
    g = g_ref[...]
    k = k_ref[...]
    v = v_ref[...]
    contract_first = (((0,), (0,)), ((), ()))
    scores = jnp.dot(q, kt_ref[...], preferred_element_type=jnp.float32) * scaling
    allowed = (qdoc_ref[...] == kdoc_ref[...]) & (kpos_ref[...] <= qpos_ref[...])
    scores = jnp.where(allowed, scores, -jnp.inf)
    row_max = jnp.max(scores, axis=1, keepdims=True)
    log_total = row_max + jnp.log(jnp.sum(jnp.exp(scores - row_max), axis=1, keepdims=True))
    probs = jnp.exp(scores - log_total)
    probs_low = probs.astype(jnp.bfloat16)
    attn = jnp.dot(probs_low, v, preferred_element_type=jnp.float32).astype(jnp.bfloat16)
    o_ref[...] = attn
    inner_prod = jnp.sum(
        g.astype(jnp.float32) * attn.astype(jnp.float32), axis=1, keepdims=True
    )
    grad_probs = jnp.dot(g, vt_ref[...], preferred_element_type=jnp.float32)
    score_grads = (probs * (grad_probs - inner_prod)).astype(jnp.bfloat16)
    dq_ref[...] = (
        jnp.dot(score_grads, k, preferred_element_type=jnp.float32) * scaling
    ).astype(jnp.bfloat16)
    dkt_ref[...] += (
        lax.dot_general(q, score_grads, contract_first, preferred_element_type=jnp.float32)
        * scaling
    )
    dvt_ref[...] += lax.dot_general(
        g, probs_low, contract_first, preferred_element_type=jnp.float32
    )


def attend(rows, q_first, g_first, query_pos, query_doc, ctx, key_pos, key_doc, n_heads):
    n_rows = rows.shape[0]
    n_keys, kv_width = ctx.shape
    head_dim = kv_width // 2
    width_q = n_heads * head_dim
    block_q = min(256, n_rows)
    grid = (n_rows // block_q, n_heads)
    q_spec = pl.BlockSpec((block_q, head_dim), lambda i, h: (i, q_first + h))
    g_spec = pl.BlockSpec((block_q, head_dim), lambda i, h: (i, g_first + h))
    row_spec = pl.BlockSpec((block_q, head_dim), lambda i, h: (i, h))
    col_spec = pl.BlockSpec((block_q, 1), lambda i, h: (i, 0))
    key_meta_spec = pl.BlockSpec((1, n_keys), lambda i, h: (0, 0))
    k_spec = pl.BlockSpec((n_keys, head_dim), lambda i, h: (0, 0))
    v_spec = pl.BlockSpec((n_keys, head_dim), lambda i, h: (0, 1))
    kt_spec = pl.BlockSpec((head_dim, n_keys), lambda i, h: (0, 0))
    vt_spec = pl.BlockSpec((head_dim, n_keys), lambda i, h: (1, 0))
    key_t_spec = pl.BlockSpec((head_dim, n_keys), lambda i, h: (0, 0))
    ctx_t = ctx.T
    kernel = functools.partial(attention_kernel, scaling=1.0 / math.sqrt(head_dim))
    attn, q_grads, k_grads_t, v_grads_t = pl.pallas_call(
        kernel,
        grid=grid,
        in_specs=[col_spec, col_spec, key_meta_spec, key_meta_spec,
                  q_spec, g_spec, k_spec, v_spec, kt_spec, vt_spec],
        out_specs=[row_spec, row_spec, key_t_spec, key_t_spec],
        out_shape=[
            jax.ShapeDtypeStruct((n_rows, width_q), jnp.bfloat16),
            jax.ShapeDtypeStruct((n_rows, width_q), jnp.bfloat16),
            jax.ShapeDtypeStruct((head_dim, n_keys), jnp.float32),
            jax.ShapeDtypeStruct((head_dim, n_keys), jnp.float32),
        ],
        compiler_params=pltpu.CompilerParams(dimension_semantics=("arbitrary", "arbitrary")),
    )(
        query_doc.reshape(n_rows, 1),
        query_pos.reshape(n_rows, 1),
        key_doc.reshape(1, n_keys),
        key_pos.reshape(1, n_keys),
        rows,
        rows,
        ctx,
        ctx,
        ctx_t,
        ctx_t,
    )
    return attn, q_grads, k_grads_t, v_grads_t


def shards(queries, keys, values, grad_out, doc_starts):
    n_inner = lax.axis_size("inner")
    n_outer = lax.axis_size("outer")
    n_units = queries.shape[1]
    piece_len = queries.shape[3]
    width_q = queries.shape[4]
    head_dim = keys.shape[4]
    n_heads = width_q // head_dim
    tok_dev = piece_len * n_inner
    outer_id = lax.axis_index("outer")
    inner_id = lax.axis_index("inner")
    docs_all = doc_table(doc_starts, tok_dev)
    offsets = jnp.arange(tok_dev, dtype=jnp.int32)

    packed = jnp.concatenate(
        [queries[0, :, 0], keys[0, :, 0], values[0, :, 0], grad_out[0, :, 0]], axis=-1
    )
    arrived = lax.all_to_all(packed, "inner", 0, 0, tiled=True).reshape(tok_dev, -1)
    kv_own = arrived[:, width_q : width_q + 2 * head_dim]

    pairs_up = [(2 * p, 2 * p + 1) for p in range(n_inner // 2)]
    kv_partner = lax.ppermute(kv_own, "inner", pairs_up)

    both = ("outer", "inner")
    last_a, last_b = n_inner - 2, n_inner - 1
    send_a = [((o - 1) * n_inner + last_a, o * n_inner) for o in range(1, n_outer)] + [
        ((o - 1) * n_inner + last_b, o * n_inner + 1) for o in range(1, n_outer)
    ]
    send_b = [((o - 1) * n_inner + last_a, o * n_inner + 1) for o in range(1, n_outer)] + [
        ((o - 1) * n_inner + last_b, o * n_inner) for o in range(1, n_outer)
    ]
    recv_a = lax.ppermute(kv_own, both, send_a)
    recv_b = lax.ppermute(kv_own, both, send_b)
    first = inner_id == 0
    kv_prev_a = jnp.where(first, recv_a, recv_b)
    kv_prev_b = jnp.where(first, recv_b, recv_a)

    unit_id = outer_id * n_units + inner_id
    before = jnp.maximum(outer_id - 1, 0)
    has_prev = (outer_id > 0) & (inner_id < 2)
    has_partner = inner_id % 2 == 1
    query_doc = docs_all[outer_id, inner_id]
    query_pos = unit_id * tok_dev + offsets
    partner_doc = jnp.where(has_partner, docs_all[outer_id, jnp.maximum(inner_id - 1, 0)], -3)
    prev_a_doc = jnp.where(has_prev, docs_all[before, last_a], -4)
    prev_b_doc = jnp.where(has_prev, docs_all[before, last_b], -5)
    key_doc = jnp.concatenate([prev_a_doc, prev_b_doc, partner_doc, query_doc])
    key_pos = jnp.concatenate(
        [
            (before * n_units + last_a) * tok_dev + offsets,
            (before * n_units + last_b) * tok_dev + offsets,
            (unit_id - 1) * tok_dev + offsets,
            query_pos,
        ]
    )
    n_slots = 4
    slot_kv = jnp.stack([kv_prev_a, kv_prev_b, kv_partner, kv_own])
    slot_doc = key_doc.reshape(n_slots, tok_dev)
    slot_pos = key_pos.reshape(n_slots, tok_dev)
    needed = (
        (jnp.min(slot_doc, axis=1) <= jnp.max(query_doc))
        & (jnp.max(slot_doc, axis=1) >= jnp.min(query_doc))
        & (jnp.min(slot_pos, axis=1) <= jnp.max(query_pos))
    )
    needed = needed | (jnp.arange(n_slots) == n_slots - 1)
    needed_i = needed.astype(jnp.int32)
    count = jnp.sum(needed_i)
    rank = jnp.where(
        needed, jnp.cumsum(needed_i) - 1, count + jnp.cumsum(1 - needed_i) - 1
    )
    slot_ids = jnp.arange(n_slots, dtype=jnp.int32)
    order = jnp.sum(
        jnp.where(rank[None, :] == slot_ids[:, None], slot_ids[None, :], 0), axis=1
    )
    kv_sorted = slot_kv[order]
    doc_sorted = slot_doc[order]
    pos_sorted = slot_pos[order]

    def branch(n_used):
        def run(kv_sorted, doc_sorted, pos_sorted):
            ctx = kv_sorted[:n_used].reshape(n_used * tok_dev, 2 * head_dim)
            attn, q_grads, k_grads_t, v_grads_t = attend(
                arrived,
                0,
                width_q // head_dim + 2,
                query_pos,
                query_doc,
                ctx,
                pos_sorted[:n_used].reshape(-1),
                doc_sorted[:n_used].reshape(-1),
                n_heads,
            )
            grads = jnp.concatenate([k_grads_t, v_grads_t], axis=0).T.reshape(
                n_used, tok_dev, 2 * head_dim
            )
            grads = jnp.concatenate(
                [grads, jnp.zeros((n_slots - n_used, tok_dev, 2 * head_dim), jnp.float32)]
            )
            return attn, q_grads, grads

        return run

    attn, q_grads, grads_sorted = lax.switch(
        count - 1, [branch(n) for n in range(1, n_slots + 1)], kv_sorted, doc_sorted, pos_sorted
    )
    kv_grads = grads_sorted[rank]

    pairs_down = [(b, a) for a, b in pairs_up]
    from_partner = lax.ppermute(kv_grads[2], "inner", pairs_down)
    back_a = [(b, a) for a, b in send_a]
    back_b = [(b, a) for a, b in send_b]
    grads_a = jnp.where(first, kv_grads[0], kv_grads[1])
    grads_b = jnp.where(first, kv_grads[1], kv_grads[0])
    from_next_a = lax.ppermute(grads_a, both, back_a)
    from_next_b = lax.ppermute(grads_b, both, back_b)
    kv_total = (kv_grads[3] + from_partner + from_next_a + from_next_b).astype(jnp.bfloat16)

    result = jnp.concatenate([attn, q_grads, kv_total], axis=-1).reshape(
        n_inner, piece_len, -1
    )
    returned = lax.all_to_all(result, "inner", 0, 0, tiled=True)
    shape_q = (1, n_units, 1, piece_len, width_q)
    shape_k = (1, n_units, 1, piece_len, head_dim)
    return (
        returned[..., :width_q].reshape(shape_q),
        returned[..., width_q : 2 * width_q].reshape(shape_q),
        returned[..., 2 * width_q : 2 * width_q + head_dim].reshape(shape_k),
        returned[..., 2 * width_q + head_dim :].reshape(shape_k),
    )


def solution(mesh):
    return jax.shard_map(
        shards,
        mesh=mesh,
        in_specs=(
            P("outer", None, "inner", None, None),
            P("outer", None, "inner", None, None),
            P("outer", None, "inner", None, None),
            P("outer", None, "inner", None, None),
            P(),
        ),
        out_specs=(
            P("outer", None, "inner", None, None),
            P("outer", None, "inner", None, None),
            P("outer", None, "inner", None, None),
            P("outer", None, "inner", None, None),
        ),
        check_vma=False,
    )
```

```python
import functools
import math

import jax
import jax.numpy as jnp
from jax import lax
from jax.experimental import pallas as pl
from jax.experimental.pallas import tpu as pltpu
from jax.sharding import PartitionSpec as P


def doc_table(doc_starts, tok_dev):
    n_outer, n_inner, n_slots = doc_starts.shape
    flat_starts = doc_starts.reshape(n_outer * n_inner, n_slots)
    start_counts = jnp.sum((flat_starts < tok_dev).astype(jnp.int32), axis=1)
    first_index = jnp.cumsum(start_counts) - start_counts
    offsets = jnp.arange(tok_dev, dtype=jnp.int32)
    inside_count = jnp.sum(
        (flat_starts[:, None, :] <= offsets[None, :, None]).astype(jnp.int32), axis=2
    )
    return (first_index[:, None] + inside_count - 1).reshape(n_outer, n_inner, tok_dev)


def attention_kernel(
    qmeta_ref, kmeta_ref, q_ref, g_ref, k_ref, v_ref, kt_ref, vt_ref,
    o_ref, dq_ref, dkt_ref, dvt_ref, *, scaling, n_heads, head_dim
):
    @pl.when(pl.program_id(0) == 0)
    def _():
        dkt_ref[...] = jnp.zeros_like(dkt_ref)
        dvt_ref[...] = jnp.zeros_like(dvt_ref)

    k = k_ref[...]
    v = v_ref[...]
    kt = kt_ref[...]
    vt = vt_ref[...]
    contract_first = (((0,), (0,)), ((), ()))
    allowed = (qmeta_ref[:, 0:1] == kmeta_ref[0:1, :]) & (
        kmeta_ref[1:2, :] <= qmeta_ref[:, 1:2]
    )
    for h in range(n_heads):
        cols = slice(h * head_dim, (h + 1) * head_dim)
        q = q_ref[:, cols]
        g = g_ref[:, cols]
        scores = jnp.dot(q, kt, preferred_element_type=jnp.float32) * scaling
        scores = jnp.where(allowed, scores, -jnp.inf)
        row_max = jnp.max(scores, axis=1, keepdims=True)
        log_total = row_max + jnp.log(
            jnp.sum(jnp.exp(scores - row_max), axis=1, keepdims=True)
        )
        probs = jnp.exp(scores - log_total)
        probs_low = probs.astype(jnp.bfloat16)
        attn = jnp.dot(probs_low, v, preferred_element_type=jnp.float32).astype(jnp.bfloat16)
        o_ref[:, cols] = attn
        inner_prod = jnp.sum(
            g.astype(jnp.float32) * attn.astype(jnp.float32), axis=1, keepdims=True
        )
        grad_probs = jnp.dot(g, vt, preferred_element_type=jnp.float32)
        score_grads = (probs * (grad_probs - inner_prod)).astype(jnp.bfloat16)
        dq_ref[:, cols] = (
            jnp.dot(score_grads, k, preferred_element_type=jnp.float32) * scaling
        ).astype(jnp.bfloat16)
        dkt_ref[...] += (
            lax.dot_general(q, score_grads, contract_first, preferred_element_type=jnp.float32)
            * scaling
        )
        dvt_ref[...] += lax.dot_general(
            g, probs_low, contract_first, preferred_element_type=jnp.float32
        )


def attend(rows, query_pos, query_doc, ctx, key_pos, key_doc, n_heads):
    n_rows = rows.shape[0]
    n_keys, kv_width = ctx.shape
    head_dim = kv_width // 2
    width_q = n_heads * head_dim
    block_q = min(256, n_rows)
    grid = (n_rows // block_q,)
    q_spec = pl.BlockSpec((block_q, width_q), lambda i: (i, 0))
    g_spec = pl.BlockSpec((block_q, width_q), lambda i: (i, 1))
    qmeta_spec = pl.BlockSpec((block_q, 2), lambda i: (i, 0))
    kmeta_spec = pl.BlockSpec((2, n_keys), lambda i: (0, 0))
    k_spec = pl.BlockSpec((n_keys, head_dim), lambda i: (0, 0))
    v_spec = pl.BlockSpec((n_keys, head_dim), lambda i: (0, 1))
    kt_spec = pl.BlockSpec((head_dim, n_keys), lambda i: (0, 0))
    vt_spec = pl.BlockSpec((head_dim, n_keys), lambda i: (1, 0))
    out_spec = pl.BlockSpec((block_q, width_q), lambda i: (i, 0))
    key_t_spec = pl.BlockSpec((head_dim, n_keys), lambda i: (0, 0))
    ctx_t = ctx.T
    kernel = functools.partial(
        attention_kernel,
        scaling=1.0 / math.sqrt(head_dim),
        n_heads=n_heads,
        head_dim=head_dim,
    )
    return pl.pallas_call(
        kernel,
        grid=grid,
        in_specs=[qmeta_spec, kmeta_spec, q_spec, g_spec, k_spec, v_spec, kt_spec, vt_spec],
        out_specs=[out_spec, out_spec, key_t_spec, key_t_spec],
        out_shape=[
            jax.ShapeDtypeStruct((n_rows, width_q), jnp.bfloat16),
            jax.ShapeDtypeStruct((n_rows, width_q), jnp.bfloat16),
            jax.ShapeDtypeStruct((head_dim, n_keys), jnp.float32),
            jax.ShapeDtypeStruct((head_dim, n_keys), jnp.float32),
        ],
        compiler_params=pltpu.CompilerParams(dimension_semantics=("arbitrary",)),
    )(
        jnp.stack([query_doc, query_pos], axis=1),
        jnp.stack([key_doc, key_pos]),
        rows,
        rows,
        ctx,
        ctx,
        ctx_t,
        ctx_t,
    )


def shards(queries, keys, values, grad_out, doc_starts):
    n_inner = lax.axis_size("inner")
    n_outer = lax.axis_size("outer")
    n_units = queries.shape[1]
    piece_len = queries.shape[3]
    width_q = queries.shape[4]
    head_dim = keys.shape[4]
    n_heads = width_q // head_dim
    tok_dev = piece_len * n_inner
    outer_id = lax.axis_index("outer")
    inner_id = lax.axis_index("inner")
    docs_all = doc_table(doc_starts, tok_dev)
    offsets = jnp.arange(tok_dev, dtype=jnp.int32)

    packed = jnp.concatenate(
        [queries[0, :, 0], grad_out[0, :, 0], keys[0, :, 0], values[0, :, 0]], axis=-1
    )
    arrived = lax.all_to_all(packed, "inner", 0, 0, tiled=True).reshape(tok_dev, -1)
    kv_own = arrived[:, 2 * width_q :]

    pairs_up = [(2 * p, 2 * p + 1) for p in range(n_inner // 2)]
    kv_partner = lax.ppermute(kv_own, "inner", pairs_up)

    both = ("outer", "inner")
    last_a, last_b = n_inner - 2, n_inner - 1
    send_a = [((o - 1) * n_inner + last_a, o * n_inner) for o in range(1, n_outer)] + [
        ((o - 1) * n_inner + last_b, o * n_inner + 1) for o in range(1, n_outer)
    ]
    send_b = [((o - 1) * n_inner + last_a, o * n_inner + 1) for o in range(1, n_outer)] + [
        ((o - 1) * n_inner + last_b, o * n_inner) for o in range(1, n_outer)
    ]
    recv_a = lax.ppermute(kv_own, both, send_a)
    recv_b = lax.ppermute(kv_own, both, send_b)
    first = inner_id == 0
    kv_prev_a = jnp.where(first, recv_a, recv_b)
    kv_prev_b = jnp.where(first, recv_b, recv_a)

    unit_id = outer_id * n_units + inner_id
    before = jnp.maximum(outer_id - 1, 0)
    has_prev = (outer_id > 0) & (inner_id < 2)
    has_partner = inner_id % 2 == 1
    query_doc = docs_all[outer_id, inner_id]
    query_pos = unit_id * tok_dev + offsets
    partner_doc = jnp.where(has_partner, docs_all[outer_id, jnp.maximum(inner_id - 1, 0)], -3)
    prev_a_doc = jnp.where(has_prev, docs_all[before, last_a], -4)
    prev_b_doc = jnp.where(has_prev, docs_all[before, last_b], -5)
    key_doc = jnp.concatenate([prev_a_doc, prev_b_doc, partner_doc, query_doc])
    key_pos = jnp.concatenate(
        [
            (before * n_units + last_a) * tok_dev + offsets,
            (before * n_units + last_b) * tok_dev + offsets,
            (unit_id - 1) * tok_dev + offsets,
            query_pos,
        ]
    )
    n_slots = 4
    slot_kv = jnp.stack([kv_prev_a, kv_prev_b, kv_partner, kv_own])
    slot_doc = key_doc.reshape(n_slots, tok_dev)
    slot_pos = key_pos.reshape(n_slots, tok_dev)
    needed = (
        (jnp.min(slot_doc, axis=1) <= jnp.max(query_doc))
        & (jnp.max(slot_doc, axis=1) >= jnp.min(query_doc))
        & (jnp.min(slot_pos, axis=1) <= jnp.max(query_pos))
    )
    needed = needed | (jnp.arange(n_slots) == n_slots - 1)
    needed_i = needed.astype(jnp.int32)
    count = jnp.sum(needed_i)
    rank = jnp.where(
        needed, jnp.cumsum(needed_i) - 1, count + jnp.cumsum(1 - needed_i) - 1
    )
    slot_ids = jnp.arange(n_slots, dtype=jnp.int32)
    order = jnp.sum(
        jnp.where(rank[None, :] == slot_ids[:, None], slot_ids[None, :], 0), axis=1
    )
    kv_sorted = slot_kv[order]
    doc_sorted = slot_doc[order]
    pos_sorted = slot_pos[order]

    def branch(n_used):
        def run(kv_sorted, doc_sorted, pos_sorted):
            ctx = kv_sorted[:n_used].reshape(n_used * tok_dev, 2 * head_dim)
            attn, q_grads, k_grads_t, v_grads_t = attend(
                arrived,
                query_pos,
                query_doc,
                ctx,
                pos_sorted[:n_used].reshape(-1),
                doc_sorted[:n_used].reshape(-1),
                n_heads,
            )
            grads = jnp.concatenate([k_grads_t, v_grads_t], axis=0).T.reshape(
                n_used, tok_dev, 2 * head_dim
            )
            grads = jnp.concatenate(
                [grads, jnp.zeros((n_slots - n_used, tok_dev, 2 * head_dim), jnp.float32)]
            )
            return attn, q_grads, grads

        return run

    attn, q_grads, grads_sorted = lax.switch(
        count - 1, [branch(n) for n in range(1, n_slots + 1)], kv_sorted, doc_sorted, pos_sorted
    )
    kv_grads = grads_sorted[rank]

    pairs_down = [(b, a) for a, b in pairs_up]
    from_partner = lax.ppermute(kv_grads[2], "inner", pairs_down)
    back_a = [(b, a) for a, b in send_a]
    back_b = [(b, a) for a, b in send_b]
    grads_a = jnp.where(first, kv_grads[0], kv_grads[1])
    grads_b = jnp.where(first, kv_grads[1], kv_grads[0])
    from_next_a = lax.ppermute(grads_a, both, back_a)
    from_next_b = lax.ppermute(grads_b, both, back_b)
    kv_total = (kv_grads[3] + from_partner + from_next_a + from_next_b).astype(jnp.bfloat16)

    result = jnp.concatenate([attn, q_grads, kv_total], axis=-1).reshape(
        n_inner, piece_len, -1
    )
    returned = lax.all_to_all(result, "inner", 0, 0, tiled=True)
    shape_q = (1, n_units, 1, piece_len, width_q)
    shape_k = (1, n_units, 1, piece_len, head_dim)
    return (
        returned[..., :width_q].reshape(shape_q),
        returned[..., width_q : 2 * width_q].reshape(shape_q),
        returned[..., 2 * width_q : 2 * width_q + head_dim].reshape(shape_k),
        returned[..., 2 * width_q + head_dim :].reshape(shape_k),
    )


def solution(mesh):
    return jax.shard_map(
        shards,
        mesh=mesh,
        in_specs=(
            P("outer", None, "inner", None, None),
            P("outer", None, "inner", None, None),
            P("outer", None, "inner", None, None),
            P("outer", None, "inner", None, None),
            P(),
        ),
        out_specs=(
            P("outer", None, "inner", None, None),
            P("outer", None, "inner", None, None),
            P("outer", None, "inner", None, None),
            P("outer", None, "inner", None, None),
        ),
        check_vma=False,
    )
```

```python
import functools
import math

import jax
import jax.numpy as jnp
from jax import lax
from jax.experimental import pallas as pl
from jax.experimental.pallas import tpu as pltpu
from jax.sharding import PartitionSpec as P


def doc_table(doc_starts, tok_dev):
    n_outer, n_inner, n_slots = doc_starts.shape
    flat_starts = doc_starts.reshape(n_outer * n_inner, n_slots)
    start_counts = jnp.sum((flat_starts < tok_dev).astype(jnp.int32), axis=1)
    first_index = jnp.cumsum(start_counts) - start_counts
    offsets = jnp.arange(tok_dev, dtype=jnp.int32)
    inside_count = jnp.sum(
        (flat_starts[:, None, :] <= offsets[None, :, None]).astype(jnp.int32), axis=2
    )
    return (first_index[:, None] + inside_count - 1).reshape(n_outer, n_inner, tok_dev)


def attention_kernel(
    qmeta_ref, kmeta_ref, q_ref, g_ref, k_ref, v_ref, kt_ref, vt_ref,
    o_ref, dq_ref, dkt_ref, dvt_ref, *, scaling, n_heads, head_dim
):
    @pl.when(pl.program_id(0) == 0)
    def _():
        dkt_ref[...] = jnp.zeros_like(dkt_ref)
        dvt_ref[...] = jnp.zeros_like(dvt_ref)

    k = k_ref[...]
    v = v_ref[...]
    kt = kt_ref[...]
    vt = vt_ref[...]
    contract_first = (((0,), (0,)), ((), ()))
    allowed = (qmeta_ref[:, 0:1] == kmeta_ref[0:1, :]) & (
        kmeta_ref[1:2, :] <= qmeta_ref[:, 1:2]
    )
    for h in range(n_heads):
        cols = slice(h * head_dim, (h + 1) * head_dim)
        q = q_ref[:, cols]
        g = g_ref[:, cols]
        scores = jnp.dot(q, kt, preferred_element_type=jnp.float32) * scaling
        scores = jnp.where(allowed, scores, -jnp.inf)
        row_max = jnp.max(scores, axis=1, keepdims=True)
        log_total = row_max + jnp.log(
            jnp.sum(jnp.exp(scores - row_max), axis=1, keepdims=True)
        )
        probs = jnp.exp(scores - log_total)
        probs_low = probs.astype(jnp.bfloat16)
        attn = jnp.dot(probs_low, v, preferred_element_type=jnp.float32).astype(jnp.bfloat16)
        o_ref[:, cols] = attn
        inner_prod = jnp.sum(
            g.astype(jnp.float32) * attn.astype(jnp.float32), axis=1, keepdims=True
        )
        grad_probs = jnp.dot(g, vt, preferred_element_type=jnp.float32)
        score_grads = (probs * (grad_probs - inner_prod)).astype(jnp.bfloat16)
        dq_ref[:, cols] = (
            jnp.dot(score_grads, k, preferred_element_type=jnp.float32) * scaling
        ).astype(jnp.bfloat16)
        dkt_ref[...] += (
            lax.dot_general(q, score_grads, contract_first, preferred_element_type=jnp.float32)
            * scaling
        )
        dvt_ref[...] += lax.dot_general(
            g, probs_low, contract_first, preferred_element_type=jnp.float32
        )


def attend(rows, query_pos, query_doc, ctx, key_pos, key_doc, n_heads):
    n_rows = rows.shape[0]
    n_keys, kv_width = ctx.shape
    head_dim = kv_width // 2
    width_q = n_heads * head_dim
    block_q = min(256, n_rows)
    grid = (n_rows // block_q,)
    q_spec = pl.BlockSpec((block_q, width_q), lambda i: (i, 0))
    g_spec = pl.BlockSpec((block_q, width_q), lambda i: (i, 1))
    qmeta_spec = pl.BlockSpec((block_q, 2), lambda i: (i, 0))
    kmeta_spec = pl.BlockSpec((2, n_keys), lambda i: (0, 0))
    k_spec = pl.BlockSpec((n_keys, head_dim), lambda i: (0, 0))
    v_spec = pl.BlockSpec((n_keys, head_dim), lambda i: (0, 1))
    kt_spec = pl.BlockSpec((head_dim, n_keys), lambda i: (0, 0))
    vt_spec = pl.BlockSpec((head_dim, n_keys), lambda i: (1, 0))
    out_spec = pl.BlockSpec((block_q, width_q), lambda i: (i, 0))
    key_t_spec = pl.BlockSpec((head_dim, n_keys), lambda i: (0, 0))
    ctx_t = ctx.T
    kernel = functools.partial(
        attention_kernel,
        scaling=1.0 / math.sqrt(head_dim),
        n_heads=n_heads,
        head_dim=head_dim,
    )
    return pl.pallas_call(
        kernel,
        grid=grid,
        in_specs=[qmeta_spec, kmeta_spec, q_spec, g_spec, k_spec, v_spec, kt_spec, vt_spec],
        out_specs=[out_spec, out_spec, key_t_spec, key_t_spec],
        out_shape=[
            jax.ShapeDtypeStruct((n_rows, width_q), jnp.bfloat16),
            jax.ShapeDtypeStruct((n_rows, width_q), jnp.bfloat16),
            jax.ShapeDtypeStruct((head_dim, n_keys), jnp.float32),
            jax.ShapeDtypeStruct((head_dim, n_keys), jnp.float32),
        ],
        compiler_params=pltpu.CompilerParams(dimension_semantics=("arbitrary",)),
    )(
        jnp.stack([query_doc, query_pos], axis=1),
        jnp.stack([key_doc, key_pos]),
        rows,
        rows,
        ctx,
        ctx,
        ctx_t,
        ctx_t,
    )


def shards(queries, keys, values, grad_out, doc_starts):
    n_inner = lax.axis_size("inner")
    n_outer = lax.axis_size("outer")
    n_units = queries.shape[1]
    piece_len = queries.shape[3]
    width_q = queries.shape[4]
    head_dim = keys.shape[4]
    n_heads = width_q // head_dim
    tok_dev = piece_len * n_inner
    outer_id = lax.axis_index("outer")
    inner_id = lax.axis_index("inner")
    docs_all = doc_table(doc_starts, tok_dev)
    offsets = jnp.arange(tok_dev, dtype=jnp.int32)

    packed = jnp.concatenate(
        [queries[0, :, 0], grad_out[0, :, 0], keys[0, :, 0], values[0, :, 0]], axis=-1
    )
    unit_local = (inner_id + 2 * outer_id) % n_units
    packed = jnp.roll(packed, -2 * outer_id, axis=0)
    arrived = lax.all_to_all(packed, "inner", 0, 0, tiled=True).reshape(tok_dev, -1)
    kv_own = arrived[:, 2 * width_q :]

    pairs_up = [(2 * p, 2 * p + 1) for p in range(n_inner // 2)]
    kv_partner = lax.ppermute(kv_own, "inner", pairs_up)

    both = ("outer", "inner")
    last_a, last_b = n_inner - 2, n_inner - 1
    lead = [(-2 * o) % n_inner for o in range(n_outer)]
    send_a = [((o - 1) * n_inner + lead[o] + r, o * n_inner + lead[o] + r)
              for o in range(1, n_outer) for r in range(2)]
    send_b = [((o - 1) * n_inner + lead[o] + r, o * n_inner + lead[o] + 1 - r)
              for o in range(1, n_outer) for r in range(2)]
    recv_a = lax.ppermute(kv_own, both, send_a)
    recv_b = lax.ppermute(kv_own, both, send_b)
    first = unit_local == 0
    kv_prev_a = jnp.where(first, recv_a, recv_b)
    kv_prev_b = jnp.where(first, recv_b, recv_a)

    unit_id = outer_id * n_units + unit_local
    before = jnp.maximum(outer_id - 1, 0)
    has_prev = (outer_id > 0) & (unit_local < 2)
    has_partner = unit_local % 2 == 1
    query_doc = docs_all[outer_id, unit_local]
    query_pos = unit_id * tok_dev + offsets
    partner_doc = jnp.where(has_partner, docs_all[outer_id, jnp.maximum(unit_local - 1, 0)], -3)
    prev_a_doc = jnp.where(has_prev, docs_all[before, last_a], -4)
    prev_b_doc = jnp.where(has_prev, docs_all[before, last_b], -5)
    key_doc = jnp.concatenate([prev_a_doc, prev_b_doc, partner_doc, query_doc])
    key_pos = jnp.concatenate(
        [
            (before * n_units + last_a) * tok_dev + offsets,
            (before * n_units + last_b) * tok_dev + offsets,
            (unit_id - 1) * tok_dev + offsets,
            query_pos,
        ]
    )
    n_slots = 4
    slot_kv = jnp.stack([kv_prev_a, kv_prev_b, kv_partner, kv_own])
    slot_doc = key_doc.reshape(n_slots, tok_dev)
    slot_pos = key_pos.reshape(n_slots, tok_dev)
    needed = (
        (jnp.min(slot_doc, axis=1) <= jnp.max(query_doc))
        & (jnp.max(slot_doc, axis=1) >= jnp.min(query_doc))
        & (jnp.min(slot_pos, axis=1) <= jnp.max(query_pos))
    )
    needed = needed | (jnp.arange(n_slots) == n_slots - 1)
    needed_i = needed.astype(jnp.int32)
    count = jnp.sum(needed_i)
    rank = jnp.where(
        needed, jnp.cumsum(needed_i) - 1, count + jnp.cumsum(1 - needed_i) - 1
    )
    slot_ids = jnp.arange(n_slots, dtype=jnp.int32)
    order = jnp.sum(
        jnp.where(rank[None, :] == slot_ids[:, None], slot_ids[None, :], 0), axis=1
    )
    kv_sorted = slot_kv[order]
    doc_sorted = slot_doc[order]
    pos_sorted = slot_pos[order]

    def branch(n_used):
        def run(kv_sorted, doc_sorted, pos_sorted):
            ctx = kv_sorted[:n_used].reshape(n_used * tok_dev, 2 * head_dim)
            attn, q_grads, k_grads_t, v_grads_t = attend(
                arrived,
                query_pos,
                query_doc,
                ctx,
                pos_sorted[:n_used].reshape(-1),
                doc_sorted[:n_used].reshape(-1),
                n_heads,
            )
            grads = jnp.concatenate([k_grads_t, v_grads_t], axis=0).T.reshape(
                n_used, tok_dev, 2 * head_dim
            )
            grads = jnp.concatenate(
                [grads, jnp.zeros((n_slots - n_used, tok_dev, 2 * head_dim), jnp.float32)]
            )
            return attn, q_grads, grads

        return run

    attn, q_grads, grads_sorted = lax.switch(
        count - 1, [branch(n) for n in range(1, n_slots + 1)], kv_sorted, doc_sorted, pos_sorted
    )
    kv_grads = grads_sorted[rank]

    pairs_down = [(b, a) for a, b in pairs_up]
    from_partner = lax.ppermute(kv_grads[2], "inner", pairs_down)
    back_a = [(b, a) for a, b in send_a]
    back_b = [(b, a) for a, b in send_b]
    grads_a = jnp.where(first, kv_grads[0], kv_grads[1])
    grads_b = jnp.where(first, kv_grads[1], kv_grads[0])
    from_next_a = lax.ppermute(grads_a, both, back_a)
    from_next_b = lax.ppermute(grads_b, both, back_b)
    kv_total = (kv_grads[3] + from_partner + from_next_a + from_next_b).astype(jnp.bfloat16)

    result = jnp.concatenate([attn, q_grads, kv_total], axis=-1).reshape(
        n_inner, piece_len, -1
    )
    returned = jnp.roll(
        lax.all_to_all(result, "inner", 0, 0, tiled=True), 2 * outer_id, axis=0
    )
    shape_q = (1, n_units, 1, piece_len, width_q)
    shape_k = (1, n_units, 1, piece_len, head_dim)
    return (
        returned[..., :width_q].reshape(shape_q),
        returned[..., width_q : 2 * width_q].reshape(shape_q),
        returned[..., 2 * width_q : 2 * width_q + head_dim].reshape(shape_k),
        returned[..., 2 * width_q + head_dim :].reshape(shape_k),
    )


def solution(mesh):
    return jax.shard_map(
        shards,
        mesh=mesh,
        in_specs=(
            P("outer", None, "inner", None, None),
            P("outer", None, "inner", None, None),
            P("outer", None, "inner", None, None),
            P("outer", None, "inner", None, None),
            P(),
        ),
        out_specs=(
            P("outer", None, "inner", None, None),
            P("outer", None, "inner", None, None),
            P("outer", None, "inner", None, None),
            P("outer", None, "inner", None, None),
        ),
        check_vma=False,
    )
```

```python
import functools
import math

import jax
import jax.numpy as jnp
from jax import lax
from jax.experimental import pallas as pl
from jax.experimental.pallas import tpu as pltpu
from jax.sharding import PartitionSpec as P


def doc_table(doc_starts, tok_dev):
    n_outer, n_inner, n_slots = doc_starts.shape
    flat_starts = doc_starts.reshape(n_outer * n_inner, n_slots)
    start_counts = jnp.sum((flat_starts < tok_dev).astype(jnp.int32), axis=1)
    first_index = jnp.cumsum(start_counts) - start_counts
    offsets = jnp.arange(tok_dev, dtype=jnp.int32)
    inside_count = jnp.sum(
        (flat_starts[:, None, :] <= offsets[None, :, None]).astype(jnp.int32), axis=2
    )
    return (first_index[:, None] + inside_count - 1).reshape(n_outer, n_inner, tok_dev)


def attention_kernel(
    qmeta_ref, kmeta_ref, q_ref, g_ref, k_ref, v_ref, kt_ref, vt_ref,
    o_ref, dq_ref, dkt_ref, dvt_ref, *, scaling, n_heads, head_dim
):
    @pl.when(pl.program_id(0) == 0)
    def _():
        dkt_ref[...] = jnp.zeros_like(dkt_ref)
        dvt_ref[...] = jnp.zeros_like(dvt_ref)

    k = k_ref[...]
    v = v_ref[...]
    kt = kt_ref[...]
    vt = vt_ref[...]
    contract_first = (((0,), (0,)), ((), ()))
    allowed = (qmeta_ref[:, 0:1] == kmeta_ref[0:1, :]) & (
        kmeta_ref[1:2, :] <= qmeta_ref[:, 1:2]
    )
    for h in range(n_heads):
        cols = slice(h * head_dim, (h + 1) * head_dim)
        q = q_ref[:, cols]
        g = g_ref[:, cols]
        scores = jnp.dot(q, kt, preferred_element_type=jnp.float32) * scaling
        scores = jnp.where(allowed, scores, -jnp.inf)
        row_max = jnp.max(scores, axis=1, keepdims=True)
        shifted = jnp.exp(scores - row_max)
        probs = shifted * (1.0 / jnp.sum(shifted, axis=1, keepdims=True))
        probs_low = probs.astype(jnp.bfloat16)
        attn = jnp.dot(probs_low, v, preferred_element_type=jnp.float32).astype(jnp.bfloat16)
        o_ref[:, cols] = attn
        inner_prod = jnp.sum(
            g.astype(jnp.float32) * attn.astype(jnp.float32), axis=1, keepdims=True
        )
        grad_probs = jnp.dot(g, vt, preferred_element_type=jnp.float32)
        score_grads = (probs * (grad_probs - inner_prod)).astype(jnp.bfloat16)
        dq_ref[:, cols] = (
            jnp.dot(score_grads, k, preferred_element_type=jnp.float32) * scaling
        ).astype(jnp.bfloat16)
        dkt_ref[...] += (
            lax.dot_general(q, score_grads, contract_first, preferred_element_type=jnp.float32)
            * scaling
        )
        dvt_ref[...] += lax.dot_general(
            g, probs_low, contract_first, preferred_element_type=jnp.float32
        )


def attend(rows, query_pos, query_doc, ctx, key_pos, key_doc, n_heads):
    n_rows = rows.shape[0]
    n_keys, kv_width = ctx.shape
    head_dim = kv_width // 2
    width_q = n_heads * head_dim
    block_q = min(256, n_rows)
    grid = (n_rows // block_q,)
    q_spec = pl.BlockSpec((block_q, width_q), lambda i: (i, 0))
    g_spec = pl.BlockSpec((block_q, width_q), lambda i: (i, 1))
    qmeta_spec = pl.BlockSpec((block_q, 2), lambda i: (i, 0))
    kmeta_spec = pl.BlockSpec((2, n_keys), lambda i: (0, 0))
    k_spec = pl.BlockSpec((n_keys, head_dim), lambda i: (0, 0))
    v_spec = pl.BlockSpec((n_keys, head_dim), lambda i: (0, 1))
    kt_spec = pl.BlockSpec((head_dim, n_keys), lambda i: (0, 0))
    vt_spec = pl.BlockSpec((head_dim, n_keys), lambda i: (1, 0))
    out_spec = pl.BlockSpec((block_q, width_q), lambda i: (i, 0))
    key_t_spec = pl.BlockSpec((head_dim, n_keys), lambda i: (0, 0))
    ctx_t = ctx.T
    kernel = functools.partial(
        attention_kernel,
        scaling=1.0 / math.sqrt(head_dim),
        n_heads=n_heads,
        head_dim=head_dim,
    )
    return pl.pallas_call(
        kernel,
        grid=grid,
        in_specs=[qmeta_spec, kmeta_spec, q_spec, g_spec, k_spec, v_spec, kt_spec, vt_spec],
        out_specs=[out_spec, out_spec, key_t_spec, key_t_spec],
        out_shape=[
            jax.ShapeDtypeStruct((n_rows, width_q), jnp.bfloat16),
            jax.ShapeDtypeStruct((n_rows, width_q), jnp.bfloat16),
            jax.ShapeDtypeStruct((head_dim, n_keys), jnp.float32),
            jax.ShapeDtypeStruct((head_dim, n_keys), jnp.float32),
        ],
        compiler_params=pltpu.CompilerParams(dimension_semantics=("arbitrary",)),
    )(
        jnp.stack([query_doc, query_pos], axis=1),
        jnp.stack([key_doc, key_pos]),
        rows,
        rows,
        ctx,
        ctx,
        ctx_t,
        ctx_t,
    )


def shards(queries, keys, values, grad_out, doc_starts):
    n_inner = lax.axis_size("inner")
    n_outer = lax.axis_size("outer")
    n_units = queries.shape[1]
    piece_len = queries.shape[3]
    width_q = queries.shape[4]
    head_dim = keys.shape[4]
    n_heads = width_q // head_dim
    tok_dev = piece_len * n_inner
    outer_id = lax.axis_index("outer")
    inner_id = lax.axis_index("inner")
    docs_all = doc_table(doc_starts, tok_dev)
    offsets = jnp.arange(tok_dev, dtype=jnp.int32)

    rotated = (jnp.arange(n_units, dtype=jnp.int32) + 2 * outer_id) % n_units
    packed = jnp.concatenate(
        [queries[0, rotated, 0], grad_out[0, rotated, 0], keys[0, rotated, 0],
         values[0, rotated, 0]],
        axis=-1,
    )
    unit_local = (inner_id + 2 * outer_id) % n_units
    arrived = lax.all_to_all(packed, "inner", 0, 0, tiled=True).reshape(tok_dev, -1)
    kv_own = arrived[:, 2 * width_q :]

    pairs_up = [(2 * p, 2 * p + 1) for p in range(n_inner // 2)]
    kv_partner = lax.ppermute(kv_own, "inner", pairs_up)

    both = ("outer", "inner")
    last_a, last_b = n_inner - 2, n_inner - 1
    lead = [(-2 * o) % n_inner for o in range(n_outer)]
    send_a = [((o - 1) * n_inner + lead[o] + r, o * n_inner + lead[o] + r)
              for o in range(1, n_outer) for r in range(2)]
    send_b = [((o - 1) * n_inner + lead[o] + r, o * n_inner + lead[o] + 1 - r)
              for o in range(1, n_outer) for r in range(2)]
    recv_a = lax.ppermute(kv_own, both, send_a)
    recv_b = lax.ppermute(kv_own, both, send_b)
    first = unit_local == 0
    kv_prev_a = jnp.where(first, recv_a, recv_b)
    kv_prev_b = jnp.where(first, recv_b, recv_a)

    unit_id = outer_id * n_units + unit_local
    before = jnp.maximum(outer_id - 1, 0)
    has_prev = (outer_id > 0) & (unit_local < 2)
    has_partner = unit_local % 2 == 1
    query_doc = docs_all[outer_id, unit_local]
    query_pos = unit_id * tok_dev + offsets
    partner_doc = jnp.where(has_partner, docs_all[outer_id, jnp.maximum(unit_local - 1, 0)], -3)
    prev_a_doc = jnp.where(has_prev, docs_all[before, last_a], -4)
    prev_b_doc = jnp.where(has_prev, docs_all[before, last_b], -5)
    key_doc = jnp.concatenate([prev_a_doc, prev_b_doc, partner_doc, query_doc])
    key_pos = jnp.concatenate(
        [
            (before * n_units + last_a) * tok_dev + offsets,
            (before * n_units + last_b) * tok_dev + offsets,
            (unit_id - 1) * tok_dev + offsets,
            query_pos,
        ]
    )
    n_slots = 4
    slot_kv = jnp.stack([kv_prev_a, kv_prev_b, kv_partner, kv_own])
    slot_doc = key_doc.reshape(n_slots, tok_dev)
    slot_pos = key_pos.reshape(n_slots, tok_dev)
    needed = (
        (jnp.min(slot_doc, axis=1) <= jnp.max(query_doc))
        & (jnp.max(slot_doc, axis=1) >= jnp.min(query_doc))
        & (jnp.min(slot_pos, axis=1) <= jnp.max(query_pos))
    )
    needed = needed | (jnp.arange(n_slots) == n_slots - 1)
    needed_i = needed.astype(jnp.int32)
    count = jnp.sum(needed_i)
    rank = jnp.where(
        needed, jnp.cumsum(needed_i) - 1, count + jnp.cumsum(1 - needed_i) - 1
    )
    slot_ids = jnp.arange(n_slots, dtype=jnp.int32)
    order = jnp.sum(
        jnp.where(rank[None, :] == slot_ids[:, None], slot_ids[None, :], 0), axis=1
    )
    kv_sorted = slot_kv[order]
    doc_sorted = slot_doc[order]
    pos_sorted = slot_pos[order]

    def branch(n_used):
        def run(kv_sorted, doc_sorted, pos_sorted):
            ctx = kv_sorted[:n_used].reshape(n_used * tok_dev, 2 * head_dim)
            attn, q_grads, k_grads_t, v_grads_t = attend(
                arrived,
                query_pos,
                query_doc,
                ctx,
                pos_sorted[:n_used].reshape(-1),
                doc_sorted[:n_used].reshape(-1),
                n_heads,
            )
            grads = jnp.concatenate([k_grads_t, v_grads_t], axis=0).T.reshape(
                n_used, tok_dev, 2 * head_dim
            )
            grads = jnp.concatenate(
                [grads, jnp.zeros((n_slots - n_used, tok_dev, 2 * head_dim), jnp.float32)]
            )
            return attn, q_grads, grads

        return run

    attn, q_grads, grads_sorted = lax.switch(
        count - 1, [branch(n) for n in range(1, n_slots + 1)], kv_sorted, doc_sorted, pos_sorted
    )
    kv_grads = grads_sorted[rank]

    pairs_down = [(b, a) for a, b in pairs_up]
    from_partner = lax.ppermute(kv_grads[2], "inner", pairs_down)
    back_a = [(b, a) for a, b in send_a]
    back_b = [(b, a) for a, b in send_b]
    grads_a = jnp.where(first, kv_grads[0], kv_grads[1])
    grads_b = jnp.where(first, kv_grads[1], kv_grads[0])
    from_next_a = lax.ppermute(grads_a, both, back_a)
    from_next_b = lax.ppermute(grads_b, both, back_b)
    kv_total = (kv_grads[3] + from_partner + from_next_a + from_next_b).astype(jnp.bfloat16)

    result = jnp.concatenate([attn, q_grads, kv_total], axis=-1).reshape(
        n_inner, piece_len, -1
    )
    restored = (jnp.arange(n_units, dtype=jnp.int32) - 2 * outer_id) % n_units
    returned = lax.all_to_all(result, "inner", 0, 0, tiled=True)[restored]
    shape_q = (1, n_units, 1, piece_len, width_q)
    shape_k = (1, n_units, 1, piece_len, head_dim)
    return (
        returned[..., :width_q].reshape(shape_q),
        returned[..., width_q : 2 * width_q].reshape(shape_q),
        returned[..., 2 * width_q : 2 * width_q + head_dim].reshape(shape_k),
        returned[..., 2 * width_q + head_dim :].reshape(shape_k),
    )


def solution(mesh):
    return jax.shard_map(
        shards,
        mesh=mesh,
        in_specs=(
            P("outer", None, "inner", None, None),
            P("outer", None, "inner", None, None),
            P("outer", None, "inner", None, None),
            P("outer", None, "inner", None, None),
            P(),
        ),
        out_specs=(
            P("outer", None, "inner", None, None),
            P("outer", None, "inner", None, None),
            P("outer", None, "inner", None, None),
            P("outer", None, "inner", None, None),
        ),
        check_vma=False,
    )
```

```python
import functools
import math

import jax
import jax.numpy as jnp
from jax import lax
from jax.experimental import pallas as pl
from jax.experimental.pallas import tpu as pltpu
from jax.sharding import PartitionSpec as P


def doc_table(doc_starts, tok_dev):
    n_outer, n_inner, n_slots = doc_starts.shape
    flat_starts = doc_starts.reshape(n_outer * n_inner, n_slots)
    start_counts = jnp.sum((flat_starts < tok_dev).astype(jnp.int32), axis=1)
    first_index = jnp.cumsum(start_counts) - start_counts
    offsets = jnp.arange(tok_dev, dtype=jnp.int32)
    inside_count = jnp.sum(
        (flat_starts[:, None, :] <= offsets[None, :, None]).astype(jnp.int32), axis=2
    )
    return (first_index[:, None] + inside_count - 1).reshape(n_outer, n_inner, tok_dev)


def attention_kernel(
    qmeta_ref, kmeta_ref, q_ref, g_ref, k_ref, v_ref,
    o_ref, dq_ref, dkt_ref, dvt_ref, *, scaling, n_heads, head_dim
):
    @pl.when(pl.program_id(0) == 0)
    def _():
        dkt_ref[...] = jnp.zeros_like(dkt_ref)
        dvt_ref[...] = jnp.zeros_like(dvt_ref)

    k = k_ref[...]
    v = v_ref[...]
    kt = k.T
    vt = v.T
    contract_first = (((0,), (0,)), ((), ()))
    allowed = (qmeta_ref[:, 0:1] == kmeta_ref[0:1, :]) & (
        kmeta_ref[1:2, :] <= qmeta_ref[:, 1:2]
    )
    for h in range(n_heads):
        cols = slice(h * head_dim, (h + 1) * head_dim)
        q = q_ref[:, cols]
        g = g_ref[:, cols]
        scores = jnp.dot(q, kt, preferred_element_type=jnp.float32) * scaling
        scores = jnp.where(allowed, scores, -jnp.inf)
        row_max = jnp.max(scores, axis=1, keepdims=True)
        log_total = row_max + jnp.log(
            jnp.sum(jnp.exp(scores - row_max), axis=1, keepdims=True)
        )
        probs = jnp.exp(scores - log_total)
        probs_low = probs.astype(jnp.bfloat16)
        attn = jnp.dot(probs_low, v, preferred_element_type=jnp.float32).astype(jnp.bfloat16)
        o_ref[:, cols] = attn
        inner_prod = jnp.sum(
            g.astype(jnp.float32) * attn.astype(jnp.float32), axis=1, keepdims=True
        )
        grad_probs = jnp.dot(g, vt, preferred_element_type=jnp.float32)
        score_grads = (probs * (grad_probs - inner_prod)).astype(jnp.bfloat16)
        dq_ref[:, cols] = (
            jnp.dot(score_grads, k, preferred_element_type=jnp.float32) * scaling
        ).astype(jnp.bfloat16)
        dkt_ref[...] += (
            lax.dot_general(q, score_grads, contract_first, preferred_element_type=jnp.float32)
            * scaling
        )
        dvt_ref[...] += lax.dot_general(
            g, probs_low, contract_first, preferred_element_type=jnp.float32
        )


def attend(rows, qmeta, ctx_all, kmeta_all, n_keys, n_heads):
    n_rows = rows.shape[0]
    head_dim = ctx_all.shape[1] // 2
    width_q = n_heads * head_dim
    block_q = min(256, n_rows)
    grid = (n_rows // block_q,)
    q_spec = pl.BlockSpec((block_q, width_q), lambda i: (i, 0))
    g_spec = pl.BlockSpec((block_q, width_q), lambda i: (i, 1))
    qmeta_spec = pl.BlockSpec((block_q, 2), lambda i: (i, 0))
    kmeta_spec = pl.BlockSpec((2, n_keys), lambda i: (0, 0))
    k_spec = pl.BlockSpec((n_keys, head_dim), lambda i: (0, 0))
    v_spec = pl.BlockSpec((n_keys, head_dim), lambda i: (0, 1))
    out_spec = pl.BlockSpec((block_q, width_q), lambda i: (i, 0))
    key_t_spec = pl.BlockSpec((head_dim, n_keys), lambda i: (0, 0))
    kernel = functools.partial(
        attention_kernel,
        scaling=1.0 / math.sqrt(head_dim),
        n_heads=n_heads,
        head_dim=head_dim,
    )
    return pl.pallas_call(
        kernel,
        grid=grid,
        in_specs=[qmeta_spec, kmeta_spec, q_spec, g_spec, k_spec, v_spec],
        out_specs=[out_spec, out_spec, key_t_spec, key_t_spec],
        out_shape=[
            jax.ShapeDtypeStruct((n_rows, width_q), jnp.bfloat16),
            jax.ShapeDtypeStruct((n_rows, width_q), jnp.bfloat16),
            jax.ShapeDtypeStruct((head_dim, n_keys), jnp.float32),
            jax.ShapeDtypeStruct((head_dim, n_keys), jnp.float32),
        ],
        compiler_params=pltpu.CompilerParams(dimension_semantics=("arbitrary",)),
    )(qmeta, kmeta_all, rows, rows, ctx_all, ctx_all)


def shards(queries, keys, values, grad_out, doc_starts):
    n_inner = lax.axis_size("inner")
    n_outer = lax.axis_size("outer")
    n_units = queries.shape[1]
    piece_len = queries.shape[3]
    width_q = queries.shape[4]
    head_dim = keys.shape[4]
    n_heads = width_q // head_dim
    tok_dev = piece_len * n_inner
    outer_id = lax.axis_index("outer")
    inner_id = lax.axis_index("inner")
    docs_all = doc_table(doc_starts, tok_dev)
    offsets = jnp.arange(tok_dev, dtype=jnp.int32)

    packed = jnp.concatenate(
        [queries[0, :, 0], grad_out[0, :, 0], keys[0, :, 0], values[0, :, 0]], axis=-1
    )
    unit_local = (inner_id + 2 * outer_id) % n_units
    packed = jnp.roll(packed, -2 * outer_id, axis=0)
    arrived = lax.all_to_all(packed, "inner", 0, 0, tiled=True).reshape(tok_dev, -1)
    kv_own = arrived[:, 2 * width_q :]

    pairs_up = [(2 * p, 2 * p + 1) for p in range(n_inner // 2)]
    kv_partner = lax.ppermute(kv_own, "inner", pairs_up)

    both = ("outer", "inner")
    last_a, last_b = n_inner - 2, n_inner - 1
    lead = [(-2 * o) % n_inner for o in range(n_outer)]
    send_a = [((o - 1) * n_inner + lead[o] + r, o * n_inner + lead[o] + r)
              for o in range(1, n_outer) for r in range(2)]
    send_b = [((o - 1) * n_inner + lead[o] + r, o * n_inner + lead[o] + 1 - r)
              for o in range(1, n_outer) for r in range(2)]
    recv_a = lax.ppermute(kv_own, both, send_a)
    recv_b = lax.ppermute(kv_own, both, send_b)
    first = unit_local == 0
    kv_prev_a = jnp.where(first, recv_a, recv_b)
    kv_prev_b = jnp.where(first, recv_b, recv_a)

    unit_id = outer_id * n_units + unit_local
    before = jnp.maximum(outer_id - 1, 0)
    has_prev = (outer_id > 0) & (unit_local < 2)
    has_partner = unit_local % 2 == 1
    query_doc = docs_all[outer_id, unit_local]
    query_pos = unit_id * tok_dev + offsets
    partner_doc = jnp.where(has_partner, docs_all[outer_id, jnp.maximum(unit_local - 1, 0)], -3)
    prev_a_doc = jnp.where(has_prev, docs_all[before, last_a], -4)
    prev_b_doc = jnp.where(has_prev, docs_all[before, last_b], -5)
    key_doc = jnp.concatenate([prev_a_doc, prev_b_doc, partner_doc, query_doc])
    key_pos = jnp.concatenate(
        [
            (before * n_units + last_a) * tok_dev + offsets,
            (before * n_units + last_b) * tok_dev + offsets,
            (unit_id - 1) * tok_dev + offsets,
            query_pos,
        ]
    )
    n_slots = 4
    slot_kv = jnp.stack([kv_prev_a, kv_prev_b, kv_partner, kv_own])
    slot_doc = key_doc.reshape(n_slots, tok_dev)
    slot_pos = key_pos.reshape(n_slots, tok_dev)
    needed = (
        (jnp.min(slot_doc, axis=1) <= jnp.max(query_doc))
        & (jnp.max(slot_doc, axis=1) >= jnp.min(query_doc))
        & (jnp.min(slot_pos, axis=1) <= jnp.max(query_pos))
    )
    needed = needed | (jnp.arange(n_slots) == n_slots - 1)
    needed_i = needed.astype(jnp.int32)
    count = jnp.sum(needed_i)
    rank = jnp.where(
        needed, jnp.cumsum(needed_i) - 1, count + jnp.cumsum(1 - needed_i) - 1
    )
    slot_ids = jnp.arange(n_slots, dtype=jnp.int32)
    order = jnp.sum(
        jnp.where(rank[None, :] == slot_ids[:, None], slot_ids[None, :], 0), axis=1
    )
    kv_sorted = slot_kv[order].reshape(n_slots * tok_dev, 2 * head_dim)
    kmeta_sorted = jnp.stack([slot_doc[order].reshape(-1), slot_pos[order].reshape(-1)])
    qmeta = jnp.stack([query_doc, query_pos], axis=1)

    def branch(n_used):
        def run(kv_sorted, kmeta_sorted, qmeta):
            attn, q_grads, k_grads_t, v_grads_t = attend(
                arrived, qmeta, kv_sorted, kmeta_sorted, n_used * tok_dev, n_heads
            )
            grads = jnp.concatenate([k_grads_t, v_grads_t], axis=0).T.reshape(
                n_used, tok_dev, 2 * head_dim
            )
            grads = jnp.concatenate(
                [grads, jnp.zeros((n_slots - n_used, tok_dev, 2 * head_dim), jnp.float32)]
            )
            return attn, q_grads, grads

        return run

    attn, q_grads, grads_sorted = lax.switch(
        count - 1, [branch(n) for n in range(1, n_slots + 1)], kv_sorted, kmeta_sorted, qmeta
    )
    kv_grads = grads_sorted[rank]

    pairs_down = [(b, a) for a, b in pairs_up]
    from_partner = lax.ppermute(kv_grads[2], "inner", pairs_down)
    back_a = [(b, a) for a, b in send_a]
    back_b = [(b, a) for a, b in send_b]
    grads_a = jnp.where(first, kv_grads[0], kv_grads[1])
    grads_b = jnp.where(first, kv_grads[1], kv_grads[0])
    from_next_a = lax.ppermute(grads_a, both, back_a)
    from_next_b = lax.ppermute(grads_b, both, back_b)
    kv_total = (kv_grads[3] + from_partner + from_next_a + from_next_b).astype(jnp.bfloat16)

    result = jnp.concatenate([attn, q_grads, kv_total], axis=-1).reshape(
        n_inner, piece_len, -1
    )
    returned = jnp.roll(
        lax.all_to_all(result, "inner", 0, 0, tiled=True), 2 * outer_id, axis=0
    )
    shape_q = (1, n_units, 1, piece_len, width_q)
    shape_k = (1, n_units, 1, piece_len, head_dim)
    return (
        returned[..., :width_q].reshape(shape_q),
        returned[..., width_q : 2 * width_q].reshape(shape_q),
        returned[..., 2 * width_q : 2 * width_q + head_dim].reshape(shape_k),
        returned[..., 2 * width_q + head_dim :].reshape(shape_k),
    )


def solution(mesh):
    return jax.shard_map(
        shards,
        mesh=mesh,
        in_specs=(
            P("outer", None, "inner", None, None),
            P("outer", None, "inner", None, None),
            P("outer", None, "inner", None, None),
            P("outer", None, "inner", None, None),
            P(),
        ),
        out_specs=(
            P("outer", None, "inner", None, None),
            P("outer", None, "inner", None, None),
            P("outer", None, "inner", None, None),
            P("outer", None, "inner", None, None),
        ),
        check_vma=False,
    )
```

```python
import functools
import math

import jax
import jax.numpy as jnp
from jax import lax
from jax.experimental import pallas as pl
from jax.experimental.pallas import tpu as pltpu
from jax.sharding import PartitionSpec as P


def doc_table(doc_starts, tok_dev):
    n_outer, n_inner, n_slots = doc_starts.shape
    flat_starts = doc_starts.reshape(n_outer * n_inner, n_slots)
    start_counts = jnp.sum((flat_starts < tok_dev).astype(jnp.int32), axis=1)
    first_index = jnp.cumsum(start_counts) - start_counts
    offsets = jnp.arange(tok_dev, dtype=jnp.int32)
    inside_count = jnp.sum(
        (flat_starts[:, None, :] <= offsets[None, :, None]).astype(jnp.int32), axis=2
    )
    return (first_index[:, None] + inside_count - 1).reshape(n_outer, n_inner, tok_dev)


def attention_kernel(
    qmeta_ref, kmeta_ref, q_ref, g_ref, k_ref, v_ref,
    o_ref, dq_ref, dkt_ref, dvt_ref, *, scaling, n_heads, head_dim
):
    @pl.when(pl.program_id(0) == 0)
    def _():
        dkt_ref[...] = jnp.zeros_like(dkt_ref)
        dvt_ref[...] = jnp.zeros_like(dvt_ref)

    k = k_ref[...]
    v = v_ref[...]
    kt = k.T
    vt = v.T
    contract_first = (((0,), (0,)), ((), ()))
    allowed = (qmeta_ref[:, 0:1] == kmeta_ref[0:1, :]) & (
        kmeta_ref[1:2, :] <= qmeta_ref[:, 1:2]
    )
    for h in range(n_heads):
        cols = slice(h * head_dim, (h + 1) * head_dim)
        q = q_ref[:, cols]
        g = g_ref[:, cols]
        scores = jnp.dot(q, kt, preferred_element_type=jnp.float32) * scaling
        scores = jnp.where(allowed, scores, -jnp.inf)
        row_max = jnp.max(scores, axis=1, keepdims=True)
        log_total = row_max + jnp.log(
            jnp.sum(jnp.exp(scores - row_max), axis=1, keepdims=True)
        )
        probs = jnp.exp(scores - log_total)
        probs_low = probs.astype(jnp.bfloat16)
        attn = jnp.dot(probs_low, v, preferred_element_type=jnp.float32).astype(jnp.bfloat16)
        o_ref[:, cols] = attn
        inner_prod = jnp.sum(
            g.astype(jnp.float32) * attn.astype(jnp.float32), axis=1, keepdims=True
        )
        grad_probs = jnp.dot(g, vt, preferred_element_type=jnp.float32)
        score_grads = (probs * (grad_probs - inner_prod)).astype(jnp.bfloat16)
        dq_ref[:, cols] = (
            jnp.dot(score_grads, k, preferred_element_type=jnp.float32) * scaling
        ).astype(jnp.bfloat16)
        dkt_ref[...] += (
            lax.dot_general(q, score_grads, contract_first, preferred_element_type=jnp.float32)
            * scaling
        )
        dvt_ref[...] += lax.dot_general(
            g, probs_low, contract_first, preferred_element_type=jnp.float32
        )


def attend(rows, qmeta, ctx_all, kmeta_all, n_keys, n_heads):
    n_rows = rows.shape[0]
    head_dim = ctx_all.shape[1] // 2
    width_q = n_heads * head_dim
    block_q = min(256, n_rows)
    grid = (n_rows // block_q,)
    q_spec = pl.BlockSpec((block_q, width_q), lambda i: (i, 0))
    g_spec = pl.BlockSpec((block_q, width_q), lambda i: (i, 1))
    qmeta_spec = pl.BlockSpec((block_q, 2), lambda i: (i, 0))
    kmeta_spec = pl.BlockSpec((2, n_keys), lambda i: (0, 0))
    k_spec = pl.BlockSpec((n_keys, head_dim), lambda i: (0, 0))
    v_spec = pl.BlockSpec((n_keys, head_dim), lambda i: (0, 1))
    out_spec = pl.BlockSpec((block_q, width_q), lambda i: (i, 0))
    key_t_spec = pl.BlockSpec((head_dim, n_keys), lambda i: (0, 0))
    kernel = functools.partial(
        attention_kernel,
        scaling=1.0 / math.sqrt(head_dim),
        n_heads=n_heads,
        head_dim=head_dim,
    )
    return pl.pallas_call(
        kernel,
        grid=grid,
        in_specs=[qmeta_spec, kmeta_spec, q_spec, g_spec, k_spec, v_spec],
        out_specs=[out_spec, out_spec, key_t_spec, key_t_spec],
        out_shape=[
            jax.ShapeDtypeStruct((n_rows, width_q), jnp.bfloat16),
            jax.ShapeDtypeStruct((n_rows, width_q), jnp.bfloat16),
            jax.ShapeDtypeStruct((head_dim, n_keys), jnp.float32),
            jax.ShapeDtypeStruct((head_dim, n_keys), jnp.float32),
        ],
        compiler_params=pltpu.CompilerParams(dimension_semantics=("arbitrary",)),
    )(qmeta, kmeta_all, rows, rows, ctx_all, ctx_all)


def shards(queries, keys, values, grad_out, doc_starts):
    n_inner = lax.axis_size("inner")
    n_outer = lax.axis_size("outer")
    n_units = queries.shape[1]
    piece_len = queries.shape[3]
    width_q = queries.shape[4]
    head_dim = keys.shape[4]
    n_heads = width_q // head_dim
    tok_dev = piece_len * n_inner
    outer_id = lax.axis_index("outer")
    inner_id = lax.axis_index("inner")
    docs_all = doc_table(doc_starts, tok_dev)
    offsets = jnp.arange(tok_dev, dtype=jnp.int32)

    packed = jnp.concatenate(
        [queries[0, :, 0], grad_out[0, :, 0], keys[0, :, 0], values[0, :, 0]], axis=-1
    )
    unit_local = (inner_id + 2 * outer_id) % n_units
    packed = jnp.roll(packed, -2 * outer_id, axis=0)
    arrived = lax.all_to_all(packed, "inner", 0, 0, tiled=True).reshape(tok_dev, -1)
    kv_own = arrived[:, 2 * width_q :]

    pairs_up = [(2 * p, 2 * p + 1) for p in range(n_inner // 2)]
    kv_partner = lax.ppermute(kv_own, "inner", pairs_up)

    both = ("outer", "inner")
    last_a, last_b = n_inner - 2, n_inner - 1
    lead = [(-2 * o) % n_inner for o in range(n_outer)]
    send_a = [((o - 1) * n_inner + lead[o] + r, o * n_inner + lead[o] + r)
              for o in range(1, n_outer) for r in range(2)]
    send_b = [((o - 1) * n_inner + lead[o] + r, o * n_inner + lead[o] + 1 - r)
              for o in range(1, n_outer) for r in range(2)]
    recv_a = lax.ppermute(kv_own, both, send_a)
    recv_b = lax.ppermute(kv_own, both, send_b)
    first = unit_local == 0
    kv_prev_a = jnp.where(first, recv_a, recv_b)
    kv_prev_b = jnp.where(first, recv_b, recv_a)

    unit_id = outer_id * n_units + unit_local
    before = jnp.maximum(outer_id - 1, 0)
    has_prev = (outer_id > 0) & (unit_local < 2)
    has_partner = unit_local % 2 == 1
    query_doc = docs_all[outer_id, unit_local]
    query_pos = unit_id * tok_dev + offsets
    partner_doc = jnp.where(has_partner, docs_all[outer_id, jnp.maximum(unit_local - 1, 0)], -3)
    prev_a_doc = jnp.where(has_prev, docs_all[before, last_a], -4)
    prev_b_doc = jnp.where(has_prev, docs_all[before, last_b], -5)
    key_doc = jnp.concatenate([prev_a_doc, prev_b_doc, partner_doc, query_doc])
    key_pos = jnp.concatenate(
        [
            (before * n_units + last_a) * tok_dev + offsets,
            (before * n_units + last_b) * tok_dev + offsets,
            (unit_id - 1) * tok_dev + offsets,
            query_pos,
        ]
    )
    n_slots = 4
    slot_kv = jnp.stack([kv_prev_a, kv_prev_b, kv_partner, kv_own])
    slot_doc = key_doc.reshape(n_slots, tok_dev)
    slot_pos = key_pos.reshape(n_slots, tok_dev)
    needed = (
        (jnp.min(slot_doc, axis=1) <= jnp.max(query_doc))
        & (jnp.max(slot_doc, axis=1) >= jnp.min(query_doc))
        & (jnp.min(slot_pos, axis=1) <= jnp.max(query_pos))
    )
    needed = needed | (jnp.arange(n_slots) == n_slots - 1)
    needed_i = needed.astype(jnp.int32)
    count = jnp.sum(needed_i)
    rank = jnp.where(
        needed, jnp.cumsum(needed_i) - 1, count + jnp.cumsum(1 - needed_i) - 1
    )
    slot_ids = jnp.arange(n_slots, dtype=jnp.int32)
    order = jnp.sum(
        jnp.where(rank[None, :] == slot_ids[:, None], slot_ids[None, :], 0), axis=1
    )
    kv_sorted = slot_kv[order].reshape(n_slots * tok_dev, 2 * head_dim)
    kmeta_sorted = jnp.stack([slot_doc[order].reshape(-1), slot_pos[order].reshape(-1)])
    qmeta = jnp.stack([query_doc, query_pos], axis=1)

    def branch(n_used):
        def run(kv_sorted, kmeta_sorted, qmeta):
            attn, q_grads, k_grads_t, v_grads_t = attend(
                arrived, qmeta, kv_sorted, kmeta_sorted, n_used * tok_dev, n_heads
            )
            grads = jnp.concatenate([k_grads_t, v_grads_t], axis=0).T.reshape(
                n_used, tok_dev, 2 * head_dim
            )
            grads = jnp.concatenate(
                [grads, jnp.zeros((n_slots - n_used, tok_dev, 2 * head_dim), jnp.float32)]
            )
            return attn, q_grads, grads

        return run

    attn, q_grads, grads_sorted = lax.switch(
        count - 1, [branch(n) for n in range(1, n_slots + 1)], kv_sorted, kmeta_sorted, qmeta
    )
    kv_grads = grads_sorted[rank]

    pairs_down = [(b, a) for a, b in pairs_up]
    low = jnp.bfloat16
    from_partner = lax.ppermute(kv_grads[2].astype(low), "inner", pairs_down)
    back_a = [(b, a) for a, b in send_a]
    back_b = [(b, a) for a, b in send_b]
    grads_a = jnp.where(first, kv_grads[0], kv_grads[1])
    grads_b = jnp.where(first, kv_grads[1], kv_grads[0])
    from_next_a = lax.ppermute(grads_a.astype(low), both, back_a)
    from_next_b = lax.ppermute(grads_b.astype(low), both, back_b)
    kv_total = (
        kv_grads[3]
        + from_partner.astype(jnp.float32)
        + from_next_a.astype(jnp.float32)
        + from_next_b.astype(jnp.float32)
    ).astype(jnp.bfloat16)

    result = jnp.concatenate([attn, q_grads, kv_total], axis=-1).reshape(
        n_inner, piece_len, -1
    )
    returned = jnp.roll(
        lax.all_to_all(result, "inner", 0, 0, tiled=True), 2 * outer_id, axis=0
    )
    shape_q = (1, n_units, 1, piece_len, width_q)
    shape_k = (1, n_units, 1, piece_len, head_dim)
    return (
        returned[..., :width_q].reshape(shape_q),
        returned[..., width_q : 2 * width_q].reshape(shape_q),
        returned[..., 2 * width_q : 2 * width_q + head_dim].reshape(shape_k),
        returned[..., 2 * width_q + head_dim :].reshape(shape_k),
    )


def solution(mesh):
    return jax.shard_map(
        shards,
        mesh=mesh,
        in_specs=(
            P("outer", None, "inner", None, None),
            P("outer", None, "inner", None, None),
            P("outer", None, "inner", None, None),
            P("outer", None, "inner", None, None),
            P(),
        ),
        out_specs=(
            P("outer", None, "inner", None, None),
            P("outer", None, "inner", None, None),
            P("outer", None, "inner", None, None),
            P("outer", None, "inner", None, None),
        ),
        check_vma=False,
    )
```

```python
import functools
import math

import jax
import jax.numpy as jnp
from jax import lax
from jax.experimental import pallas as pl
from jax.experimental.pallas import tpu as pltpu
from jax.sharding import PartitionSpec as P


def doc_table(doc_starts, tok_dev):
    n_outer, n_inner, n_slots = doc_starts.shape
    flat_starts = doc_starts.reshape(n_outer * n_inner, n_slots)
    start_counts = jnp.sum((flat_starts < tok_dev).astype(jnp.int32), axis=1)
    first_index = jnp.cumsum(start_counts) - start_counts
    offsets = jnp.arange(tok_dev, dtype=jnp.int32)
    inside_count = jnp.sum(
        (flat_starts[:, None, :] <= offsets[None, :, None]).astype(jnp.int32), axis=2
    )
    return (first_index[:, None] + inside_count - 1).reshape(n_outer, n_inner, tok_dev)


def attention_kernel(
    order_ref, qmeta_ref, kmeta_ref, q_ref, g_ref, k_ref, v_ref,
    o_ref, dq_ref, dkv_ref, dkt_ref, dvt_ref, *, scaling, n_heads, head_dim, slot_len
):
    step = pl.program_id(0)

    @pl.when(step == 0)
    def _():
        dkt_ref[...] = jnp.zeros_like(dkt_ref)
        dvt_ref[...] = jnp.zeros_like(dvt_ref)
        dkv_ref[...] = jnp.zeros_like(dkv_ref)

    k = k_ref[...]
    v = v_ref[...]
    kt = k.T
    vt = v.T
    contract_first = (((0,), (0,)), ((), ()))
    allowed = (qmeta_ref[:, 0:1] == kmeta_ref[0:1, :]) & (
        kmeta_ref[1:2, :] <= qmeta_ref[:, 1:2]
    )
    for h in range(n_heads):
        cols = slice(h * head_dim, (h + 1) * head_dim)
        q = q_ref[:, cols]
        g = g_ref[:, cols]
        scores = jnp.dot(q, kt, preferred_element_type=jnp.float32) * scaling
        scores = jnp.where(allowed, scores, -jnp.inf)
        row_max = jnp.max(scores, axis=1, keepdims=True)
        log_total = row_max + jnp.log(
            jnp.sum(jnp.exp(scores - row_max), axis=1, keepdims=True)
        )
        probs = jnp.exp(scores - log_total)
        probs_low = probs.astype(jnp.bfloat16)
        attn = jnp.dot(probs_low, v, preferred_element_type=jnp.float32).astype(jnp.bfloat16)
        o_ref[:, cols] = attn
        inner_prod = jnp.sum(
            g.astype(jnp.float32) * attn.astype(jnp.float32), axis=1, keepdims=True
        )
        grad_probs = jnp.dot(g, vt, preferred_element_type=jnp.float32)
        score_grads = (probs * (grad_probs - inner_prod)).astype(jnp.bfloat16)
        dq_ref[:, cols] = (
            jnp.dot(score_grads, k, preferred_element_type=jnp.float32) * scaling
        ).astype(jnp.bfloat16)
        dkt_ref[...] += (
            lax.dot_general(q, score_grads, contract_first, preferred_element_type=jnp.float32)
            * scaling
        )
        dvt_ref[...] += lax.dot_general(
            g, probs_low, contract_first, preferred_element_type=jnp.float32
        )

    @pl.when(step == pl.num_programs(0) - 1)
    def _():
        for r in range(dkt_ref.shape[1] // slot_len):
            cols = slice(r * slot_len, (r + 1) * slot_len)
            slot = order_ref[r]
            dkv_ref[slot, :, 0:head_dim] = dkt_ref[:, cols].T
            dkv_ref[slot, :, head_dim : 2 * head_dim] = dvt_ref[:, cols].T


def attend(rows, qmeta, ctx_all, kmeta_all, order, n_keys, n_heads):
    n_rows = rows.shape[0]
    n_slots = order.shape[0]
    slot_len = ctx_all.shape[0] // n_slots
    head_dim = ctx_all.shape[1] // 2
    width_q = n_heads * head_dim
    block_q = min(256, n_rows)
    grid = (n_rows // block_q,)
    q_spec = pl.BlockSpec((block_q, width_q), lambda i, o: (i, 0))
    g_spec = pl.BlockSpec((block_q, width_q), lambda i, o: (i, 1))
    qmeta_spec = pl.BlockSpec((block_q, 2), lambda i, o: (i, 0))
    kmeta_spec = pl.BlockSpec((2, n_keys), lambda i, o: (0, 0))
    k_spec = pl.BlockSpec((n_keys, head_dim), lambda i, o: (0, 0))
    v_spec = pl.BlockSpec((n_keys, head_dim), lambda i, o: (0, 1))
    out_spec = pl.BlockSpec((block_q, width_q), lambda i, o: (i, 0))
    grads_spec = pl.BlockSpec((n_slots, slot_len, 2 * head_dim), lambda i, o: (0, 0, 0))
    kernel = functools.partial(
        attention_kernel,
        scaling=1.0 / math.sqrt(head_dim),
        n_heads=n_heads,
        head_dim=head_dim,
        slot_len=slot_len,
    )
    return pl.pallas_call(
        kernel,
        grid_spec=pltpu.PrefetchScalarGridSpec(
            num_scalar_prefetch=1,
            grid=grid,
            in_specs=[qmeta_spec, kmeta_spec, q_spec, g_spec, k_spec, v_spec],
            out_specs=[out_spec, out_spec, grads_spec],
            scratch_shapes=[
                pltpu.VMEM((head_dim, n_keys), jnp.float32),
                pltpu.VMEM((head_dim, n_keys), jnp.float32),
            ],
        ),
        out_shape=[
            jax.ShapeDtypeStruct((n_rows, width_q), jnp.bfloat16),
            jax.ShapeDtypeStruct((n_rows, width_q), jnp.bfloat16),
            jax.ShapeDtypeStruct((n_slots, slot_len, 2 * head_dim), jnp.float32),
        ],
        compiler_params=pltpu.CompilerParams(dimension_semantics=("arbitrary",)),
    )(order, qmeta, kmeta_all, rows, rows, ctx_all, ctx_all)


def shards(queries, keys, values, grad_out, doc_starts):
    n_inner = lax.axis_size("inner")
    n_outer = lax.axis_size("outer")
    n_units = queries.shape[1]
    piece_len = queries.shape[3]
    width_q = queries.shape[4]
    head_dim = keys.shape[4]
    n_heads = width_q // head_dim
    tok_dev = piece_len * n_inner
    outer_id = lax.axis_index("outer")
    inner_id = lax.axis_index("inner")
    docs_all = doc_table(doc_starts, tok_dev)
    offsets = jnp.arange(tok_dev, dtype=jnp.int32)

    packed = jnp.concatenate(
        [queries[0, :, 0], grad_out[0, :, 0], keys[0, :, 0], values[0, :, 0]], axis=-1
    )
    unit_local = (inner_id + 2 * outer_id) % n_units
    packed = jnp.roll(packed, -2 * outer_id, axis=0)
    arrived = lax.all_to_all(packed, "inner", 0, 0, tiled=True).reshape(tok_dev, -1)
    kv_own = arrived[:, 2 * width_q :]

    pairs_up = [(2 * p, 2 * p + 1) for p in range(n_inner // 2)]
    kv_partner = lax.ppermute(kv_own, "inner", pairs_up)

    both = ("outer", "inner")
    last_a, last_b = n_inner - 2, n_inner - 1
    lead = [(-2 * o) % n_inner for o in range(n_outer)]
    send_a = [((o - 1) * n_inner + lead[o] + r, o * n_inner + lead[o] + r)
              for o in range(1, n_outer) for r in range(2)]
    send_b = [((o - 1) * n_inner + lead[o] + r, o * n_inner + lead[o] + 1 - r)
              for o in range(1, n_outer) for r in range(2)]
    recv_a = lax.ppermute(kv_own, both, send_a)
    recv_b = lax.ppermute(kv_own, both, send_b)
    first = unit_local == 0
    kv_prev_a = jnp.where(first, recv_a, recv_b)
    kv_prev_b = jnp.where(first, recv_b, recv_a)

    unit_id = outer_id * n_units + unit_local
    before = jnp.maximum(outer_id - 1, 0)
    has_prev = (outer_id > 0) & (unit_local < 2)
    has_partner = unit_local % 2 == 1
    query_doc = docs_all[outer_id, unit_local]
    query_pos = unit_id * tok_dev + offsets
    partner_doc = jnp.where(has_partner, docs_all[outer_id, jnp.maximum(unit_local - 1, 0)], -3)
    prev_a_doc = jnp.where(has_prev, docs_all[before, last_a], -4)
    prev_b_doc = jnp.where(has_prev, docs_all[before, last_b], -5)
    key_doc = jnp.concatenate([prev_a_doc, prev_b_doc, partner_doc, query_doc])
    key_pos = jnp.concatenate(
        [
            (before * n_units + last_a) * tok_dev + offsets,
            (before * n_units + last_b) * tok_dev + offsets,
            (unit_id - 1) * tok_dev + offsets,
            query_pos,
        ]
    )
    n_slots = 4
    slot_kv = jnp.stack([kv_prev_a, kv_prev_b, kv_partner, kv_own])
    slot_doc = key_doc.reshape(n_slots, tok_dev)
    slot_pos = key_pos.reshape(n_slots, tok_dev)
    needed = (
        (jnp.min(slot_doc, axis=1) <= jnp.max(query_doc))
        & (jnp.max(slot_doc, axis=1) >= jnp.min(query_doc))
        & (jnp.min(slot_pos, axis=1) <= jnp.max(query_pos))
    )
    needed = needed | (jnp.arange(n_slots) == n_slots - 1)
    needed_i = needed.astype(jnp.int32)
    count = jnp.sum(needed_i)
    rank = jnp.where(
        needed, jnp.cumsum(needed_i) - 1, count + jnp.cumsum(1 - needed_i) - 1
    )
    slot_ids = jnp.arange(n_slots, dtype=jnp.int32)
    order = jnp.sum(
        jnp.where(rank[None, :] == slot_ids[:, None], slot_ids[None, :], 0), axis=1
    )
    kv_sorted = slot_kv[order].reshape(n_slots * tok_dev, 2 * head_dim)
    kmeta_sorted = jnp.stack([slot_doc[order].reshape(-1), slot_pos[order].reshape(-1)])
    qmeta = jnp.stack([query_doc, query_pos], axis=1)

    def branch(n_used):
        def run(kv_sorted, kmeta_sorted, qmeta, order):
            return attend(
                arrived, qmeta, kv_sorted, kmeta_sorted, order, n_used * tok_dev, n_heads
            )

        return run

    attn, q_grads, kv_grads = lax.switch(
        count - 1,
        [branch(n) for n in range(1, n_slots + 1)],
        kv_sorted,
        kmeta_sorted,
        qmeta,
        order,
    )

    pairs_down = [(b, a) for a, b in pairs_up]
    low = jnp.bfloat16
    from_partner = lax.ppermute(kv_grads[2].astype(low), "inner", pairs_down)
    back_a = [(b, a) for a, b in send_a]
    back_b = [(b, a) for a, b in send_b]
    grads_a = jnp.where(first, kv_grads[0], kv_grads[1])
    grads_b = jnp.where(first, kv_grads[1], kv_grads[0])
    from_next_a = lax.ppermute(grads_a.astype(low), both, back_a)
    from_next_b = lax.ppermute(grads_b.astype(low), both, back_b)
    kv_total = (
        kv_grads[3]
        + from_partner.astype(jnp.float32)
        + from_next_a.astype(jnp.float32)
        + from_next_b.astype(jnp.float32)
    ).astype(jnp.bfloat16)

    result = jnp.concatenate([attn, q_grads, kv_total], axis=-1).reshape(
        n_inner, piece_len, -1
    )
    returned = jnp.roll(
        lax.all_to_all(result, "inner", 0, 0, tiled=True), 2 * outer_id, axis=0
    )
    shape_q = (1, n_units, 1, piece_len, width_q)
    shape_k = (1, n_units, 1, piece_len, head_dim)
    return (
        returned[..., :width_q].reshape(shape_q),
        returned[..., width_q : 2 * width_q].reshape(shape_q),
        returned[..., 2 * width_q : 2 * width_q + head_dim].reshape(shape_k),
        returned[..., 2 * width_q + head_dim :].reshape(shape_k),
    )


def solution(mesh):
    return jax.shard_map(
        shards,
        mesh=mesh,
        in_specs=(
            P("outer", None, "inner", None, None),
            P("outer", None, "inner", None, None),
            P("outer", None, "inner", None, None),
            P("outer", None, "inner", None, None),
            P(),
        ),
        out_specs=(
            P("outer", None, "inner", None, None),
            P("outer", None, "inner", None, None),
            P("outer", None, "inner", None, None),
            P("outer", None, "inner", None, None),
        ),
        check_vma=False,
    )
```

```python
import functools
import math

import jax
import jax.numpy as jnp
from jax import lax
from jax.experimental import pallas as pl
from jax.experimental.pallas import tpu as pltpu
from jax.sharding import PartitionSpec as P


def doc_table(doc_starts, tok_dev):
    n_outer, n_inner, n_slots = doc_starts.shape
    flat_starts = doc_starts.reshape(n_outer * n_inner, n_slots)
    start_counts = jnp.sum((flat_starts < tok_dev).astype(jnp.int32), axis=1)
    first_index = jnp.cumsum(start_counts) - start_counts
    offsets = jnp.arange(tok_dev, dtype=jnp.int32)
    inside_count = jnp.sum(
        (flat_starts[:, None, :] <= offsets[None, :, None]).astype(jnp.int32), axis=2
    )
    return (first_index[:, None] + inside_count - 1).reshape(n_outer, n_inner, tok_dev)


def attention_kernel(
    order_ref, qmeta_ref, kmeta_ref, q_ref, g_ref, k_ref, v_ref,
    o_ref, dq_ref, dkv_ref, dkt_ref, dvt_ref, *, scaling, n_heads, head_dim, slot_len
):
    step = pl.program_id(0)

    @pl.when(step == 0)
    def _():
        dkt_ref[...] = jnp.zeros_like(dkt_ref)
        dvt_ref[...] = jnp.zeros_like(dvt_ref)

    k = k_ref[...]
    v = v_ref[...]
    kt = k.T
    vt = v.T
    contract_first = (((0,), (0,)), ((), ()))
    lanes = qmeta_ref.shape[1] // 2
    allowed = (qmeta_ref[:, 0:1] == kmeta_ref[0:1, :]) & (
        kmeta_ref[1:2, :] <= qmeta_ref[:, lanes : lanes + 1]
    )
    for h in range(n_heads):
        cols = slice(h * head_dim, (h + 1) * head_dim)
        q = q_ref[:, cols]
        g = g_ref[:, cols]
        scores = jnp.dot(q, kt, preferred_element_type=jnp.float32) * scaling
        scores = jnp.where(allowed, scores, -jnp.inf)
        row_max = jnp.max(scores, axis=1, keepdims=True)
        log_total = row_max + jnp.log(
            jnp.sum(jnp.exp(scores - row_max), axis=1, keepdims=True)
        )
        probs = jnp.exp(scores - log_total)
        probs_low = probs.astype(jnp.bfloat16)
        attn = jnp.dot(probs_low, v, preferred_element_type=jnp.float32).astype(jnp.bfloat16)
        o_ref[:, cols] = attn
        inner_prod = jnp.sum(
            g.astype(jnp.float32) * attn.astype(jnp.float32), axis=1, keepdims=True
        )
        grad_probs = jnp.dot(g, vt, preferred_element_type=jnp.float32)
        score_grads = (probs * (grad_probs - inner_prod)).astype(jnp.bfloat16)
        dq_ref[:, cols] = (
            jnp.dot(score_grads, k, preferred_element_type=jnp.float32) * scaling
        ).astype(jnp.bfloat16)
        dkt_ref[...] += (
            lax.dot_general(q, score_grads, contract_first, preferred_element_type=jnp.float32)
            * scaling
        )
        dvt_ref[...] += lax.dot_general(
            g, probs_low, contract_first, preferred_element_type=jnp.float32
        )

    @pl.when(step == pl.num_programs(0) - 1)
    def _():
        n_used = dkt_ref.shape[1] // slot_len
        for r in range(n_used):
            cols = slice(r * slot_len, (r + 1) * slot_len)
            slot = order_ref[r]
            dkv_ref[slot, :, 0:head_dim] = dkt_ref[:, cols].T
            dkv_ref[slot, :, head_dim : 2 * head_dim] = dvt_ref[:, cols].T
        for r in range(n_used, dkv_ref.shape[0]):
            dkv_ref[order_ref[r]] = jnp.zeros(dkv_ref.shape[1:], dkv_ref.dtype)


def attend(rows, qmeta, ctx_all, kmeta_all, order, n_keys, n_heads):
    n_rows = rows.shape[0]
    n_slots = order.shape[0]
    slot_len = ctx_all.shape[0] // n_slots
    head_dim = ctx_all.shape[1] // 2
    width_q = n_heads * head_dim
    block_q = min(256, n_rows)
    grid = (n_rows // block_q,)
    q_spec = pl.BlockSpec((block_q, width_q), lambda i, o: (i, 0))
    g_spec = pl.BlockSpec((block_q, width_q), lambda i, o: (i, 1))
    qmeta_spec = pl.BlockSpec((block_q, qmeta.shape[1]), lambda i, o: (i, 0))
    kmeta_spec = pl.BlockSpec((2, n_keys), lambda i, o: (0, 0))
    k_spec = pl.BlockSpec((n_keys, head_dim), lambda i, o: (0, 0))
    v_spec = pl.BlockSpec((n_keys, head_dim), lambda i, o: (0, 1))
    out_spec = pl.BlockSpec((block_q, width_q), lambda i, o: (i, 0))
    grads_spec = pl.BlockSpec((n_slots, slot_len, 2 * head_dim), lambda i, o: (0, 0, 0))
    kernel = functools.partial(
        attention_kernel,
        scaling=1.0 / math.sqrt(head_dim),
        n_heads=n_heads,
        head_dim=head_dim,
        slot_len=slot_len,
    )
    return pl.pallas_call(
        kernel,
        grid_spec=pltpu.PrefetchScalarGridSpec(
            num_scalar_prefetch=1,
            grid=grid,
            in_specs=[qmeta_spec, kmeta_spec, q_spec, g_spec, k_spec, v_spec],
            out_specs=[out_spec, out_spec, grads_spec],
            scratch_shapes=[
                pltpu.VMEM((head_dim, n_keys), jnp.float32),
                pltpu.VMEM((head_dim, n_keys), jnp.float32),
            ],
        ),
        out_shape=[
            jax.ShapeDtypeStruct((n_rows, width_q), jnp.bfloat16),
            jax.ShapeDtypeStruct((n_rows, width_q), jnp.bfloat16),
            jax.ShapeDtypeStruct((n_slots, slot_len, 2 * head_dim), jnp.float32),
        ],
        compiler_params=pltpu.CompilerParams(dimension_semantics=("arbitrary",)),
    )(order, qmeta, kmeta_all, rows, rows, ctx_all, ctx_all)


def shards(queries, keys, values, grad_out, doc_starts):
    n_inner = lax.axis_size("inner")
    n_outer = lax.axis_size("outer")
    n_units = queries.shape[1]
    piece_len = queries.shape[3]
    width_q = queries.shape[4]
    head_dim = keys.shape[4]
    n_heads = width_q // head_dim
    tok_dev = piece_len * n_inner
    outer_id = lax.axis_index("outer")
    inner_id = lax.axis_index("inner")
    docs_all = doc_table(doc_starts, tok_dev)
    offsets = jnp.arange(tok_dev, dtype=jnp.int32)

    packed = jnp.concatenate(
        [queries[0, :, 0], grad_out[0, :, 0], keys[0, :, 0], values[0, :, 0]], axis=-1
    )
    unit_local = (inner_id + 2 * outer_id) % n_units
    packed = jnp.roll(packed, -2 * outer_id, axis=0)
    arrived = lax.all_to_all(packed, "inner", 0, 0, tiled=True).reshape(tok_dev, -1)
    kv_own = arrived[:, 2 * width_q :]

    pairs_up = [(2 * p, 2 * p + 1) for p in range(n_inner // 2)]
    kv_partner = lax.ppermute(kv_own, "inner", pairs_up)

    both = ("outer", "inner")
    last_a, last_b = n_inner - 2, n_inner - 1
    lead = [(-2 * o) % n_inner for o in range(n_outer)]
    send_a = [((o - 1) * n_inner + lead[o] + r, o * n_inner + lead[o] + r)
              for o in range(1, n_outer) for r in range(2)]
    send_b = [((o - 1) * n_inner + lead[o] + r, o * n_inner + lead[o] + 1 - r)
              for o in range(1, n_outer) for r in range(2)]
    recv_a = lax.ppermute(kv_own, both, send_a)
    recv_b = lax.ppermute(kv_own, both, send_b)
    first = unit_local == 0
    kv_prev_a = jnp.where(first, recv_a, recv_b)
    kv_prev_b = jnp.where(first, recv_b, recv_a)

    unit_id = outer_id * n_units + unit_local
    before = jnp.maximum(outer_id - 1, 0)
    has_prev = (outer_id > 0) & (unit_local < 2)
    has_partner = unit_local % 2 == 1
    query_doc = docs_all[outer_id, unit_local]
    query_pos = unit_id * tok_dev + offsets
    partner_doc = jnp.where(has_partner, docs_all[outer_id, jnp.maximum(unit_local - 1, 0)], -3)
    prev_a_doc = jnp.where(has_prev, docs_all[before, last_a], -4)
    prev_b_doc = jnp.where(has_prev, docs_all[before, last_b], -5)
    key_doc = jnp.concatenate([prev_a_doc, prev_b_doc, partner_doc, query_doc])
    key_pos = jnp.concatenate(
        [
            (before * n_units + last_a) * tok_dev + offsets,
            (before * n_units + last_b) * tok_dev + offsets,
            (unit_id - 1) * tok_dev + offsets,
            query_pos,
        ]
    )
    n_slots = 4
    slot_kv = jnp.stack([kv_prev_a, kv_prev_b, kv_partner, kv_own])
    slot_doc = key_doc.reshape(n_slots, tok_dev)
    slot_pos = key_pos.reshape(n_slots, tok_dev)
    needed = (
        (jnp.min(slot_doc, axis=1) <= jnp.max(query_doc))
        & (jnp.max(slot_doc, axis=1) >= jnp.min(query_doc))
        & (jnp.min(slot_pos, axis=1) <= jnp.max(query_pos))
    )
    needed = needed | (jnp.arange(n_slots) == n_slots - 1)
    needed_i = needed.astype(jnp.int32)
    count = jnp.sum(needed_i)
    rank = jnp.where(
        needed, jnp.cumsum(needed_i) - 1, count + jnp.cumsum(1 - needed_i) - 1
    )
    slot_ids = jnp.arange(n_slots, dtype=jnp.int32)
    order = jnp.sum(
        jnp.where(rank[None, :] == slot_ids[:, None], slot_ids[None, :], 0), axis=1
    )
    kv_sorted = slot_kv[order].reshape(n_slots * tok_dev, 2 * head_dim)
    kmeta_sorted = jnp.stack([slot_doc[order].reshape(-1), slot_pos[order].reshape(-1)])
    lane_width = 128
    qmeta = jnp.concatenate(
        [
            jnp.broadcast_to(query_doc[:, None], (tok_dev, lane_width)),
            jnp.broadcast_to(query_pos[:, None], (tok_dev, lane_width)),
        ],
        axis=1,
    )

    def branch(n_used):
        def run(kv_sorted, kmeta_sorted, qmeta, order):
            return attend(
                arrived, qmeta, kv_sorted, kmeta_sorted, order, n_used * tok_dev, n_heads
            )

        return run

    attn, q_grads, kv_grads = lax.switch(
        count - 1,
        [branch(n) for n in range(1, n_slots + 1)],
        kv_sorted,
        kmeta_sorted,
        qmeta,
        order,
    )

    pairs_down = [(b, a) for a, b in pairs_up]
    low = jnp.bfloat16
    from_partner = lax.ppermute(kv_grads[2].astype(low), "inner", pairs_down)
    back_a = [(b, a) for a, b in send_a]
    back_b = [(b, a) for a, b in send_b]
    grads_a = jnp.where(first, kv_grads[0], kv_grads[1])
    grads_b = jnp.where(first, kv_grads[1], kv_grads[0])
    from_next_a = lax.ppermute(grads_a.astype(low), both, back_a)
    from_next_b = lax.ppermute(grads_b.astype(low), both, back_b)
    kv_total = (
        kv_grads[3]
        + from_partner.astype(jnp.float32)
        + from_next_a.astype(jnp.float32)
        + from_next_b.astype(jnp.float32)
    ).astype(jnp.bfloat16)

    result = jnp.concatenate([attn, q_grads, kv_total], axis=-1).reshape(
        n_inner, piece_len, -1
    )
    returned = jnp.roll(
        lax.all_to_all(result, "inner", 0, 0, tiled=True), 2 * outer_id, axis=0
    )
    shape_q = (1, n_units, 1, piece_len, width_q)
    shape_k = (1, n_units, 1, piece_len, head_dim)
    return (
        returned[..., :width_q].reshape(shape_q),
        returned[..., width_q : 2 * width_q].reshape(shape_q),
        returned[..., 2 * width_q : 2 * width_q + head_dim].reshape(shape_k),
        returned[..., 2 * width_q + head_dim :].reshape(shape_k),
    )


def solution(mesh):
    return jax.shard_map(
        shards,
        mesh=mesh,
        in_specs=(
            P("outer", None, "inner", None, None),
            P("outer", None, "inner", None, None),
            P("outer", None, "inner", None, None),
            P("outer", None, "inner", None, None),
            P(),
        ),
        out_specs=(
            P("outer", None, "inner", None, None),
            P("outer", None, "inner", None, None),
            P("outer", None, "inner", None, None),
            P("outer", None, "inner", None, None),
        ),
        check_vma=False,
    )
```

```python
import functools
import math

import jax
import jax.numpy as jnp
from jax import lax
from jax.experimental import pallas as pl
from jax.experimental.pallas import tpu as pltpu
from jax.sharding import PartitionSpec as P


def doc_table(doc_starts, tok_dev):
    n_outer, n_inner, n_slots = doc_starts.shape
    flat_starts = doc_starts.reshape(n_outer * n_inner, n_slots)
    start_counts = jnp.sum((flat_starts < tok_dev).astype(jnp.int32), axis=1)
    first_index = jnp.cumsum(start_counts) - start_counts
    offsets = jnp.arange(tok_dev, dtype=jnp.int32)
    inside_count = jnp.sum(
        (flat_starts[:, None, :] <= offsets[None, :, None]).astype(jnp.int32), axis=2
    )
    return (first_index[:, None] + inside_count - 1).reshape(n_outer, n_inner, tok_dev)


def attention_kernel(
    order_ref, qmeta_ref, kmeta_ref, q_ref, g_ref, k_ref, v_ref,
    o_ref, dq_ref, dkv_ref, dkt_ref, dvt_ref, *, scaling, n_heads, head_dim, slot_len
):
    step = pl.program_id(0)

    @pl.when(step == 0)
    def _():
        dkt_ref[...] = jnp.zeros_like(dkt_ref)
        dvt_ref[...] = jnp.zeros_like(dvt_ref)

    k = k_ref[...]
    v = v_ref[...]
    kt = k.T
    vt = v.T
    contract_first = (((0,), (0,)), ((), ()))
    lanes = qmeta_ref.shape[1] // 2
    allowed = (qmeta_ref[:, 0:1] == kmeta_ref[0:1, :]) & (
        kmeta_ref[1:2, :] <= qmeta_ref[:, lanes : lanes + 1]
    )
    for h in range(n_heads):
        cols = slice(h * head_dim, (h + 1) * head_dim)
        q = q_ref[:, cols]
        g = g_ref[:, cols]
        scores = jnp.dot(q, kt, preferred_element_type=jnp.float32) * scaling
        scores = jnp.where(allowed, scores, -jnp.inf)
        row_max = jnp.max(scores, axis=1, keepdims=True)
        log_total = row_max + jnp.log(
            jnp.sum(jnp.exp(scores - row_max), axis=1, keepdims=True)
        )
        probs = jnp.exp(scores - log_total)
        probs_low = probs.astype(jnp.bfloat16)
        attn = jnp.dot(probs_low, v, preferred_element_type=jnp.float32).astype(jnp.bfloat16)
        o_ref[:, cols] = attn
        inner_prod = jnp.sum(
            g.astype(jnp.float32) * attn.astype(jnp.float32), axis=1, keepdims=True
        )
        grad_probs = jnp.dot(g, vt, preferred_element_type=jnp.float32)
        score_grads = (probs * (grad_probs - inner_prod)).astype(jnp.bfloat16)
        dq_ref[:, cols] = (
            jnp.dot(score_grads, k, preferred_element_type=jnp.float32) * scaling
        ).astype(jnp.bfloat16)
        dkt_ref[...] += (
            lax.dot_general(q, score_grads, contract_first, preferred_element_type=jnp.float32)
            * scaling
        )
        dvt_ref[...] += lax.dot_general(
            g, probs_low, contract_first, preferred_element_type=jnp.float32
        )

    @pl.when(step == pl.num_programs(0) - 1)
    def _():
        n_used = dkt_ref.shape[1] // slot_len
        for r in range(n_used):
            cols = slice(r * slot_len, (r + 1) * slot_len)
            slot = order_ref[r]
            dkv_ref[slot, :, 0:head_dim] = dkt_ref[:, cols].T
            dkv_ref[slot, :, head_dim : 2 * head_dim] = dvt_ref[:, cols].T
        for r in range(n_used, dkv_ref.shape[0]):
            dkv_ref[order_ref[r]] = jnp.zeros(dkv_ref.shape[1:], dkv_ref.dtype)


def attend(rows, qmeta, ctx_all, kmeta_all, order, n_keys, n_heads):
    n_rows = rows.shape[0]
    n_slots = order.shape[0]
    slot_len = ctx_all.shape[0] // n_slots
    head_dim = ctx_all.shape[1] // 2
    width_q = n_heads * head_dim
    block_q = min(256, n_rows)
    grid = (n_rows // block_q,)
    q_spec = pl.BlockSpec((block_q, width_q), lambda i, o: (i, 0))
    g_spec = pl.BlockSpec((block_q, width_q), lambda i, o: (i, 1))
    qmeta_spec = pl.BlockSpec((block_q, qmeta.shape[1]), lambda i, o: (i, 0))
    kmeta_spec = pl.BlockSpec((2, n_keys), lambda i, o: (0, 0))
    k_spec = pl.BlockSpec((n_keys, head_dim), lambda i, o: (0, 0))
    v_spec = pl.BlockSpec((n_keys, head_dim), lambda i, o: (0, 1))
    out_spec = pl.BlockSpec((block_q, width_q), lambda i, o: (i, 0))
    grads_spec = pl.BlockSpec((n_slots, slot_len, 2 * head_dim), lambda i, o: (0, 0, 0))
    kernel = functools.partial(
        attention_kernel,
        scaling=1.0 / math.sqrt(head_dim),
        n_heads=n_heads,
        head_dim=head_dim,
        slot_len=slot_len,
    )
    return pl.pallas_call(
        kernel,
        grid_spec=pltpu.PrefetchScalarGridSpec(
            num_scalar_prefetch=1,
            grid=grid,
            in_specs=[qmeta_spec, kmeta_spec, q_spec, g_spec, k_spec, v_spec],
            out_specs=[out_spec, out_spec, grads_spec],
            scratch_shapes=[
                pltpu.VMEM((head_dim, n_keys), jnp.float32),
                pltpu.VMEM((head_dim, n_keys), jnp.float32),
            ],
        ),
        out_shape=[
            jax.ShapeDtypeStruct((n_rows, width_q), jnp.bfloat16),
            jax.ShapeDtypeStruct((n_rows, width_q), jnp.bfloat16),
            jax.ShapeDtypeStruct((n_slots, slot_len, 2 * head_dim), jnp.float32),
        ],
        compiler_params=pltpu.CompilerParams(dimension_semantics=("arbitrary",)),
    )(order, qmeta, kmeta_all, rows, rows, ctx_all, ctx_all)


def shards(queries, keys, values, grad_out, doc_starts):
    n_inner = lax.axis_size("inner")
    n_outer = lax.axis_size("outer")
    n_units = queries.shape[1]
    piece_len = queries.shape[3]
    width_q = queries.shape[4]
    head_dim = keys.shape[4]
    n_heads = width_q // head_dim
    tok_dev = piece_len * n_inner
    outer_id = lax.axis_index("outer")
    inner_id = lax.axis_index("inner")
    docs_all = doc_table(doc_starts, tok_dev)
    offsets = jnp.arange(tok_dev, dtype=jnp.int32)

    def packed_for(shift):
        def pack(q, g, k, v):
            return jnp.roll(jnp.concatenate([q, g, k, v], axis=-1), -2 * shift, axis=0)

        return pack

    packed = lax.switch(
        outer_id,
        [packed_for(o) for o in range(n_outer)],
        queries[0, :, 0],
        grad_out[0, :, 0],
        keys[0, :, 0],
        values[0, :, 0],
    )
    unit_local = (inner_id + 2 * outer_id) % n_units
    arrived = lax.all_to_all(packed, "inner", 0, 0, tiled=True).reshape(tok_dev, -1)
    kv_own = arrived[:, 2 * width_q :]

    pairs_up = [(2 * p, 2 * p + 1) for p in range(n_inner // 2)]
    kv_partner = lax.ppermute(kv_own, "inner", pairs_up)

    both = ("outer", "inner")
    last_a, last_b = n_inner - 2, n_inner - 1
    lead = [(-2 * o) % n_inner for o in range(n_outer)]
    send_a = [((o - 1) * n_inner + lead[o] + r, o * n_inner + lead[o] + r)
              for o in range(1, n_outer) for r in range(2)]
    send_b = [((o - 1) * n_inner + lead[o] + r, o * n_inner + lead[o] + 1 - r)
              for o in range(1, n_outer) for r in range(2)]
    recv_a = lax.ppermute(kv_own, both, send_a)
    recv_b = lax.ppermute(kv_own, both, send_b)
    first = unit_local == 0
    kv_prev_a = jnp.where(first, recv_a, recv_b)
    kv_prev_b = jnp.where(first, recv_b, recv_a)

    unit_id = outer_id * n_units + unit_local
    before = jnp.maximum(outer_id - 1, 0)
    has_prev = (outer_id > 0) & (unit_local < 2)
    has_partner = unit_local % 2 == 1
    query_doc = docs_all[outer_id, unit_local]
    query_pos = unit_id * tok_dev + offsets
    partner_doc = jnp.where(has_partner, docs_all[outer_id, jnp.maximum(unit_local - 1, 0)], -3)
    prev_a_doc = jnp.where(has_prev, docs_all[before, last_a], -4)
    prev_b_doc = jnp.where(has_prev, docs_all[before, last_b], -5)
    key_doc = jnp.concatenate([prev_a_doc, prev_b_doc, partner_doc, query_doc])
    key_pos = jnp.concatenate(
        [
            (before * n_units + last_a) * tok_dev + offsets,
            (before * n_units + last_b) * tok_dev + offsets,
            (unit_id - 1) * tok_dev + offsets,
            query_pos,
        ]
    )
    n_slots = 4
    slot_kv = jnp.stack([kv_prev_a, kv_prev_b, kv_partner, kv_own])
    slot_doc = key_doc.reshape(n_slots, tok_dev)
    slot_pos = key_pos.reshape(n_slots, tok_dev)
    needed = (
        (jnp.min(slot_doc, axis=1) <= jnp.max(query_doc))
        & (jnp.max(slot_doc, axis=1) >= jnp.min(query_doc))
        & (jnp.min(slot_pos, axis=1) <= jnp.max(query_pos))
    )
    needed = needed | (jnp.arange(n_slots) == n_slots - 1)
    needed_i = needed.astype(jnp.int32)
    count = jnp.sum(needed_i)
    rank = jnp.where(
        needed, jnp.cumsum(needed_i) - 1, count + jnp.cumsum(1 - needed_i) - 1
    )
    slot_ids = jnp.arange(n_slots, dtype=jnp.int32)
    order = jnp.sum(
        jnp.where(rank[None, :] == slot_ids[:, None], slot_ids[None, :], 0), axis=1
    )
    kv_sorted = slot_kv[order].reshape(n_slots * tok_dev, 2 * head_dim)
    kmeta_sorted = jnp.stack([slot_doc[order].reshape(-1), slot_pos[order].reshape(-1)])
    lane_width = 128
    qmeta = jnp.concatenate(
        [
            jnp.broadcast_to(query_doc[:, None], (tok_dev, lane_width)),
            jnp.broadcast_to(query_pos[:, None], (tok_dev, lane_width)),
        ],
        axis=1,
    )

    def branch(n_used):
        def run(kv_sorted, kmeta_sorted, qmeta, order):
            return attend(
                arrived, qmeta, kv_sorted, kmeta_sorted, order, n_used * tok_dev, n_heads
            )

        return run

    attn, q_grads, kv_grads = lax.switch(
        count - 1,
        [branch(n) for n in range(1, n_slots + 1)],
        kv_sorted,
        kmeta_sorted,
        qmeta,
        order,
    )

    pairs_down = [(b, a) for a, b in pairs_up]
    low = jnp.bfloat16
    from_partner = lax.ppermute(kv_grads[2].astype(low), "inner", pairs_down)
    back_a = [(b, a) for a, b in send_a]
    back_b = [(b, a) for a, b in send_b]
    grads_a = jnp.where(first, kv_grads[0], kv_grads[1])
    grads_b = jnp.where(first, kv_grads[1], kv_grads[0])
    from_next_a = lax.ppermute(grads_a.astype(low), both, back_a)
    from_next_b = lax.ppermute(grads_b.astype(low), both, back_b)
    kv_total = (
        kv_grads[3]
        + from_partner.astype(jnp.float32)
        + from_next_a.astype(jnp.float32)
        + from_next_b.astype(jnp.float32)
    ).astype(jnp.bfloat16)

    result = jnp.concatenate([attn, q_grads, kv_total], axis=-1).reshape(
        n_inner, piece_len, -1
    )
    returned = jnp.roll(
        lax.all_to_all(result, "inner", 0, 0, tiled=True), 2 * outer_id, axis=0
    )
    shape_q = (1, n_units, 1, piece_len, width_q)
    shape_k = (1, n_units, 1, piece_len, head_dim)
    return (
        returned[..., :width_q].reshape(shape_q),
        returned[..., width_q : 2 * width_q].reshape(shape_q),
        returned[..., 2 * width_q : 2 * width_q + head_dim].reshape(shape_k),
        returned[..., 2 * width_q + head_dim :].reshape(shape_k),
    )


def solution(mesh):
    return jax.shard_map(
        shards,
        mesh=mesh,
        in_specs=(
            P("outer", None, "inner", None, None),
            P("outer", None, "inner", None, None),
            P("outer", None, "inner", None, None),
            P("outer", None, "inner", None, None),
            P(),
        ),
        out_specs=(
            P("outer", None, "inner", None, None),
            P("outer", None, "inner", None, None),
            P("outer", None, "inner", None, None),
            P("outer", None, "inner", None, None),
        ),
        check_vma=False,
    )
```

```python
import functools
import math

import jax
import jax.numpy as jnp
from jax import lax
from jax.experimental import pallas as pl
from jax.experimental.pallas import tpu as pltpu
from jax.sharding import PartitionSpec as P


def doc_table(doc_starts, tok_dev):
    n_outer, n_inner, n_slots = doc_starts.shape
    flat_starts = doc_starts.reshape(n_outer * n_inner, n_slots)
    start_counts = jnp.sum((flat_starts < tok_dev).astype(jnp.int32), axis=1)
    first_index = jnp.cumsum(start_counts) - start_counts
    offsets = jnp.arange(tok_dev, dtype=jnp.int32)
    inside_count = jnp.sum(
        (flat_starts[:, None, :] <= offsets[None, :, None]).astype(jnp.int32), axis=2
    )
    return (first_index[:, None] + inside_count - 1).reshape(n_outer, n_inner, tok_dev)


def attention_kernel(
    order_ref, qmeta_ref, kmeta_ref, q_ref, g_ref, k_ref, v_ref,
    out_ref, dkv_ref, dkt_ref, dvt_ref, *, scaling, n_heads, head_dim, slot_len
):
    step = pl.program_id(0)

    @pl.when(step == 0)
    def _():
        dkt_ref[...] = jnp.zeros_like(dkt_ref)
        dvt_ref[...] = jnp.zeros_like(dvt_ref)

    k = k_ref[...]
    v = v_ref[...]
    kt = k.T
    vt = v.T
    contract_first = (((0,), (0,)), ((), ()))
    lanes = qmeta_ref.shape[1] // 2
    allowed = (qmeta_ref[:, 0:1] == kmeta_ref[0:1, :]) & (
        kmeta_ref[1:2, :] <= qmeta_ref[:, lanes : lanes + 1]
    )
    for h in range(n_heads):
        cols = slice(h * head_dim, (h + 1) * head_dim)
        q = q_ref[:, cols]
        g = g_ref[:, cols]
        scores = jnp.dot(q, kt, preferred_element_type=jnp.float32) * scaling
        scores = jnp.where(allowed, scores, -jnp.inf)
        row_max = jnp.max(scores, axis=1, keepdims=True)
        log_total = row_max + jnp.log(
            jnp.sum(jnp.exp(scores - row_max), axis=1, keepdims=True)
        )
        probs = jnp.exp(scores - log_total)
        probs_low = probs.astype(jnp.bfloat16)
        attn = jnp.dot(probs_low, v, preferred_element_type=jnp.float32).astype(jnp.bfloat16)
        out_ref[:, cols] = attn
        inner_prod = jnp.sum(
            g.astype(jnp.float32) * attn.astype(jnp.float32), axis=1, keepdims=True
        )
        grad_probs = jnp.dot(g, vt, preferred_element_type=jnp.float32)
        score_grads = (probs * (grad_probs - inner_prod)).astype(jnp.bfloat16)
        dq_cols = slice((n_heads + h) * head_dim, (n_heads + h + 1) * head_dim)
        out_ref[:, dq_cols] = (
            jnp.dot(score_grads, k, preferred_element_type=jnp.float32) * scaling
        ).astype(jnp.bfloat16)
        dkt_ref[...] += (
            lax.dot_general(q, score_grads, contract_first, preferred_element_type=jnp.float32)
            * scaling
        )
        dvt_ref[...] += lax.dot_general(
            g, probs_low, contract_first, preferred_element_type=jnp.float32
        )

    @pl.when(step == pl.num_programs(0) - 1)
    def _():
        n_used = dkt_ref.shape[1] // slot_len
        for r in range(n_used):
            cols = slice(r * slot_len, (r + 1) * slot_len)
            slot = order_ref[r]
            dkv_ref[slot, :, 0:head_dim] = dkt_ref[:, cols].T
            dkv_ref[slot, :, head_dim : 2 * head_dim] = dvt_ref[:, cols].T
        for r in range(n_used, dkv_ref.shape[0]):
            dkv_ref[order_ref[r]] = jnp.zeros(dkv_ref.shape[1:], dkv_ref.dtype)


def attend(rows, qmeta, ctx_all, kmeta_all, order, n_keys, n_heads):
    n_rows = rows.shape[0]
    n_slots = order.shape[0]
    slot_len = ctx_all.shape[0] // n_slots
    head_dim = ctx_all.shape[1] // 2
    width_q = n_heads * head_dim
    block_q = min(256, n_rows)
    grid = (n_rows // block_q,)
    q_spec = pl.BlockSpec((block_q, width_q), lambda i, o: (i, 0))
    g_spec = pl.BlockSpec((block_q, width_q), lambda i, o: (i, 1))
    qmeta_spec = pl.BlockSpec((block_q, qmeta.shape[1]), lambda i, o: (i, 0))
    kmeta_spec = pl.BlockSpec((2, n_keys), lambda i, o: (0, 0))
    k_spec = pl.BlockSpec((n_keys, head_dim), lambda i, o: (0, 0))
    v_spec = pl.BlockSpec((n_keys, head_dim), lambda i, o: (0, 1))
    out_width = 2 * width_q + 2 * head_dim
    out_spec = pl.BlockSpec((block_q, out_width), lambda i, o: (i, 0))
    grads_spec = pl.BlockSpec((n_slots, slot_len, 2 * head_dim), lambda i, o: (0, 0, 0))
    kernel = functools.partial(
        attention_kernel,
        scaling=1.0 / math.sqrt(head_dim),
        n_heads=n_heads,
        head_dim=head_dim,
        slot_len=slot_len,
    )
    return pl.pallas_call(
        kernel,
        grid_spec=pltpu.PrefetchScalarGridSpec(
            num_scalar_prefetch=1,
            grid=grid,
            in_specs=[qmeta_spec, kmeta_spec, q_spec, g_spec, k_spec, v_spec],
            out_specs=[out_spec, grads_spec],
            scratch_shapes=[
                pltpu.VMEM((head_dim, n_keys), jnp.float32),
                pltpu.VMEM((head_dim, n_keys), jnp.float32),
            ],
        ),
        out_shape=[
            jax.ShapeDtypeStruct((n_rows, out_width), jnp.bfloat16),
            jax.ShapeDtypeStruct((n_slots, slot_len, 2 * head_dim), jnp.float32),
        ],
        compiler_params=pltpu.CompilerParams(dimension_semantics=("arbitrary",)),
    )(order, qmeta, kmeta_all, rows, rows, ctx_all, ctx_all)


def shards(queries, keys, values, grad_out, doc_starts):
    n_inner = lax.axis_size("inner")
    n_outer = lax.axis_size("outer")
    n_units = queries.shape[1]
    piece_len = queries.shape[3]
    width_q = queries.shape[4]
    head_dim = keys.shape[4]
    n_heads = width_q // head_dim
    tok_dev = piece_len * n_inner
    outer_id = lax.axis_index("outer")
    inner_id = lax.axis_index("inner")
    docs_all = doc_table(doc_starts, tok_dev)
    offsets = jnp.arange(tok_dev, dtype=jnp.int32)

    def packed_for(shift):
        def pack(q, g, k, v):
            return jnp.roll(jnp.concatenate([q, g, k, v], axis=-1), -2 * shift, axis=0)

        return pack

    packed = lax.switch(
        outer_id,
        [packed_for(o) for o in range(n_outer)],
        queries[0, :, 0],
        grad_out[0, :, 0],
        keys[0, :, 0],
        values[0, :, 0],
    )
    unit_local = (inner_id + 2 * outer_id) % n_units
    arrived = lax.all_to_all(packed, "inner", 0, 0, tiled=True).reshape(tok_dev, -1)
    kv_own = arrived[:, 2 * width_q :]

    pairs_up = [(2 * p, 2 * p + 1) for p in range(n_inner // 2)]
    kv_partner = lax.ppermute(kv_own, "inner", pairs_up)

    both = ("outer", "inner")
    last_a, last_b = n_inner - 2, n_inner - 1
    lead = [(-2 * o) % n_inner for o in range(n_outer)]
    send_a = [((o - 1) * n_inner + lead[o] + r, o * n_inner + lead[o] + r)
              for o in range(1, n_outer) for r in range(2)]
    send_b = [((o - 1) * n_inner + lead[o] + r, o * n_inner + lead[o] + 1 - r)
              for o in range(1, n_outer) for r in range(2)]
    recv_a = lax.ppermute(kv_own, both, send_a)
    recv_b = lax.ppermute(kv_own, both, send_b)
    first = unit_local == 0
    kv_prev_a = jnp.where(first, recv_a, recv_b)
    kv_prev_b = jnp.where(first, recv_b, recv_a)

    unit_id = outer_id * n_units + unit_local
    before = jnp.maximum(outer_id - 1, 0)
    has_prev = (outer_id > 0) & (unit_local < 2)
    has_partner = unit_local % 2 == 1
    query_doc = docs_all[outer_id, unit_local]
    query_pos = unit_id * tok_dev + offsets
    partner_doc = jnp.where(has_partner, docs_all[outer_id, jnp.maximum(unit_local - 1, 0)], -3)
    prev_a_doc = jnp.where(has_prev, docs_all[before, last_a], -4)
    prev_b_doc = jnp.where(has_prev, docs_all[before, last_b], -5)
    key_doc = jnp.concatenate([prev_a_doc, prev_b_doc, partner_doc, query_doc])
    key_pos = jnp.concatenate(
        [
            (before * n_units + last_a) * tok_dev + offsets,
            (before * n_units + last_b) * tok_dev + offsets,
            (unit_id - 1) * tok_dev + offsets,
            query_pos,
        ]
    )
    n_slots = 4
    slot_kv = jnp.stack([kv_prev_a, kv_prev_b, kv_partner, kv_own])
    slot_doc = key_doc.reshape(n_slots, tok_dev)
    slot_pos = key_pos.reshape(n_slots, tok_dev)
    needed = (
        (jnp.min(slot_doc, axis=1) <= jnp.max(query_doc))
        & (jnp.max(slot_doc, axis=1) >= jnp.min(query_doc))
        & (jnp.min(slot_pos, axis=1) <= jnp.max(query_pos))
    )
    needed = needed | (jnp.arange(n_slots) == n_slots - 1)
    needed_i = needed.astype(jnp.int32)
    count = jnp.sum(needed_i)
    rank = jnp.where(
        needed, jnp.cumsum(needed_i) - 1, count + jnp.cumsum(1 - needed_i) - 1
    )
    slot_ids = jnp.arange(n_slots, dtype=jnp.int32)
    order = jnp.sum(
        jnp.where(rank[None, :] == slot_ids[:, None], slot_ids[None, :], 0), axis=1
    )
    kv_sorted = slot_kv[order].reshape(n_slots * tok_dev, 2 * head_dim)
    kmeta_sorted = jnp.stack([slot_doc[order].reshape(-1), slot_pos[order].reshape(-1)])
    lane_width = 128
    qmeta = jnp.concatenate(
        [
            jnp.broadcast_to(query_doc[:, None], (tok_dev, lane_width)),
            jnp.broadcast_to(query_pos[:, None], (tok_dev, lane_width)),
        ],
        axis=1,
    )

    def branch(n_used):
        def run(kv_sorted, kmeta_sorted, qmeta, order):
            return attend(
                arrived, qmeta, kv_sorted, kmeta_sorted, order, n_used * tok_dev, n_heads
            )

        return run

    out_rows, kv_grads = lax.switch(
        count - 1,
        [branch(n) for n in range(1, n_slots + 1)],
        kv_sorted,
        kmeta_sorted,
        qmeta,
        order,
    )

    pairs_down = [(b, a) for a, b in pairs_up]
    low = jnp.bfloat16
    from_partner = lax.ppermute(kv_grads[2].astype(low), "inner", pairs_down)
    back_a = [(b, a) for a, b in send_a]
    back_b = [(b, a) for a, b in send_b]
    grads_a = jnp.where(first, kv_grads[0], kv_grads[1])
    grads_b = jnp.where(first, kv_grads[1], kv_grads[0])
    from_next_a = lax.ppermute(grads_a.astype(low), both, back_a)
    from_next_b = lax.ppermute(grads_b.astype(low), both, back_b)
    kv_total = (
        kv_grads[3]
        + from_partner.astype(jnp.float32)
        + from_next_a.astype(jnp.float32)
        + from_next_b.astype(jnp.float32)
    ).astype(jnp.bfloat16)

    result = out_rows.at[:, 2 * width_q :].set(kv_total).reshape(
        n_inner, piece_len, -1
    )
    returned = jnp.roll(
        lax.all_to_all(result, "inner", 0, 0, tiled=True), 2 * outer_id, axis=0
    )
    shape_q = (1, n_units, 1, piece_len, width_q)
    shape_k = (1, n_units, 1, piece_len, head_dim)
    return (
        returned[..., :width_q].reshape(shape_q),
        returned[..., width_q : 2 * width_q].reshape(shape_q),
        returned[..., 2 * width_q : 2 * width_q + head_dim].reshape(shape_k),
        returned[..., 2 * width_q + head_dim :].reshape(shape_k),
    )


def solution(mesh):
    return jax.shard_map(
        shards,
        mesh=mesh,
        in_specs=(
            P("outer", None, "inner", None, None),
            P("outer", None, "inner", None, None),
            P("outer", None, "inner", None, None),
            P("outer", None, "inner", None, None),
            P(),
        ),
        out_specs=(
            P("outer", None, "inner", None, None),
            P("outer", None, "inner", None, None),
            P("outer", None, "inner", None, None),
            P("outer", None, "inner", None, None),
        ),
        check_vma=False,
    )
```

```python
import functools
import math

import jax
import jax.numpy as jnp
from jax import lax
from jax.experimental import pallas as pl
from jax.experimental.pallas import tpu as pltpu
from jax.sharding import PartitionSpec as P


def doc_table(doc_starts, tok_dev):
    n_outer, n_inner, n_slots = doc_starts.shape
    flat_starts = doc_starts.reshape(n_outer * n_inner, n_slots)
    start_counts = jnp.sum((flat_starts < tok_dev).astype(jnp.int32), axis=1)
    first_index = jnp.cumsum(start_counts) - start_counts
    offsets = jnp.arange(tok_dev, dtype=jnp.int32)
    inside_count = jnp.sum(
        (flat_starts[:, None, :] <= offsets[None, :, None]).astype(jnp.int32), axis=2
    )
    return (first_index[:, None] + inside_count - 1).reshape(n_outer, n_inner, tok_dev)


def attention_kernel(
    order_ref, qmeta_ref, kmeta_ref, q_ref, g_ref, k_ref, v_ref,
    o_ref, dq_ref, dkv_ref, dkt_ref, dvt_ref, *, scaling, n_heads, head_dim, slot_len
):
    step = pl.program_id(0)

    @pl.when(step == 0)
    def _():
        dkt_ref[...] = jnp.zeros_like(dkt_ref)
        dvt_ref[...] = jnp.zeros_like(dvt_ref)

    k = k_ref[...]
    v = v_ref[...]
    kt = k.T
    vt = v.T
    contract_first = (((0,), (0,)), ((), ()))
    lanes = qmeta_ref.shape[1] // 2
    allowed = (qmeta_ref[:, 0:1] == kmeta_ref[0:1, :]) & (
        kmeta_ref[1:2, :] <= qmeta_ref[:, lanes : lanes + 1]
    )
    for h in range(n_heads):
        cols = slice(h * head_dim, (h + 1) * head_dim)
        q = q_ref[:, cols]
        g = g_ref[:, cols]
        scores = jnp.dot(q, kt, preferred_element_type=jnp.float32) * scaling
        scores = jnp.where(allowed, scores, -jnp.inf)
        row_max = jnp.max(scores, axis=1, keepdims=True)
        log_total = row_max + jnp.log(
            jnp.sum(jnp.exp(scores - row_max), axis=1, keepdims=True)
        )
        probs = jnp.exp(scores - log_total)
        probs_low = probs.astype(jnp.bfloat16)
        attn = jnp.dot(probs_low, v, preferred_element_type=jnp.float32).astype(jnp.bfloat16)
        o_ref[:, cols] = attn
        inner_prod = jnp.sum(
            g.astype(jnp.float32) * attn.astype(jnp.float32), axis=1, keepdims=True
        )
        grad_probs = jnp.dot(g, vt, preferred_element_type=jnp.float32)
        score_grads = (probs * (grad_probs - inner_prod)).astype(jnp.bfloat16)
        dq_ref[:, cols] = (
            jnp.dot(score_grads, k, preferred_element_type=jnp.float32) * scaling
        ).astype(jnp.bfloat16)
        dkt_ref[...] += (
            lax.dot_general(q, score_grads, contract_first, preferred_element_type=jnp.float32)
            * scaling
        )
        dvt_ref[...] += lax.dot_general(
            g, probs_low, contract_first, preferred_element_type=jnp.float32
        )

    @pl.when(step == pl.num_programs(0) - 1)
    def _():
        n_used = dkt_ref.shape[1] // slot_len
        for r in range(n_used):
            cols = slice(r * slot_len, (r + 1) * slot_len)
            slot = order_ref[r]
            dkv_ref[slot, :, 0:head_dim] = dkt_ref[:, cols].T
            dkv_ref[slot, :, head_dim : 2 * head_dim] = dvt_ref[:, cols].T
        for r in range(n_used, dkv_ref.shape[0]):
            dkv_ref[order_ref[r]] = jnp.zeros(dkv_ref.shape[1:], dkv_ref.dtype)


def attend(rows, qmeta, ctx_all, kmeta_all, order, n_keys, n_heads):
    n_rows = rows.shape[0]
    n_slots = order.shape[0]
    slot_len = ctx_all.shape[0] // n_slots
    head_dim = ctx_all.shape[1] // 2
    width_q = n_heads * head_dim
    block_q = min(128, n_rows)
    grid = (n_rows // block_q,)
    q_spec = pl.BlockSpec((block_q, width_q), lambda i, o: (i, 0))
    g_spec = pl.BlockSpec((block_q, width_q), lambda i, o: (i, 1))
    qmeta_spec = pl.BlockSpec((block_q, qmeta.shape[1]), lambda i, o: (i, 0))
    kmeta_spec = pl.BlockSpec((2, n_keys), lambda i, o: (0, 0))
    k_spec = pl.BlockSpec((n_keys, head_dim), lambda i, o: (0, 0))
    v_spec = pl.BlockSpec((n_keys, head_dim), lambda i, o: (0, 1))
    out_spec = pl.BlockSpec((block_q, width_q), lambda i, o: (i, 0))
    grads_spec = pl.BlockSpec((n_slots, slot_len, 2 * head_dim), lambda i, o: (0, 0, 0))
    kernel = functools.partial(
        attention_kernel,
        scaling=1.0 / math.sqrt(head_dim),
        n_heads=n_heads,
        head_dim=head_dim,
        slot_len=slot_len,
    )
    return pl.pallas_call(
        kernel,
        grid_spec=pltpu.PrefetchScalarGridSpec(
            num_scalar_prefetch=1,
            grid=grid,
            in_specs=[qmeta_spec, kmeta_spec, q_spec, g_spec, k_spec, v_spec],
            out_specs=[out_spec, out_spec, grads_spec],
            scratch_shapes=[
                pltpu.VMEM((head_dim, n_keys), jnp.float32),
                pltpu.VMEM((head_dim, n_keys), jnp.float32),
            ],
        ),
        out_shape=[
            jax.ShapeDtypeStruct((n_rows, width_q), jnp.bfloat16),
            jax.ShapeDtypeStruct((n_rows, width_q), jnp.bfloat16),
            jax.ShapeDtypeStruct((n_slots, slot_len, 2 * head_dim), jnp.float32),
        ],
        compiler_params=pltpu.CompilerParams(dimension_semantics=("arbitrary",)),
    )(order, qmeta, kmeta_all, rows, rows, ctx_all, ctx_all)


def shards(queries, keys, values, grad_out, doc_starts):
    n_inner = lax.axis_size("inner")
    n_outer = lax.axis_size("outer")
    n_units = queries.shape[1]
    piece_len = queries.shape[3]
    width_q = queries.shape[4]
    head_dim = keys.shape[4]
    n_heads = width_q // head_dim
    tok_dev = piece_len * n_inner
    outer_id = lax.axis_index("outer")
    inner_id = lax.axis_index("inner")
    docs_all = doc_table(doc_starts, tok_dev)
    offsets = jnp.arange(tok_dev, dtype=jnp.int32)

    def packed_for(shift):
        def pack(q, g, k, v):
            return jnp.roll(jnp.concatenate([q, g, k, v], axis=-1), -2 * shift, axis=0)

        return pack

    packed = lax.switch(
        outer_id,
        [packed_for(o) for o in range(n_outer)],
        queries[0, :, 0],
        grad_out[0, :, 0],
        keys[0, :, 0],
        values[0, :, 0],
    )
    unit_local = (inner_id + 2 * outer_id) % n_units
    arrived = lax.all_to_all(packed, "inner", 0, 0, tiled=True).reshape(tok_dev, -1)
    kv_own = arrived[:, 2 * width_q :]

    pairs_up = [(2 * p, 2 * p + 1) for p in range(n_inner // 2)]
    kv_partner = lax.ppermute(kv_own, "inner", pairs_up)

    both = ("outer", "inner")
    last_a, last_b = n_inner - 2, n_inner - 1
    lead = [(-2 * o) % n_inner for o in range(n_outer)]
    send_a = [((o - 1) * n_inner + lead[o] + r, o * n_inner + lead[o] + r)
              for o in range(1, n_outer) for r in range(2)]
    send_b = [((o - 1) * n_inner + lead[o] + r, o * n_inner + lead[o] + 1 - r)
              for o in range(1, n_outer) for r in range(2)]
    recv_a = lax.ppermute(kv_own, both, send_a)
    recv_b = lax.ppermute(kv_own, both, send_b)
    first = unit_local == 0
    kv_prev_a = jnp.where(first, recv_a, recv_b)
    kv_prev_b = jnp.where(first, recv_b, recv_a)

    unit_id = outer_id * n_units + unit_local
    before = jnp.maximum(outer_id - 1, 0)
    has_prev = (outer_id > 0) & (unit_local < 2)
    has_partner = unit_local % 2 == 1
    query_doc = docs_all[outer_id, unit_local]
    query_pos = unit_id * tok_dev + offsets
    partner_doc = jnp.where(has_partner, docs_all[outer_id, jnp.maximum(unit_local - 1, 0)], -3)
    prev_a_doc = jnp.where(has_prev, docs_all[before, last_a], -4)
    prev_b_doc = jnp.where(has_prev, docs_all[before, last_b], -5)
    key_doc = jnp.concatenate([prev_a_doc, prev_b_doc, partner_doc, query_doc])
    key_pos = jnp.concatenate(
        [
            (before * n_units + last_a) * tok_dev + offsets,
            (before * n_units + last_b) * tok_dev + offsets,
            (unit_id - 1) * tok_dev + offsets,
            query_pos,
        ]
    )
    n_slots = 4
    slot_kv = jnp.stack([kv_prev_a, kv_prev_b, kv_partner, kv_own])
    slot_doc = key_doc.reshape(n_slots, tok_dev)
    slot_pos = key_pos.reshape(n_slots, tok_dev)
    needed = (
        (jnp.min(slot_doc, axis=1) <= jnp.max(query_doc))
        & (jnp.max(slot_doc, axis=1) >= jnp.min(query_doc))
        & (jnp.min(slot_pos, axis=1) <= jnp.max(query_pos))
    )
    needed = needed | (jnp.arange(n_slots) == n_slots - 1)
    needed_i = needed.astype(jnp.int32)
    count = jnp.sum(needed_i)
    rank = jnp.where(
        needed, jnp.cumsum(needed_i) - 1, count + jnp.cumsum(1 - needed_i) - 1
    )
    slot_ids = jnp.arange(n_slots, dtype=jnp.int32)
    order = jnp.sum(
        jnp.where(rank[None, :] == slot_ids[:, None], slot_ids[None, :], 0), axis=1
    )
    kv_sorted = slot_kv[order].reshape(n_slots * tok_dev, 2 * head_dim)
    kmeta_sorted = jnp.stack([slot_doc[order].reshape(-1), slot_pos[order].reshape(-1)])
    lane_width = 128
    qmeta = jnp.concatenate(
        [
            jnp.broadcast_to(query_doc[:, None], (tok_dev, lane_width)),
            jnp.broadcast_to(query_pos[:, None], (tok_dev, lane_width)),
        ],
        axis=1,
    )

    def branch(n_used):
        def run(kv_sorted, kmeta_sorted, qmeta, order):
            return attend(
                arrived, qmeta, kv_sorted, kmeta_sorted, order, n_used * tok_dev, n_heads
            )

        return run

    attn, q_grads, kv_grads = lax.switch(
        count - 1,
        [branch(n) for n in range(1, n_slots + 1)],
        kv_sorted,
        kmeta_sorted,
        qmeta,
        order,
    )

    pairs_down = [(b, a) for a, b in pairs_up]
    low = jnp.bfloat16
    from_partner = lax.ppermute(kv_grads[2].astype(low), "inner", pairs_down)
    back_a = [(b, a) for a, b in send_a]
    back_b = [(b, a) for a, b in send_b]
    grads_a = jnp.where(first, kv_grads[0], kv_grads[1])
    grads_b = jnp.where(first, kv_grads[1], kv_grads[0])
    from_next_a = lax.ppermute(grads_a.astype(low), both, back_a)
    from_next_b = lax.ppermute(grads_b.astype(low), both, back_b)
    kv_total = (
        kv_grads[3]
        + from_partner.astype(jnp.float32)
        + from_next_a.astype(jnp.float32)
        + from_next_b.astype(jnp.float32)
    ).astype(jnp.bfloat16)

    result = jnp.concatenate([attn, q_grads, kv_total], axis=-1).reshape(
        n_inner, piece_len, -1
    )
    returned = jnp.roll(
        lax.all_to_all(result, "inner", 0, 0, tiled=True), 2 * outer_id, axis=0
    )
    shape_q = (1, n_units, 1, piece_len, width_q)
    shape_k = (1, n_units, 1, piece_len, head_dim)
    return (
        returned[..., :width_q].reshape(shape_q),
        returned[..., width_q : 2 * width_q].reshape(shape_q),
        returned[..., 2 * width_q : 2 * width_q + head_dim].reshape(shape_k),
        returned[..., 2 * width_q + head_dim :].reshape(shape_k),
    )


def solution(mesh):
    return jax.shard_map(
        shards,
        mesh=mesh,
        in_specs=(
            P("outer", None, "inner", None, None),
            P("outer", None, "inner", None, None),
            P("outer", None, "inner", None, None),
            P("outer", None, "inner", None, None),
            P(),
        ),
        out_specs=(
            P("outer", None, "inner", None, None),
            P("outer", None, "inner", None, None),
            P("outer", None, "inner", None, None),
            P("outer", None, "inner", None, None),
        ),
        check_vma=False,
    )
```

```python
import functools
import math

import jax
import jax.numpy as jnp
from jax import lax
from jax.experimental import pallas as pl
from jax.experimental.pallas import tpu as pltpu
from jax.sharding import PartitionSpec as P


def doc_table(doc_starts, tok_dev):
    n_outer, n_inner, n_slots = doc_starts.shape
    flat_starts = doc_starts.reshape(n_outer * n_inner, n_slots)
    start_counts = jnp.sum((flat_starts < tok_dev).astype(jnp.int32), axis=1)
    first_index = jnp.cumsum(start_counts) - start_counts
    offsets = jnp.arange(tok_dev, dtype=jnp.int32)
    inside_count = jnp.sum(
        (flat_starts[:, None, :] <= offsets[None, :, None]).astype(jnp.int32), axis=2
    )
    return (first_index[:, None] + inside_count - 1).reshape(n_outer, n_inner, tok_dev)


def attention_kernel(
    order_ref, qmeta_ref, kmeta_ref, q_ref, g_ref, k_ref, v_ref,
    o_ref, dq_ref, dkv_ref, dkt_ref, dvt_ref, *, scaling, n_heads, head_dim, slot_len
):
    step = pl.program_id(0)

    @pl.when(step == 0)
    def _():
        dkt_ref[...] = jnp.zeros_like(dkt_ref)
        dvt_ref[...] = jnp.zeros_like(dvt_ref)

    k = k_ref[...]
    v = v_ref[...]
    kt = k.T
    vt = v.T
    contract_first = (((0,), (0,)), ((), ()))
    lanes = qmeta_ref.shape[1] // 2
    allowed = (qmeta_ref[:, 0:1] == kmeta_ref[0:1, :]) & (
        kmeta_ref[1:2, :] <= qmeta_ref[:, lanes : lanes + 1]
    )
    for h in range(n_heads):
        cols = slice(h * head_dim, (h + 1) * head_dim)
        q = q_ref[:, cols]
        g = g_ref[:, cols]
        scores = jnp.dot(q, kt, preferred_element_type=jnp.float32) * scaling
        scores = jnp.where(allowed, scores, -jnp.inf)
        row_max = jnp.max(scores, axis=1, keepdims=True)
        log_total = row_max + jnp.log(
            jnp.sum(jnp.exp(scores - row_max), axis=1, keepdims=True)
        )
        probs = jnp.exp(scores - log_total)
        probs_low = probs.astype(jnp.bfloat16)
        attn = jnp.dot(probs_low, v, preferred_element_type=jnp.float32).astype(jnp.bfloat16)
        o_ref[:, cols] = attn
        inner_prod = jnp.sum(
            g.astype(jnp.float32) * attn.astype(jnp.float32), axis=1, keepdims=True
        )
        grad_probs = jnp.dot(g, vt, preferred_element_type=jnp.float32)
        score_grads = (probs * (grad_probs - inner_prod)).astype(jnp.bfloat16)
        dq_ref[:, cols] = (
            jnp.dot(score_grads, k, preferred_element_type=jnp.float32) * scaling
        ).astype(jnp.bfloat16)
        dkt_ref[...] += (
            lax.dot_general(q, score_grads, contract_first, preferred_element_type=jnp.float32)
            * scaling
        )
        dvt_ref[...] += lax.dot_general(
            g, probs_low, contract_first, preferred_element_type=jnp.float32
        )

    @pl.when(step == pl.num_programs(0) - 1)
    def _():
        n_used = dkt_ref.shape[1] // slot_len
        for r in range(n_used):
            cols = slice(r * slot_len, (r + 1) * slot_len)
            slot = order_ref[r]
            dkv_ref[slot, :, 0:head_dim] = dkt_ref[:, cols].T
            dkv_ref[slot, :, head_dim : 2 * head_dim] = dvt_ref[:, cols].T
        for r in range(n_used, dkv_ref.shape[0]):
            dkv_ref[order_ref[r]] = jnp.zeros(dkv_ref.shape[1:], dkv_ref.dtype)


def attend(rows, qmeta, ctx_all, kmeta_all, order, n_keys, n_heads):
    n_rows = rows.shape[0]
    n_slots = order.shape[0]
    slot_len = ctx_all.shape[0] // n_slots
    head_dim = ctx_all.shape[1] // 2
    width_q = n_heads * head_dim
    block_q = min(256, n_rows)
    grid = (n_rows // block_q,)
    q_spec = pl.BlockSpec((block_q, width_q), lambda i, o: (i, 0))
    g_spec = pl.BlockSpec((block_q, width_q), lambda i, o: (i, 1))
    qmeta_spec = pl.BlockSpec((block_q, qmeta.shape[1]), lambda i, o: (i, 0))
    kmeta_spec = pl.BlockSpec((2, n_keys), lambda i, o: (0, 0))
    k_spec = pl.BlockSpec((n_keys, head_dim), lambda i, o: (0, 0))
    v_spec = pl.BlockSpec((n_keys, head_dim), lambda i, o: (0, 1))
    out_spec = pl.BlockSpec((block_q, width_q), lambda i, o: (i, 0))
    grads_spec = pl.BlockSpec((n_slots, slot_len, 2 * head_dim), lambda i, o: (0, 0, 0))
    kernel = functools.partial(
        attention_kernel,
        scaling=1.0 / math.sqrt(head_dim),
        n_heads=n_heads,
        head_dim=head_dim,
        slot_len=slot_len,
    )
    return pl.pallas_call(
        kernel,
        grid_spec=pltpu.PrefetchScalarGridSpec(
            num_scalar_prefetch=1,
            grid=grid,
            in_specs=[qmeta_spec, kmeta_spec, q_spec, g_spec, k_spec, v_spec],
            out_specs=[out_spec, out_spec, grads_spec],
            scratch_shapes=[
                pltpu.VMEM((head_dim, n_keys), jnp.float32),
                pltpu.VMEM((head_dim, n_keys), jnp.float32),
            ],
        ),
        out_shape=[
            jax.ShapeDtypeStruct((n_rows, width_q), jnp.bfloat16),
            jax.ShapeDtypeStruct((n_rows, width_q), jnp.bfloat16),
            jax.ShapeDtypeStruct((n_slots, slot_len, 2 * head_dim), jnp.float32),
        ],
        compiler_params=pltpu.CompilerParams(dimension_semantics=("arbitrary",)),
    )(order, qmeta, kmeta_all, rows, rows, ctx_all, ctx_all)


def shards(queries, keys, values, grad_out, doc_starts):
    n_inner = lax.axis_size("inner")
    n_outer = lax.axis_size("outer")
    n_units = queries.shape[1]
    piece_len = queries.shape[3]
    width_q = queries.shape[4]
    head_dim = keys.shape[4]
    n_heads = width_q // head_dim
    tok_dev = piece_len * n_inner
    outer_id = lax.axis_index("outer")
    inner_id = lax.axis_index("inner")
    docs_all = doc_table(doc_starts, tok_dev)
    offsets = jnp.arange(tok_dev, dtype=jnp.int32)

    def packed_for(shift):
        def pack(q, g, k, v):
            return jnp.roll(jnp.concatenate([q, g, k, v], axis=-1), -2 * shift, axis=0)

        return pack

    packed = lax.switch(
        outer_id,
        [packed_for(o) for o in range(n_outer)],
        queries[0, :, 0],
        grad_out[0, :, 0],
        keys[0, :, 0],
        values[0, :, 0],
    )
    unit_local = (inner_id + 2 * outer_id) % n_units
    arrived = lax.all_to_all(packed, "inner", 0, 0, tiled=True).reshape(tok_dev, -1)
    kv_own = arrived[:, 2 * width_q :]

    pairs_up = [(2 * p, 2 * p + 1) for p in range(n_inner // 2)]
    kv_partner = lax.ppermute(kv_own, "inner", pairs_up)

    both = ("outer", "inner")
    last_a, last_b = n_inner - 2, n_inner - 1
    lead = [(-2 * o) % n_inner for o in range(n_outer)]
    send_a = [((o - 1) * n_inner + lead[o] + r, o * n_inner + lead[o] + r)
              for o in range(1, n_outer) for r in range(2)]
    send_b = [((o - 1) * n_inner + lead[o] + r, o * n_inner + lead[o] + 1 - r)
              for o in range(1, n_outer) for r in range(2)]
    recv_a = lax.ppermute(kv_own, both, send_a)
    recv_b = lax.ppermute(kv_own, both, send_b)
    first = unit_local == 0
    kv_prev_a = jnp.where(first, recv_a, recv_b)
    kv_prev_b = jnp.where(first, recv_b, recv_a)

    unit_id = outer_id * n_units + unit_local
    before = jnp.maximum(outer_id - 1, 0)
    has_prev = (outer_id > 0) & (unit_local < 2)
    has_partner = unit_local % 2 == 1
    query_doc = docs_all[outer_id, unit_local]
    query_pos = unit_id * tok_dev + offsets
    partner_doc = jnp.where(has_partner, docs_all[outer_id, jnp.maximum(unit_local - 1, 0)], -3)
    prev_a_doc = jnp.where(has_prev, docs_all[before, last_a], -4)
    prev_b_doc = jnp.where(has_prev, docs_all[before, last_b], -5)
    key_doc = jnp.concatenate([prev_a_doc, prev_b_doc, partner_doc, query_doc])
    key_pos = jnp.concatenate(
        [
            (before * n_units + last_a) * tok_dev + offsets,
            (before * n_units + last_b) * tok_dev + offsets,
            (unit_id - 1) * tok_dev + offsets,
            query_pos,
        ]
    )
    n_slots = 8
    slot_len = tok_dev * 4 // n_slots
    slot_kv = jnp.stack([kv_prev_a, kv_prev_b, kv_partner, kv_own]).reshape(
        n_slots, slot_len, 2 * head_dim
    )
    slot_doc = key_doc.reshape(n_slots, slot_len)
    slot_pos = key_pos.reshape(n_slots, slot_len)
    needed = (
        (jnp.min(slot_doc, axis=1) <= jnp.max(query_doc))
        & (jnp.max(slot_doc, axis=1) >= jnp.min(query_doc))
        & (jnp.min(slot_pos, axis=1) <= jnp.max(query_pos))
    )
    needed = needed | (jnp.arange(n_slots) >= n_slots - 2)
    needed_i = needed.astype(jnp.int32)
    count = jnp.sum(needed_i)
    rank = jnp.where(
        needed, jnp.cumsum(needed_i) - 1, count + jnp.cumsum(1 - needed_i) - 1
    )
    slot_ids = jnp.arange(n_slots, dtype=jnp.int32)
    order = jnp.sum(
        jnp.where(rank[None, :] == slot_ids[:, None], slot_ids[None, :], 0), axis=1
    )
    kv_sorted = slot_kv[order].reshape(n_slots * slot_len, 2 * head_dim)
    kmeta_sorted = jnp.stack([slot_doc[order].reshape(-1), slot_pos[order].reshape(-1)])
    lane_width = 128
    qmeta = jnp.concatenate(
        [
            jnp.broadcast_to(query_doc[:, None], (tok_dev, lane_width)),
            jnp.broadcast_to(query_pos[:, None], (tok_dev, lane_width)),
        ],
        axis=1,
    )

    def branch(n_used):
        def run(kv_sorted, kmeta_sorted, qmeta, order):
            return attend(
                arrived, qmeta, kv_sorted, kmeta_sorted, order, n_used * slot_len, n_heads
            )

        return run

    sizes = [2, 3, 4, n_slots]
    bucket = sum((count > n).astype(jnp.int32) for n in sizes[:-1])
    attn, q_grads, kv_grads = lax.switch(
        bucket,
        [branch(n) for n in sizes],
        kv_sorted,
        kmeta_sorted,
        qmeta,
        order,
    )

    kv_grads = kv_grads.reshape(4, tok_dev, 2 * head_dim)
    pairs_down = [(b, a) for a, b in pairs_up]
    low = jnp.bfloat16
    from_partner = lax.ppermute(kv_grads[2].astype(low), "inner", pairs_down)
    back_a = [(b, a) for a, b in send_a]
    back_b = [(b, a) for a, b in send_b]
    grads_a = jnp.where(first, kv_grads[0], kv_grads[1])
    grads_b = jnp.where(first, kv_grads[1], kv_grads[0])
    from_next_a = lax.ppermute(grads_a.astype(low), both, back_a)
    from_next_b = lax.ppermute(grads_b.astype(low), both, back_b)
    kv_total = (
        kv_grads[3]
        + from_partner.astype(jnp.float32)
        + from_next_a.astype(jnp.float32)
        + from_next_b.astype(jnp.float32)
    ).astype(jnp.bfloat16)

    result = jnp.concatenate([attn, q_grads, kv_total], axis=-1).reshape(
        n_inner, piece_len, -1
    )
    returned = jnp.roll(
        lax.all_to_all(result, "inner", 0, 0, tiled=True), 2 * outer_id, axis=0
    )
    shape_q = (1, n_units, 1, piece_len, width_q)
    shape_k = (1, n_units, 1, piece_len, head_dim)
    return (
        returned[..., :width_q].reshape(shape_q),
        returned[..., width_q : 2 * width_q].reshape(shape_q),
        returned[..., 2 * width_q : 2 * width_q + head_dim].reshape(shape_k),
        returned[..., 2 * width_q + head_dim :].reshape(shape_k),
    )


def solution(mesh):
    return jax.shard_map(
        shards,
        mesh=mesh,
        in_specs=(
            P("outer", None, "inner", None, None),
            P("outer", None, "inner", None, None),
            P("outer", None, "inner", None, None),
            P("outer", None, "inner", None, None),
            P(),
        ),
        out_specs=(
            P("outer", None, "inner", None, None),
            P("outer", None, "inner", None, None),
            P("outer", None, "inner", None, None),
            P("outer", None, "inner", None, None),
        ),
        check_vma=False,
    )
```

```python
import functools
import math

import jax
import jax.numpy as jnp
from jax import lax
from jax.experimental import pallas as pl
from jax.experimental.pallas import tpu as pltpu
from jax.sharding import PartitionSpec as P


def doc_table(doc_starts, tok_dev):
    n_outer, n_inner, n_slots = doc_starts.shape
    flat_starts = doc_starts.reshape(n_outer * n_inner, n_slots)
    start_counts = jnp.sum((flat_starts < tok_dev).astype(jnp.int32), axis=1)
    first_index = jnp.cumsum(start_counts) - start_counts
    offsets = jnp.arange(tok_dev, dtype=jnp.int32)
    inside_count = jnp.sum(
        (flat_starts[:, None, :] <= offsets[None, :, None]).astype(jnp.int32), axis=2
    )
    return (first_index[:, None] + inside_count - 1).reshape(n_outer, n_inner, tok_dev)


def attention_kernel(
    order_ref, qmeta_ref, kmeta_ref, q_ref, g_ref, k_ref, v_ref,
    o_ref, dq_ref, dkv_ref, dkt_ref, dvt_ref, *, scaling, n_heads, head_dim, slot_len
):
    step = pl.program_id(0)

    @pl.when(step == 0)
    def _():
        dkt_ref[...] = jnp.zeros_like(dkt_ref)
        dvt_ref[...] = jnp.zeros_like(dvt_ref)

    k = k_ref[...]
    v = v_ref[...]
    kt = k.T
    vt = v.T
    contract_first = (((0,), (0,)), ((), ()))
    lanes = qmeta_ref.shape[1] // 2
    allowed = (qmeta_ref[:, 0:1] == kmeta_ref[0:1, :]) & (
        kmeta_ref[1:2, :] <= qmeta_ref[:, lanes : lanes + 1]
    )
    for h in range(n_heads):
        cols = slice(h * head_dim, (h + 1) * head_dim)
        q = q_ref[:, cols]
        g = g_ref[:, cols]
        scores = jnp.dot(q, kt, preferred_element_type=jnp.float32) * scaling
        scores = jnp.where(allowed, scores, -jnp.inf)
        row_max = jnp.max(scores, axis=1, keepdims=True)
        log_total = row_max + jnp.log(
            jnp.sum(jnp.exp(scores - row_max), axis=1, keepdims=True)
        )
        probs = jnp.exp(scores - log_total)
        probs_low = probs.astype(jnp.bfloat16)
        attn = jnp.dot(probs_low, v, preferred_element_type=jnp.float32).astype(jnp.bfloat16)
        o_ref[:, cols] = attn
        inner_prod = jnp.sum(
            g.astype(jnp.float32) * attn.astype(jnp.float32), axis=1, keepdims=True
        )
        grad_probs = jnp.dot(g, vt, preferred_element_type=jnp.float32)
        score_grads = (probs * (grad_probs - inner_prod)).astype(jnp.bfloat16)
        dq_ref[:, cols] = (
            jnp.dot(score_grads, k, preferred_element_type=jnp.float32) * scaling
        ).astype(jnp.bfloat16)
        dkt_ref[...] += (
            lax.dot_general(q, score_grads, contract_first, preferred_element_type=jnp.float32)
            * scaling
        )
        dvt_ref[...] += lax.dot_general(
            g, probs_low, contract_first, preferred_element_type=jnp.float32
        )

    @pl.when(step == pl.num_programs(0) - 1)
    def _():
        n_used = dkt_ref.shape[1] // slot_len
        for r in range(n_used):
            cols = slice(r * slot_len, (r + 1) * slot_len)
            slot = order_ref[r]
            dkv_ref[slot, :, 0:head_dim] = dkt_ref[:, cols].T
            dkv_ref[slot, :, head_dim : 2 * head_dim] = dvt_ref[:, cols].T
        for r in range(n_used, dkv_ref.shape[0]):
            dkv_ref[order_ref[r]] = jnp.zeros(dkv_ref.shape[1:], dkv_ref.dtype)


def attend(rows, qmeta, ctx_all, kmeta_all, order, n_keys, n_heads):
    n_rows = rows.shape[0]
    n_slots = order.shape[0]
    slot_len = ctx_all.shape[0] // n_slots
    head_dim = ctx_all.shape[1] // 2
    width_q = n_heads * head_dim
    block_q = min(256, n_rows)
    grid = (n_rows // block_q,)
    q_spec = pl.BlockSpec((block_q, width_q), lambda i, o: (i, 0))
    g_spec = pl.BlockSpec((block_q, width_q), lambda i, o: (i, 1))
    qmeta_spec = pl.BlockSpec((block_q, qmeta.shape[1]), lambda i, o: (i, 0))
    kmeta_spec = pl.BlockSpec((2, n_keys), lambda i, o: (0, 0))
    k_spec = pl.BlockSpec((n_keys, head_dim), lambda i, o: (0, 0))
    v_spec = pl.BlockSpec((n_keys, head_dim), lambda i, o: (0, 1))
    out_spec = pl.BlockSpec((block_q, width_q), lambda i, o: (i, 0))
    grads_spec = pl.BlockSpec((n_slots, slot_len, 2 * head_dim), lambda i, o: (0, 0, 0))
    kernel = functools.partial(
        attention_kernel,
        scaling=1.0 / math.sqrt(head_dim),
        n_heads=n_heads,
        head_dim=head_dim,
        slot_len=slot_len,
    )
    return pl.pallas_call(
        kernel,
        grid_spec=pltpu.PrefetchScalarGridSpec(
            num_scalar_prefetch=1,
            grid=grid,
            in_specs=[qmeta_spec, kmeta_spec, q_spec, g_spec, k_spec, v_spec],
            out_specs=[out_spec, out_spec, grads_spec],
            scratch_shapes=[
                pltpu.VMEM((head_dim, n_keys), jnp.float32),
                pltpu.VMEM((head_dim, n_keys), jnp.float32),
            ],
        ),
        out_shape=[
            jax.ShapeDtypeStruct((n_rows, width_q), jnp.bfloat16),
            jax.ShapeDtypeStruct((n_rows, width_q), jnp.bfloat16),
            jax.ShapeDtypeStruct((n_slots, slot_len, 2 * head_dim), jnp.float32),
        ],
        compiler_params=pltpu.CompilerParams(dimension_semantics=("arbitrary",)),
    )(order, qmeta, kmeta_all, rows, rows, ctx_all, ctx_all)


def shards(queries, keys, values, grad_out, doc_starts):
    n_inner = lax.axis_size("inner")
    n_outer = lax.axis_size("outer")
    n_units = queries.shape[1]
    piece_len = queries.shape[3]
    width_q = queries.shape[4]
    head_dim = keys.shape[4]
    n_heads = width_q // head_dim
    tok_dev = piece_len * n_inner
    outer_id = lax.axis_index("outer")
    inner_id = lax.axis_index("inner")
    docs_all = doc_table(doc_starts, tok_dev)
    offsets = jnp.arange(tok_dev, dtype=jnp.int32)

    def packed_for(shift):
        def pack(q, g, k, v):
            return jnp.roll(jnp.concatenate([q, g, k, v], axis=-1), -2 * shift, axis=0)

        return pack

    packed = lax.switch(
        outer_id,
        [packed_for(o) for o in range(n_outer)],
        queries[0, :, 0],
        grad_out[0, :, 0],
        keys[0, :, 0],
        values[0, :, 0],
    )
    unit_local = (inner_id + 2 * outer_id) % n_units
    arrived = lax.all_to_all(packed, "inner", 0, 0, tiled=True).reshape(tok_dev, -1)
    kv_own = arrived[:, 2 * width_q :]

    pairs_up = [(2 * p, 2 * p + 1) for p in range(n_inner // 2)]
    kv_partner = lax.ppermute(kv_own, "inner", pairs_up)

    both = ("outer", "inner")
    last_a, last_b = n_inner - 2, n_inner - 1
    lead = [(-2 * o) % n_inner for o in range(n_outer)]
    send_a = [((o - 1) * n_inner + lead[o] + r, o * n_inner + lead[o] + r)
              for o in range(1, n_outer) for r in range(2)]
    send_b = [((o - 1) * n_inner + lead[o] + r, o * n_inner + lead[o] + 1 - r)
              for o in range(1, n_outer) for r in range(2)]
    recv_a = lax.ppermute(kv_own, both, send_a)
    recv_b = lax.ppermute(kv_own, both, send_b)
    first = unit_local == 0
    kv_prev_a = jnp.where(first, recv_a, recv_b)
    kv_prev_b = jnp.where(first, recv_b, recv_a)

    unit_id = outer_id * n_units + unit_local
    before = jnp.maximum(outer_id - 1, 0)
    has_prev = (outer_id > 0) & (unit_local < 2)
    has_partner = unit_local % 2 == 1
    query_doc = docs_all[outer_id, unit_local]
    query_pos = unit_id * tok_dev + offsets
    partner_doc = jnp.where(has_partner, docs_all[outer_id, jnp.maximum(unit_local - 1, 0)], -3)
    prev_a_doc = jnp.where(has_prev, docs_all[before, last_a], -4)
    prev_b_doc = jnp.where(has_prev, docs_all[before, last_b], -5)
    key_doc = jnp.concatenate([prev_a_doc, prev_b_doc, partner_doc, query_doc])
    key_pos = jnp.concatenate(
        [
            (before * n_units + last_a) * tok_dev + offsets,
            (before * n_units + last_b) * tok_dev + offsets,
            (unit_id - 1) * tok_dev + offsets,
            query_pos,
        ]
    )
    n_slots = 8
    slot_len = tok_dev * 4 // n_slots
    slot_kv = jnp.stack([kv_prev_a, kv_prev_b, kv_partner, kv_own]).reshape(
        n_slots, slot_len, 2 * head_dim
    )
    slot_doc = key_doc.reshape(n_slots, slot_len)
    slot_pos = key_pos.reshape(n_slots, slot_len)
    needed = (
        (jnp.min(slot_doc, axis=1) <= jnp.max(query_doc))
        & (jnp.max(slot_doc, axis=1) >= jnp.min(query_doc))
        & (jnp.min(slot_pos, axis=1) <= jnp.max(query_pos))
    )
    needed = needed | (jnp.arange(n_slots) >= n_slots - 2)
    needed_i = needed.astype(jnp.int32)
    count = jnp.sum(needed_i)
    rank = jnp.where(
        needed, jnp.cumsum(needed_i) - 1, count + jnp.cumsum(1 - needed_i) - 1
    )
    slot_ids = jnp.arange(n_slots, dtype=jnp.int32)
    order = jnp.sum(
        jnp.where(rank[None, :] == slot_ids[:, None], slot_ids[None, :], 0), axis=1
    )
    kv_sorted = slot_kv[order].reshape(n_slots * slot_len, 2 * head_dim)
    kmeta_sorted = jnp.stack([slot_doc[order].reshape(-1), slot_pos[order].reshape(-1)])
    lane_width = 128
    qmeta = jnp.concatenate(
        [
            jnp.broadcast_to(query_doc[:, None], (tok_dev, lane_width)),
            jnp.broadcast_to(query_pos[:, None], (tok_dev, lane_width)),
        ],
        axis=1,
    )

    def branch(n_used):
        def run(kv_sorted, kmeta_sorted, qmeta, order):
            return attend(
                arrived, qmeta, kv_sorted, kmeta_sorted, order, n_used * slot_len, n_heads
            )

        return run

    sizes = [2, 3, 4, 5, n_slots]
    bucket = sum((count > n).astype(jnp.int32) for n in sizes[:-1])
    attn, q_grads, kv_grads = lax.switch(
        bucket,
        [branch(n) for n in sizes],
        kv_sorted,
        kmeta_sorted,
        qmeta,
        order,
    )

    kv_grads = kv_grads.reshape(4, tok_dev, 2 * head_dim)
    pairs_down = [(b, a) for a, b in pairs_up]
    low = jnp.bfloat16
    from_partner = lax.ppermute(kv_grads[2].astype(low), "inner", pairs_down)
    back_a = [(b, a) for a, b in send_a]
    back_b = [(b, a) for a, b in send_b]
    grads_a = jnp.where(first, kv_grads[0], kv_grads[1])
    grads_b = jnp.where(first, kv_grads[1], kv_grads[0])
    from_next_a = lax.ppermute(grads_a.astype(low), both, back_a)
    from_next_b = lax.ppermute(grads_b.astype(low), both, back_b)
    kv_total = (
        kv_grads[3]
        + from_partner.astype(jnp.float32)
        + from_next_a.astype(jnp.float32)
        + from_next_b.astype(jnp.float32)
    ).astype(jnp.bfloat16)

    result = jnp.concatenate([attn, q_grads, kv_total], axis=-1).reshape(
        n_inner, piece_len, -1
    )
    returned = jnp.roll(
        lax.all_to_all(result, "inner", 0, 0, tiled=True), 2 * outer_id, axis=0
    )
    shape_q = (1, n_units, 1, piece_len, width_q)
    shape_k = (1, n_units, 1, piece_len, head_dim)
    return (
        returned[..., :width_q].reshape(shape_q),
        returned[..., width_q : 2 * width_q].reshape(shape_q),
        returned[..., 2 * width_q : 2 * width_q + head_dim].reshape(shape_k),
        returned[..., 2 * width_q + head_dim :].reshape(shape_k),
    )


def solution(mesh):
    return jax.shard_map(
        shards,
        mesh=mesh,
        in_specs=(
            P("outer", None, "inner", None, None),
            P("outer", None, "inner", None, None),
            P("outer", None, "inner", None, None),
            P("outer", None, "inner", None, None),
            P(),
        ),
        out_specs=(
            P("outer", None, "inner", None, None),
            P("outer", None, "inner", None, None),
            P("outer", None, "inner", None, None),
            P("outer", None, "inner", None, None),
        ),
        check_vma=False,
    )
```

```python
import functools
import math

import jax
import jax.numpy as jnp
from jax import lax
from jax.experimental import pallas as pl
from jax.experimental.pallas import tpu as pltpu
from jax.sharding import PartitionSpec as P


def doc_table(doc_starts, tok_dev):
    n_outer, n_inner, n_slots = doc_starts.shape
    flat_starts = doc_starts.reshape(n_outer * n_inner, n_slots)
    start_counts = jnp.sum((flat_starts < tok_dev).astype(jnp.int32), axis=1)
    first_index = jnp.cumsum(start_counts) - start_counts
    offsets = jnp.arange(tok_dev, dtype=jnp.int32)
    inside_count = jnp.sum(
        (flat_starts[:, None, :] <= offsets[None, :, None]).astype(jnp.int32), axis=2
    )
    return (first_index[:, None] + inside_count - 1).reshape(n_outer, n_inner, tok_dev)


def attention_kernel(
    order_ref, qmeta_ref, kmeta_ref, q_ref, g_ref, k_ref, v_ref,
    out_ref, dkv_ref, dkt_ref, dvt_ref, *, scaling, n_heads, head_dim, slot_len
):
    step = pl.program_id(0)

    @pl.when(step == 0)
    def _():
        dkt_ref[...] = jnp.zeros_like(dkt_ref)
        dvt_ref[...] = jnp.zeros_like(dvt_ref)

    k = k_ref[...]
    v = v_ref[...]
    kt = k.T
    vt = v.T
    contract_first = (((0,), (0,)), ((), ()))
    lanes = qmeta_ref.shape[1] // 2
    allowed = (qmeta_ref[:, 0:1] == kmeta_ref[0:1, :]) & (
        kmeta_ref[1:2, :] <= qmeta_ref[:, lanes : lanes + 1]
    )
    for h in range(n_heads):
        cols = slice(h * head_dim, (h + 1) * head_dim)
        q = q_ref[:, cols]
        g = g_ref[:, cols]
        scores = jnp.dot(q, kt, preferred_element_type=jnp.float32) * scaling
        scores = jnp.where(allowed, scores, -jnp.inf)
        row_max = jnp.max(scores, axis=1, keepdims=True)
        log_total = row_max + jnp.log(
            jnp.sum(jnp.exp(scores - row_max), axis=1, keepdims=True)
        )
        probs = jnp.exp(scores - log_total)
        probs_low = probs.astype(jnp.bfloat16)
        attn = jnp.dot(probs_low, v, preferred_element_type=jnp.float32).astype(jnp.bfloat16)
        out_ref[:, cols] = attn
        inner_prod = jnp.sum(
            g.astype(jnp.float32) * attn.astype(jnp.float32), axis=1, keepdims=True
        )
        grad_probs = jnp.dot(g, vt, preferred_element_type=jnp.float32)
        score_grads = (probs * (grad_probs - inner_prod)).astype(jnp.bfloat16)
        dq_cols = slice((n_heads + h) * head_dim, (n_heads + h + 1) * head_dim)
        out_ref[:, dq_cols] = (
            jnp.dot(score_grads, k, preferred_element_type=jnp.float32) * scaling
        ).astype(jnp.bfloat16)
        dkt_ref[...] += (
            lax.dot_general(q, score_grads, contract_first, preferred_element_type=jnp.float32)
            * scaling
        )
        dvt_ref[...] += lax.dot_general(
            g, probs_low, contract_first, preferred_element_type=jnp.float32
        )

    @pl.when(step == pl.num_programs(0) - 1)
    def _():
        n_used = dkt_ref.shape[1] // slot_len
        for r in range(n_used):
            cols = slice(r * slot_len, (r + 1) * slot_len)
            slot = order_ref[r]
            dkv_ref[slot, :, 0:head_dim] = dkt_ref[:, cols].T
            dkv_ref[slot, :, head_dim : 2 * head_dim] = dvt_ref[:, cols].T
        for r in range(n_used, dkv_ref.shape[0]):
            dkv_ref[order_ref[r]] = jnp.zeros(dkv_ref.shape[1:], dkv_ref.dtype)


def attend(rows, qmeta, ctx_all, kmeta_all, order, n_keys, n_heads):
    n_rows = rows.shape[0]
    n_slots = order.shape[0]
    slot_len = ctx_all.shape[0] // n_slots
    head_dim = ctx_all.shape[1] // 2
    width_q = n_heads * head_dim
    block_q = min(256, n_rows)
    grid = (n_rows // block_q,)
    q_spec = pl.BlockSpec((block_q, width_q), lambda i, o: (i, 0))
    g_spec = pl.BlockSpec((block_q, width_q), lambda i, o: (i, 1))
    qmeta_spec = pl.BlockSpec((block_q, qmeta.shape[1]), lambda i, o: (i, 0))
    kmeta_spec = pl.BlockSpec((2, n_keys), lambda i, o: (0, 0))
    k_spec = pl.BlockSpec((n_keys, head_dim), lambda i, o: (0, 0))
    v_spec = pl.BlockSpec((n_keys, head_dim), lambda i, o: (0, 1))
    out_width = 2 * width_q + 2 * head_dim
    out_spec = pl.BlockSpec((block_q, out_width), lambda i, o: (i, 0))
    grads_spec = pl.BlockSpec((n_slots, slot_len, 2 * head_dim), lambda i, o: (0, 0, 0))
    kernel = functools.partial(
        attention_kernel,
        scaling=1.0 / math.sqrt(head_dim),
        n_heads=n_heads,
        head_dim=head_dim,
        slot_len=slot_len,
    )
    return pl.pallas_call(
        kernel,
        grid_spec=pltpu.PrefetchScalarGridSpec(
            num_scalar_prefetch=1,
            grid=grid,
            in_specs=[qmeta_spec, kmeta_spec, q_spec, g_spec, k_spec, v_spec],
            out_specs=[out_spec, grads_spec],
            scratch_shapes=[
                pltpu.VMEM((head_dim, n_keys), jnp.float32),
                pltpu.VMEM((head_dim, n_keys), jnp.float32),
            ],
        ),
        out_shape=[
            jax.ShapeDtypeStruct((n_rows, out_width), jnp.bfloat16),
            jax.ShapeDtypeStruct((n_slots, slot_len, 2 * head_dim), jnp.float32),
        ],
        compiler_params=pltpu.CompilerParams(dimension_semantics=("arbitrary",)),
    )(order, qmeta, kmeta_all, rows, rows, ctx_all, ctx_all)


def shards(queries, keys, values, grad_out, doc_starts):
    n_inner = lax.axis_size("inner")
    n_outer = lax.axis_size("outer")
    n_units = queries.shape[1]
    piece_len = queries.shape[3]
    width_q = queries.shape[4]
    head_dim = keys.shape[4]
    n_heads = width_q // head_dim
    tok_dev = piece_len * n_inner
    outer_id = lax.axis_index("outer")
    inner_id = lax.axis_index("inner")
    docs_all = doc_table(doc_starts, tok_dev)
    offsets = jnp.arange(tok_dev, dtype=jnp.int32)

    def packed_for(shift):
        def pack(q, g, k, v):
            return jnp.roll(jnp.concatenate([q, g, k, v], axis=-1), -2 * shift, axis=0)

        return pack

    packed = lax.switch(
        outer_id,
        [packed_for(o) for o in range(n_outer)],
        queries[0, :, 0],
        grad_out[0, :, 0],
        keys[0, :, 0],
        values[0, :, 0],
    )
    unit_local = (inner_id + 2 * outer_id) % n_units
    arrived = lax.all_to_all(packed, "inner", 0, 0, tiled=True).reshape(tok_dev, -1)
    kv_own = arrived[:, 2 * width_q :]

    pairs_up = [(2 * p, 2 * p + 1) for p in range(n_inner // 2)]
    kv_partner = lax.ppermute(kv_own, "inner", pairs_up)

    both = ("outer", "inner")
    last_a, last_b = n_inner - 2, n_inner - 1
    lead = [(-2 * o) % n_inner for o in range(n_outer)]
    send_a = [((o - 1) * n_inner + lead[o] + r, o * n_inner + lead[o] + r)
              for o in range(1, n_outer) for r in range(2)]
    send_b = [((o - 1) * n_inner + lead[o] + r, o * n_inner + lead[o] + 1 - r)
              for o in range(1, n_outer) for r in range(2)]
    recv_a = lax.ppermute(kv_own, both, send_a)
    recv_b = lax.ppermute(kv_own, both, send_b)
    first = unit_local == 0
    kv_prev_a = jnp.where(first, recv_a, recv_b)
    kv_prev_b = jnp.where(first, recv_b, recv_a)

    unit_id = outer_id * n_units + unit_local
    before = jnp.maximum(outer_id - 1, 0)
    has_prev = (outer_id > 0) & (unit_local < 2)
    has_partner = unit_local % 2 == 1
    query_doc = docs_all[outer_id, unit_local]
    query_pos = unit_id * tok_dev + offsets
    partner_doc = jnp.where(has_partner, docs_all[outer_id, jnp.maximum(unit_local - 1, 0)], -3)
    prev_a_doc = jnp.where(has_prev, docs_all[before, last_a], -4)
    prev_b_doc = jnp.where(has_prev, docs_all[before, last_b], -5)
    key_doc = jnp.concatenate([prev_a_doc, prev_b_doc, partner_doc, query_doc])
    key_pos = jnp.concatenate(
        [
            (before * n_units + last_a) * tok_dev + offsets,
            (before * n_units + last_b) * tok_dev + offsets,
            (unit_id - 1) * tok_dev + offsets,
            query_pos,
        ]
    )
    n_slots = 8
    slot_len = tok_dev * 4 // n_slots
    slot_kv = jnp.stack([kv_prev_a, kv_prev_b, kv_partner, kv_own]).reshape(
        n_slots, slot_len, 2 * head_dim
    )
    slot_doc = key_doc.reshape(n_slots, slot_len)
    slot_pos = key_pos.reshape(n_slots, slot_len)
    needed = (
        (jnp.min(slot_doc, axis=1) <= jnp.max(query_doc))
        & (jnp.max(slot_doc, axis=1) >= jnp.min(query_doc))
        & (jnp.min(slot_pos, axis=1) <= jnp.max(query_pos))
    )
    needed = needed | (jnp.arange(n_slots) >= n_slots - 2)
    needed_i = needed.astype(jnp.int32)
    count = jnp.sum(needed_i)
    rank = jnp.where(
        needed, jnp.cumsum(needed_i) - 1, count + jnp.cumsum(1 - needed_i) - 1
    )
    slot_ids = jnp.arange(n_slots, dtype=jnp.int32)
    order = jnp.sum(
        jnp.where(rank[None, :] == slot_ids[:, None], slot_ids[None, :], 0), axis=1
    )
    kv_sorted = slot_kv[order].reshape(n_slots * slot_len, 2 * head_dim)
    kmeta_sorted = jnp.stack([slot_doc[order].reshape(-1), slot_pos[order].reshape(-1)])
    lane_width = 128
    qmeta = jnp.concatenate(
        [
            jnp.broadcast_to(query_doc[:, None], (tok_dev, lane_width)),
            jnp.broadcast_to(query_pos[:, None], (tok_dev, lane_width)),
        ],
        axis=1,
    )

    def branch(n_used):
        def run(kv_sorted, kmeta_sorted, qmeta, order):
            return attend(
                arrived, qmeta, kv_sorted, kmeta_sorted, order, n_used * slot_len, n_heads
            )

        return run

    sizes = [2, 3, 4, 5, n_slots]
    bucket = sum((count > n).astype(jnp.int32) for n in sizes[:-1])
    out_rows, kv_grads = lax.switch(
        bucket,
        [branch(n) for n in sizes],
        kv_sorted,
        kmeta_sorted,
        qmeta,
        order,
    )

    kv_grads = kv_grads.reshape(4, tok_dev, 2 * head_dim)
    pairs_down = [(b, a) for a, b in pairs_up]
    low = jnp.bfloat16
    from_partner = lax.ppermute(kv_grads[2].astype(low), "inner", pairs_down)
    back_a = [(b, a) for a, b in send_a]
    back_b = [(b, a) for a, b in send_b]
    grads_a = jnp.where(first, kv_grads[0], kv_grads[1])
    grads_b = jnp.where(first, kv_grads[1], kv_grads[0])
    from_next_a = lax.ppermute(grads_a.astype(low), both, back_a)
    from_next_b = lax.ppermute(grads_b.astype(low), both, back_b)
    kv_total = (
        kv_grads[3]
        + from_partner.astype(jnp.float32)
        + from_next_a.astype(jnp.float32)
        + from_next_b.astype(jnp.float32)
    ).astype(jnp.bfloat16)

    result = out_rows.at[:, 2 * width_q :].set(kv_total).reshape(
        n_inner, piece_len, -1
    )
    returned = jnp.roll(
        lax.all_to_all(result, "inner", 0, 0, tiled=True), 2 * outer_id, axis=0
    )
    shape_q = (1, n_units, 1, piece_len, width_q)
    shape_k = (1, n_units, 1, piece_len, head_dim)
    return (
        returned[..., :width_q].reshape(shape_q),
        returned[..., width_q : 2 * width_q].reshape(shape_q),
        returned[..., 2 * width_q : 2 * width_q + head_dim].reshape(shape_k),
        returned[..., 2 * width_q + head_dim :].reshape(shape_k),
    )


def solution(mesh):
    return jax.shard_map(
        shards,
        mesh=mesh,
        in_specs=(
            P("outer", None, "inner", None, None),
            P("outer", None, "inner", None, None),
            P("outer", None, "inner", None, None),
            P("outer", None, "inner", None, None),
            P(),
        ),
        out_specs=(
            P("outer", None, "inner", None, None),
            P("outer", None, "inner", None, None),
            P("outer", None, "inner", None, None),
            P("outer", None, "inner", None, None),
        ),
        check_vma=False,
    )
```
